512 devices in a mesh: dp: 4 (over x), ctx: 16 (over z), mp: 8 (over y, core).
Axes of the slice: x: 4, y: 4, z: 16, core: 2. Of those that a mesh axis runs over, the one named last changes fastest.
Arguments:
- tokens: bfloat16 [4, 2048, 4096], P('dp', 'ctx'), may hold values from -52 to 52
- x_weight: bfloat16 [4096, 8192], P(('dp', 'ctx'), 'mp'), may hold values from -0.09375 to 0.09375
- bc_weight: bfloat16 [4096, 1024], P(('dp', 'ctx'), 'mp'), may hold values from -0.09375 to 0.09375
- dt_weight: bfloat16 [4096, 128], P(('dp', 'ctx'), 'mp'), may hold values from -0.0234375 to 0.0234375
- conv_x: float32 [5, 8192], P(None, 'mp'), may hold values from -0.5 to 0.5
- conv_bc: float32 [5, 1024], P(None, 'mp'), may hold values from -0.5 to 0.5
- dt_bias: float32 [128], P('mp'), may hold values from -4.5 to -2.5
- a_log: float32 [128], P('mp')
- d_skip: float32 [128], P('mp'), may hold values from 0.5 to 1.5
- norm_gain: float32 [8192], P('mp'), may hold values from 0.5 to 1.5
Outputs:
- mixer_out: bfloat16 [4, 2048, 8192], P('dp', 'ctx', 'mp')
- kurtosis: float32 [4096], P('mp')
The draws below stay inside these ranges and needn't reach their ends.
All inputs are finite; a program needn't handle non-finite values.
Results may differ from the reference program's by a relative error of at most 0.015.
Values may be sent and summed in bfloat16 or wider, within the bound.
No kernel may reach another device: no remote copies, remote signals or barrier semaphores. Data moves between devices by JAX's collectives and lax.ppermute only.
A program may use at most 64 MiB of HBM per device.

```python
import jax
import jax.numpy as jnp
from jax import lax

D = 4096
ROOT = 64
HEADS = 128
P_SIZE = 64
G = 4
NS = 128
KW = 4
TOK_DEV = 128
SEQLEN = 2048
BATCH = 4
INNER = 8192
BCW = 1024
N_CTX = 16


def draw_tokens(key, part):
    sample_key, row_key, col_key = jax.random.split(jax.random.fold_in(key, 11), 3)
    full_shape = (BATCH, SEQLEN, D)
    samples = jnp.clip(jax.random.normal(sample_key, full_shape, jnp.float32), -6.0, 6.0)
    row_scale = jnp.exp(jax.random.uniform(row_key, (BATCH, SEQLEN, 1), jnp.float32) * jnp.log(10.0))
    position = (jnp.arange(BATCH, dtype=jnp.float32)[:, None, None] * SEQLEN + jnp.arange(SEQLEN, dtype=jnp.float32)[None, :, None]) / (BATCH * SEQLEN)
    trend = jnp.exp(0.5 * jnp.log(3.0) * position)
    col_scale = jnp.exp(jax.random.uniform(col_key, (D,), jnp.float32) * jnp.log(10.0))
    return (0.05 * samples * row_scale * trend * col_scale).astype(jnp.bfloat16)


def draw_a_log(key, part):
    pick_key, level_key = jax.random.split(jax.random.fold_in(key, 23), 2)
    pick = jax.random.uniform(pick_key, (HEADS,), jnp.float32)
    level = jax.random.uniform(level_key, (HEADS,), jnp.float32)
    slow_share = 0.55
    slow_low = jnp.log(0.5 / SEQLEN)
    slow_value = slow_low + level * jnp.log(60.0)
    fast_low = jnp.log(30.0 / SEQLEN)
    fast_value = fast_low + level * (0.0 - fast_low)
    return jnp.where(pick < slow_share, slow_value, fast_value).astype(jnp.float32)


def steps_of(own_key, dims, cuts, least, top_value):
    def one(dim, blocks):
        heights = jax.random.uniform(jax.random.fold_in(jax.random.fold_in(own_key, 6), dim), (blocks,), jnp.float32, least / len(cuts), top_value / len(cuts))
        return jnp.repeat(jnp.exp(heights), dims[dim] // blocks).reshape((-1,) + (1,) * (len(dims) - dim - 1))

    gain = one(*cuts[0])
    for cut in cuts[1:]:
        gain = gain * one(*cut)
    return gain


def bell_draw(stream_key, dims, scale, bound, cuts=(), kind=jnp.bfloat16):
    array = scale * jax.random.normal(stream_key, dims, jnp.float32)
    if cuts:
        array = array * steps_of(stream_key, dims, cuts, -0.22, 0.18)
    return jnp.clip(array, -bound, bound).astype(kind)


def setup_inputs(seed: int = 0) -> dict:
    seeds = jax.random.split(jax.random.key(seed), 11)
    tokens = draw_tokens(jax.random.fold_in(seeds[10], 71), 0)
    x_weight = bell_draw(seeds[1], (D, INNER), D ** -0.5, 0.09375, ((0, 64), (1, 8)))
    bc_weight = bell_draw(seeds[2], (D, BCW), D ** -0.5, 0.09375, ((0, 64), (1, 8)))
    dt_weight = bell_draw(seeds[3], (D, HEADS), (16 * D) ** -0.5, 0.0234375, ((0, 64), (1, 8)))
    conv_x = jnp.clip(jax.random.uniform(seeds[4], (KW + 1, INNER), jnp.float32, -0.5, 0.5) * steps_of(seeds[4], (KW + 1, INNER), ((1, 8),), -0.4, 0.0), -0.5, 0.5)
    conv_bc = jnp.clip(jax.random.uniform(seeds[5], (KW + 1, BCW), jnp.float32, -0.5, 0.5) * steps_of(seeds[5], (KW + 1, BCW), ((1, 8),), -0.4, 0.0), -0.5, 0.5)
    dt_bias = jnp.clip(-4.5 + 2.0 * jax.random.uniform(seeds[6], (HEADS,), jnp.float32) ** steps_of(seeds[6], (HEADS,), ((0, 8),), -0.2, 0.2), -4.5, -2.5)
    a_log = draw_a_log(jax.random.fold_in(seeds[10], 71), 0)
    d_skip = jnp.clip(0.5 + 1.0 * jax.random.uniform(seeds[8], (HEADS,), jnp.float32) ** steps_of(seeds[8], (HEADS,), ((0, 8),), -0.2, 0.2), 0.5, 1.5)
    norm_gain = jnp.clip(1.0 + 0.1 * jax.random.normal(seeds[9], (INNER,), jnp.float32), 0.5, 1.5)
    return dict(tokens=tokens, x_weight=x_weight, bc_weight=bc_weight, dt_weight=dt_weight, conv_x=conv_x, conv_bc=conv_bc, dt_bias=dt_bias, a_log=a_log, d_skip=d_skip, norm_gain=norm_gain)


HIGH = lax.Precision.HIGHEST

def hadamard_signs(sign_order):
    row_index = lax.broadcasted_iota(jnp.int32, (sign_order, sign_order), 0)
    col_index = lax.broadcasted_iota(jnp.int32, (sign_order, sign_order), 1)
    common = jnp.bitwise_and(row_index, col_index)
    parity = jnp.zeros((sign_order, sign_order), jnp.int32)
    for bit_index in range(sign_order.bit_length() - 1):
        parity = parity + jnp.bitwise_and(jnp.right_shift(common, bit_index), 1)
    return 1.0 - 2.0 * jnp.bitwise_and(parity, 1).astype(jnp.float32)

def kurtosis_from(powers, row_count):
    average = powers[0] / row_count
    second = powers[1] / row_count - average * average
    fourth = powers[3] / row_count - 4.0 * average * powers[2] / row_count + 6.0 * average * average * powers[1] / row_count - 3.0 * average * average * average * average
    return fourth / (second * second + 1e-06)

def reference(tokens, x_weight, bc_weight, dt_weight, conv_x, conv_bc, dt_bias, a_log, d_skip, norm_gain):
    row_total = BATCH * SEQLEN
    signs = hadamard_signs(ROOT)
    flattened = tokens.reshape(row_total, ROOT, ROOT).astype(jnp.float32)
    first_pass = jnp.einsum('tab,ac->tcb', flattened, signs, precision=HIGH)
    second = jnp.einsum('tcb,bd->tcd', first_pass, signs, precision=HIGH)
    rotated = (second.reshape(row_total, D) / ROOT).astype(jnp.bfloat16)
    widened = rotated.astype(jnp.float32)
    square = widened * widened
    powers = jnp.stack([lax.optimization_barrier(jnp.sum(widened, 0)), lax.optimization_barrier(jnp.sum(square, 0)), lax.optimization_barrier(jnp.sum(square * widened, 0)), lax.optimization_barrier(jnp.sum(square * square, 0))])
    kurtosis = kurtosis_from(powers, float(row_total))
    x_proj = jnp.dot(rotated, x_weight, preferred_element_type=jnp.float32).astype(jnp.bfloat16)
    bc_proj = jnp.dot(rotated, bc_weight, preferred_element_type=jnp.float32).astype(jnp.bfloat16)
    dt_proj = lax.optimization_barrier(jnp.dot(rotated, dt_weight, preferred_element_type=jnp.float32).astype(jnp.bfloat16))
    conv_taps = jnp.concatenate([conv_x, conv_bc], 1)
    per_group = HEADS // G
    block_len = TOK_DEV
    causal = lax.broadcasted_iota(jnp.int32, (block_len, block_len), 0) >= lax.broadcasted_iota(jnp.int32, (block_len, block_len), 1)

    def one_block(state_now, blk):
        x_blk, bc_blk, dt_blk = blk
        step_size = jax.nn.softplus(dt_blk.astype(jnp.float32) + dt_bias)
        decay_rate = step_size * jnp.exp(a_log)
        cumulative = jnp.cumsum(decay_rate, 0)
        block_end = cumulative[-1]
        x_heads = x_blk.reshape(block_len, G, per_group, P_SIZE).astype(jnp.float32)
        write_all = bc_blk[:, :G * NS].reshape(block_len, G, NS).astype(jnp.float32)
        read_all = bc_blk[:, G * NS:].reshape(block_len, G, NS).astype(jnp.float32)
        spread = cumulative.T[:, :, None] - cumulative.T[:, None, :]
        decay_mask = jnp.where(causal, jnp.exp(-jnp.where(causal, spread, 0.0)), 0.0)
        scores = jnp.einsum('tgn,sgn->gts', read_all, write_all, precision=HIGH)
        weights = (scores[:, None] * decay_mask.reshape(G, per_group, block_len, block_len) * step_size.T.reshape(G, per_group, 1, block_len)).astype(jnp.bfloat16)
        within_block = jnp.einsum('ghts,sghp->tghp', weights.astype(jnp.float32), x_heads, precision=HIGH)
        from_before = jnp.exp(-cumulative).reshape(block_len, G, per_group)[..., None] * jnp.einsum('tgn,ghpn->tghp', read_all, state_now, precision=HIGH)
        output_raw = within_block + from_before + d_skip.reshape(G, per_group)[None, :, :, None] * x_heads
        update = ((jnp.exp(-(block_end - cumulative)) * step_size).reshape(block_len, G, per_group)[..., None] * x_heads).astype(jnp.bfloat16)
        contrib = jnp.einsum('sghp,sgn->ghpn', update.astype(jnp.float32), write_all, precision=HIGH)
        new_state = jnp.exp(-block_end).reshape(G, per_group)[:, :, None, None] * state_now + contrib
        mean_square = lax.optimization_barrier(jnp.mean(output_raw * output_raw, -1, keepdims=True))
        normed = output_raw * lax.rsqrt(mean_square + 1e-05) * norm_gain.reshape(G, per_group, P_SIZE)
        return (new_state, normed.reshape(block_len, INNER).astype(jnp.bfloat16))

    def one_sequence(inputs):
        x_seq, bc_seq, dt_seq = inputs
        joined = jnp.concatenate([x_seq, bc_seq], 1)
        padded = jnp.pad(joined, ((KW - 1, 0), (0, 0)))
        conv_sum = conv_taps[KW]
        for tap_index in range(KW):
            conv_sum = conv_sum + conv_taps[tap_index] * padded[tap_index:tap_index + SEQLEN]
        convolved = jax.nn.silu(conv_sum).astype(jnp.bfloat16)
        blocks_x = convolved[:, :INNER].reshape(N_CTX, block_len, INNER)
        blocks_bc = convolved[:, INNER:].reshape(N_CTX, block_len, BCW)
        blocks_dt = dt_seq.reshape(N_CTX, block_len, HEADS)
        start_state = jnp.zeros((G, per_group, P_SIZE, NS), jnp.float32)
        last_state, outputs = lax.scan(one_block, start_state, (blocks_x, blocks_bc, blocks_dt))
        return outputs.reshape(SEQLEN, INNER)
    mixer_out = lax.map(one_sequence, (x_proj.reshape(BATCH, SEQLEN, INNER), bc_proj.reshape(BATCH, SEQLEN, BCW), dt_proj.reshape(BATCH, SEQLEN, HEADS)))
    return (mixer_out, kurtosis)
```

```python
import jax
import jax.numpy as jnp
from jax import lax
from jax.sharding import PartitionSpec as P

ROOT = 64
HEADS = 128
G = 4
NS = 128


HIGH = lax.Precision.HIGHEST


def passed_along(value, axis, steps):
    count = lax.axis_size(axis)
    first, last = (max(0, -steps), min(count, count - steps))
    return lax.ppermute(value, axis, [(source, source + steps) for source in range(first, last)])


def entering(decay, contrib, axis):
    length, place = (lax.axis_size(axis), lax.axis_index(axis))
    lanes = contrib.shape[-1]
    rows = contrib.size // lanes
    tail = jnp.zeros((8, lanes), jnp.float32).at[0, : decay.size].set(decay.reshape(-1))
    flat = jnp.concatenate([contrib.reshape(rows, lanes), tail]).astype(jnp.bfloat16)
    everything = lax.all_gather(flat, axis).astype(jnp.float32)
    states = everything[:, :rows].reshape((length,) + contrib.shape)
    decays = everything[:, rows, : decay.size].reshape((length,) + decay.shape)
    source = lax.broadcasted_iota(jnp.int32, (length, length), 0)
    between = lax.broadcasted_iota(jnp.int32, (length, length), 1)
    inside = jnp.logical_and(between > source, between < place)
    factors = jnp.where(inside[:, :, None, None], decays[None], 1.0)
    weights = jnp.prod(factors, 1)
    weights = jnp.where((source[:, 0] < place)[:, None, None], weights, 0.0)
    return jnp.einsum("jgh,jghpn->ghpn", weights, states, precision=HIGH)


def hadamard_signs(sign_order):
    row_index = lax.broadcasted_iota(jnp.int32, (sign_order, sign_order), 0)
    col_index = lax.broadcasted_iota(jnp.int32, (sign_order, sign_order), 1)
    common = jnp.bitwise_and(row_index, col_index)
    parity = jnp.zeros((sign_order, sign_order), jnp.int32)
    for bit_index in range(sign_order.bit_length() - 1):
        parity = parity + jnp.bitwise_and(jnp.right_shift(common, bit_index), 1)
    return 1.0 - 2.0 * jnp.bitwise_and(parity, 1).astype(jnp.float32)


def kurtosis_from(powers, row_count):
    average = powers[0] / row_count
    second = powers[1] / row_count - average * average
    fourth = (
        powers[3] / row_count
        - 4.0 * average * powers[2] / row_count
        + 6.0 * average * average * powers[1] / row_count
        - 3.0 * average * average * average * average
    )
    return fourth / (second * second + 1e-06)


def shards(
    tokens, x_weight, bc_weight, dt_weight, conv_x, conv_bc, dt_bias, a_log, d_skip, norm_gain
):
    tok_rows = tokens.shape[1]
    model_width = tokens.shape[2]
    signs = hadamard_signs(ROOT)
    blocks = tokens.reshape(tok_rows, ROOT, ROOT)
    first_pass = jnp.einsum(
        "tab,ac->tcb", blocks, signs.astype(jnp.bfloat16), preferred_element_type=jnp.float32
    )
    second = jnp.einsum("tcb,bd->tcd", first_pass, signs, precision=HIGH)
    rotated = (second.reshape(tok_rows, model_width) / ROOT).astype(jnp.bfloat16)
    channel_share = model_width // lax.axis_size("mp")
    own_cols = lax.dynamic_slice_in_dim(
        rotated, lax.axis_index("mp") * channel_share, channel_share, 1
    ).astype(jnp.float32)
    square = own_cols * own_cols
    powers = jnp.stack(
        [
            jnp.sum(own_cols, 0),
            jnp.sum(square, 0),
            jnp.sum(square * own_cols, 0),
            jnp.sum(square * square, 0),
        ]
    )
    row_count = float(tok_rows * lax.axis_size("dp") * lax.axis_size("ctx"))
    totals = lax.psum(lax.psum(powers, "ctx"), "dp")
    totals, rotated = lax.optimization_barrier((totals, rotated))
    kurtosis = kurtosis_from(totals, row_count)
    local_panel = jnp.concatenate([x_weight, bc_weight, dt_weight], 1)
    panel = lax.all_gather(local_panel, ("dp", "ctx"), axis=0, tiled=True)
    both = jnp.dot(rotated, panel, preferred_element_type=jnp.float32)
    x_end = x_weight.shape[1]
    bc_end = x_end + bc_weight.shape[1]
    projected = (both[:, :x_end], both[:, x_end:bc_end], both[:, bc_end:])
    x_cols = x_weight.shape[1]
    joined = jnp.concatenate(
        [projected[0].astype(jnp.bfloat16), projected[1].astype(jnp.bfloat16)], 1
    )
    dt_proj = lax.optimization_barrier(projected[2].astype(jnp.bfloat16))
    conv_taps = jnp.concatenate([conv_x, conv_bc], 1)
    kernel = conv_taps.shape[0] - 1
    rim_rows = passed_along(joined[tok_rows - (kernel - 1) :], "ctx", 1)
    padded = jnp.concatenate([rim_rows, joined], 0)
    conv_sum = conv_taps[kernel]
    for tap_index in range(kernel):
        conv_sum = conv_sum + conv_taps[tap_index] * padded[tap_index : tap_index + tok_rows]
    convolved = jax.nn.silu(conv_sum).astype(jnp.bfloat16)
    x_conv = convolved[:, :x_cols]
    group_all = lax.all_gather(convolved[:, x_cols:], "mp", axis=1, tiled=True)
    heads_dev = dt_weight.shape[1]
    head_size = x_cols // heads_dev
    per_group = HEADS // G
    groups_here = max(1, heads_dev // per_group)
    heads_local = heads_dev // groups_here
    first_group = lax.axis_index("mp") * heads_dev // per_group
    write_all = group_all[:, : G * NS].reshape(tok_rows, G, NS)
    read_all = group_all[:, G * NS :].reshape(tok_rows, G, NS)
    write_here = lax.dynamic_slice_in_dim(write_all, first_group, groups_here, 1)
    read_here = lax.dynamic_slice_in_dim(read_all, first_group, groups_here, 1)
    step_size = jax.nn.softplus(dt_proj.astype(jnp.float32) + dt_bias)
    decay_rate = step_size * jnp.exp(a_log)
    cumulative = jnp.cumsum(decay_rate, 0)
    block_end = cumulative[-1]
    causal = lax.broadcasted_iota(jnp.int32, (tok_rows, tok_rows), 0) >= lax.broadcasted_iota(
        jnp.int32, (tok_rows, tok_rows), 1
    )
    spread = cumulative.T[:, :, None] - cumulative.T[:, None, :]
    decay_mask = jnp.where(causal, jnp.exp(-jnp.where(causal, spread, 0.0)), 0.0)
    scores = jnp.einsum("tgn,sgn->gts", read_here, write_here, preferred_element_type=jnp.float32)
    weights = (
        scores[:, None]
        * decay_mask.reshape(groups_here, heads_local, tok_rows, tok_rows)
        * step_size.T.reshape(groups_here, heads_local, 1, tok_rows)
    ).astype(jnp.bfloat16)
    x_heads = x_conv.reshape(tok_rows, groups_here, heads_local, head_size)
    within_block = jnp.einsum(
        "ghts,sghp->tghp", weights, x_heads, preferred_element_type=jnp.float32
    )
    update = (
        (jnp.exp(-(block_end - cumulative)) * step_size).reshape(
            tok_rows, groups_here, heads_local
        )[..., None]
        * x_heads
    ).astype(jnp.bfloat16)
    contrib = jnp.einsum("sghp,sgn->ghpn", update, write_here, preferred_element_type=jnp.float32)
    carried = entering(jnp.exp(-block_end).reshape(groups_here, heads_local), contrib, "ctx")
    from_before = jnp.exp(-cumulative).reshape(tok_rows, groups_here, heads_local)[
        ..., None
    ] * jnp.einsum("tgn,ghpn->tghp", read_here.astype(jnp.float32), carried, precision=HIGH)
    output_raw = (
        within_block
        + from_before
        + d_skip.reshape(groups_here, heads_local)[None, :, :, None] * x_heads.astype(jnp.float32)
    )
    mean_square = jnp.mean(output_raw * output_raw, -1, keepdims=True)
    normed = (
        output_raw
        * lax.rsqrt(mean_square + 1e-05)
        * norm_gain.reshape(groups_here, heads_local, head_size)
    )
    return (normed.reshape(1, tok_rows, x_cols).astype(jnp.bfloat16), kurtosis)


def solution(mesh):
    return jax.shard_map(
        shards,
        mesh=mesh,
        in_specs=(
            P("dp", "ctx", None),
            P(("dp", "ctx"), "mp"),
            P(("dp", "ctx"), "mp"),
            P(("dp", "ctx"), "mp"),
            P(None, "mp"),
            P(None, "mp"),
            P("mp"),
            P("mp"),
            P("mp"),
            P("mp"),
        ),
        out_specs=(P("dp", "ctx", "mp"), P("mp")),
        check_vma=False,
    )
```

```python
import jax
import jax.numpy as jnp
from jax import lax
from jax.sharding import PartitionSpec as P

ROOT = 64
HEADS = 128
G = 4
NS = 128


HIGH = lax.Precision.HIGHEST


def passed_along(value, axis, steps):
    count = lax.axis_size(axis)
    first, last = (max(0, -steps), min(count, count - steps))
    return lax.ppermute(value, axis, [(source, source + steps) for source in range(first, last)])


def entering(decay, contrib, axis):
    length, place = (lax.axis_size(axis), lax.axis_index(axis))
    lanes = contrib.shape[-1]
    rows = contrib.size // lanes
    tail = jnp.zeros((8, lanes), jnp.float32).at[0, : decay.size].set(decay.reshape(-1))
    flat = jnp.concatenate([contrib.reshape(rows, lanes), tail]).astype(jnp.bfloat16)
    everything = lax.all_gather(flat, axis).astype(jnp.float32)
    states = everything[:, :rows].reshape((length,) + contrib.shape)
    decays = everything[:, rows, : decay.size].reshape((length,) + decay.shape)
    source = lax.broadcasted_iota(jnp.int32, (length, length), 0)
    between = lax.broadcasted_iota(jnp.int32, (length, length), 1)
    inside = jnp.logical_and(between > source, between < place)
    factors = jnp.where(inside[:, :, None, None], decays[None], 1.0)
    weights = jnp.prod(factors, 1)
    weights = jnp.where((source[:, 0] < place)[:, None, None], weights, 0.0)
    return jnp.einsum("jgh,jghpn->ghpn", weights, states, precision=HIGH)


def hadamard_signs(sign_order):
    row_index = lax.broadcasted_iota(jnp.int32, (sign_order, sign_order), 0)
    col_index = lax.broadcasted_iota(jnp.int32, (sign_order, sign_order), 1)
    common = jnp.bitwise_and(row_index, col_index)
    parity = jnp.zeros((sign_order, sign_order), jnp.int32)
    for bit_index in range(sign_order.bit_length() - 1):
        parity = parity + jnp.bitwise_and(jnp.right_shift(common, bit_index), 1)
    return 1.0 - 2.0 * jnp.bitwise_and(parity, 1).astype(jnp.float32)


def kurtosis_from(powers, row_count):
    average = powers[0] / row_count
    second = powers[1] / row_count - average * average
    fourth = (
        powers[3] / row_count
        - 4.0 * average * powers[2] / row_count
        + 6.0 * average * average * powers[1] / row_count
        - 3.0 * average * average * average * average
    )
    return fourth / (second * second + 1e-06)


def shards(
    tokens, x_weight, bc_weight, dt_weight, conv_x, conv_bc, dt_bias, a_log, d_skip, norm_gain
):
    tok_rows = tokens.shape[1]
    model_width = tokens.shape[2]
    signs = hadamard_signs(ROOT)
    blocks = tokens.reshape(tok_rows, ROOT, ROOT)
    first_pass = jnp.einsum(
        "tab,ac->tcb", blocks, signs.astype(jnp.bfloat16), preferred_element_type=jnp.float32
    )
    second = jnp.einsum("tcb,bd->tcd", first_pass, signs, precision=HIGH)
    rotated = (second.reshape(tok_rows, model_width) / ROOT).astype(jnp.bfloat16)
    channel_share = model_width // lax.axis_size("mp")
    own_cols = lax.dynamic_slice_in_dim(
        rotated, lax.axis_index("mp") * channel_share, channel_share, 1
    ).astype(jnp.float32)
    square = own_cols * own_cols
    powers = jnp.stack(
        [
            jnp.sum(own_cols, 0),
            jnp.sum(square, 0),
            jnp.sum(square * own_cols, 0),
            jnp.sum(square * square, 0),
        ]
    )
    row_count = float(tok_rows * lax.axis_size("dp") * lax.axis_size("ctx"))
    totals = lax.psum(lax.psum(powers, "ctx"), "dp")
    totals, rotated = lax.optimization_barrier((totals, rotated))
    kurtosis = kurtosis_from(totals, row_count)
    local_panel = jnp.concatenate([x_weight, bc_weight, dt_weight], 1)
    panel = lax.all_gather(local_panel, "ctx", axis=0, tiled=True)
    seqs = lax.axis_size("dp")
    share = model_width // seqs
    outgoing = rotated.reshape(tok_rows, seqs, share).transpose(1, 0, 2)
    incoming = lax.all_to_all(outgoing, "dp", 0, 0)
    partials = jnp.einsum("kti,io->kto", incoming, panel, preferred_element_type=jnp.float32)
    both = lax.psum_scatter(partials, "dp", scatter_dimension=0, tiled=False)
    x_end = x_weight.shape[1]
    bc_end = x_end + bc_weight.shape[1]
    projected = (both[:, :x_end], both[:, x_end:bc_end], both[:, bc_end:])
    x_cols = x_weight.shape[1]
    joined = jnp.concatenate(
        [projected[0].astype(jnp.bfloat16), projected[1].astype(jnp.bfloat16)], 1
    )
    dt_proj = lax.optimization_barrier(projected[2].astype(jnp.bfloat16))
    conv_taps = jnp.concatenate([conv_x, conv_bc], 1)
    kernel = conv_taps.shape[0] - 1
    rim_rows = passed_along(joined[tok_rows - (kernel - 1) :], "ctx", 1)
    padded = jnp.concatenate([rim_rows, joined], 0)
    conv_sum = conv_taps[kernel]
    for tap_index in range(kernel):
        conv_sum = conv_sum + conv_taps[tap_index] * padded[tap_index : tap_index + tok_rows]
    convolved = jax.nn.silu(conv_sum).astype(jnp.bfloat16)
    x_conv = convolved[:, :x_cols]
    group_all = lax.all_gather(convolved[:, x_cols:], "mp", axis=1, tiled=True)
    heads_dev = dt_weight.shape[1]
    head_size = x_cols // heads_dev
    per_group = HEADS // G
    groups_here = max(1, heads_dev // per_group)
    heads_local = heads_dev // groups_here
    first_group = lax.axis_index("mp") * heads_dev // per_group
    write_all = group_all[:, : G * NS].reshape(tok_rows, G, NS)
    read_all = group_all[:, G * NS :].reshape(tok_rows, G, NS)
    write_here = lax.dynamic_slice_in_dim(write_all, first_group, groups_here, 1)
    read_here = lax.dynamic_slice_in_dim(read_all, first_group, groups_here, 1)
    step_size = jax.nn.softplus(dt_proj.astype(jnp.float32) + dt_bias)
    decay_rate = step_size * jnp.exp(a_log)
    cumulative = jnp.cumsum(decay_rate, 0)
    block_end = cumulative[-1]
    causal = lax.broadcasted_iota(jnp.int32, (tok_rows, tok_rows), 0) >= lax.broadcasted_iota(
        jnp.int32, (tok_rows, tok_rows), 1
    )
    spread = cumulative.T[:, :, None] - cumulative.T[:, None, :]
    decay_mask = jnp.where(causal, jnp.exp(-jnp.where(causal, spread, 0.0)), 0.0)
    scores = jnp.einsum("tgn,sgn->gts", read_here, write_here, preferred_element_type=jnp.float32)
    weights = (
        scores[:, None]
        * decay_mask.reshape(groups_here, heads_local, tok_rows, tok_rows)
        * step_size.T.reshape(groups_here, heads_local, 1, tok_rows)
    ).astype(jnp.bfloat16)
    x_heads = x_conv.reshape(tok_rows, groups_here, heads_local, head_size)
    within_block = jnp.einsum(
        "ghts,sghp->tghp", weights, x_heads, preferred_element_type=jnp.float32
    )
    update = (
        (jnp.exp(-(block_end - cumulative)) * step_size).reshape(
            tok_rows, groups_here, heads_local
        )[..., None]
        * x_heads
    ).astype(jnp.bfloat16)
    contrib = jnp.einsum("sghp,sgn->ghpn", update, write_here, preferred_element_type=jnp.float32)
    carried = entering(jnp.exp(-block_end).reshape(groups_here, heads_local), contrib, "ctx")
    from_before = jnp.exp(-cumulative).reshape(tok_rows, groups_here, heads_local)[
        ..., None
    ] * jnp.einsum("tgn,ghpn->tghp", read_here.astype(jnp.float32), carried, precision=HIGH)
    output_raw = (
        within_block
        + from_before
        + d_skip.reshape(groups_here, heads_local)[None, :, :, None] * x_heads.astype(jnp.float32)
    )
    mean_square = jnp.mean(output_raw * output_raw, -1, keepdims=True)
    normed = (
        output_raw
        * lax.rsqrt(mean_square + 1e-05)
        * norm_gain.reshape(groups_here, heads_local, head_size)
    )
    return (normed.reshape(1, tok_rows, x_cols).astype(jnp.bfloat16), kurtosis)


def solution(mesh):
    return jax.shard_map(
        shards,
        mesh=mesh,
        in_specs=(
            P("dp", "ctx", None),
            P(("dp", "ctx"), "mp"),
            P(("dp", "ctx"), "mp"),
            P(("dp", "ctx"), "mp"),
            P(None, "mp"),
            P(None, "mp"),
            P("mp"),
            P("mp"),
            P("mp"),
            P("mp"),
        ),
        out_specs=(P("dp", "ctx", "mp"), P("mp")),
        check_vma=False,
    )
```

```python
import jax
import jax.numpy as jnp
from jax import lax
from jax.sharding import PartitionSpec as P

ROOT = 64
HEADS = 128
G = 4
NS = 128


HIGH = lax.Precision.HIGHEST


def passed_along(value, axis, steps):
    count = lax.axis_size(axis)
    first, last = (max(0, -steps), min(count, count - steps))
    return lax.ppermute(value, axis, [(source, source + steps) for source in range(first, last)])


def entering(decay, contrib, axis):
    count, place = (lax.axis_size(axis), lax.axis_index(axis))
    lanes = contrib.shape[-1]
    head_rows = contrib.shape[-2]
    heads = decay.size
    chunk = contrib.size // lanes // count
    pieces = contrib.reshape(count, chunk, lanes)
    tail = jnp.zeros((count, 8, lanes), jnp.float32)
    tail = tail.at[:, 0, :heads].set(jnp.broadcast_to(decay.reshape(1, heads), (count, heads)))
    outgoing = jnp.concatenate([pieces, tail], 1).astype(jnp.bfloat16)
    incoming = lax.all_to_all(outgoing, axis, 0, 0).astype(jnp.float32)
    states = incoming[:, :chunk]
    decays = incoming[:, chunk, :heads]
    row_head = (place * chunk + lax.broadcasted_iota(jnp.int32, (chunk, heads), 0)) // head_rows
    pick = row_head == lax.broadcasted_iota(jnp.int32, (chunk, heads), 1)
    row_decay = jnp.sum(jnp.where(pick[None], decays[:, None, :], 0.0), -1)
    target = lax.broadcasted_iota(jnp.int32, (count, count, count), 0)
    source = lax.broadcasted_iota(jnp.int32, (count, count, count), 1)
    between = lax.broadcasted_iota(jnp.int32, (count, count, count), 2)
    inside = jnp.logical_and(between > source, between < target)
    factors = jnp.where(inside[..., None], row_decay[None, None], 1.0)
    weights = jnp.prod(factors, 2)
    weights = jnp.where((source[:, :, 0] < target[:, :, 0])[..., None], weights, 0.0)
    carried = jnp.einsum("kjr,jrl->krl", weights, states, precision=HIGH)
    returned = lax.all_to_all(carried, axis, 0, 0)
    return returned.reshape(contrib.shape)


def hadamard_signs(sign_order):
    row_index = lax.broadcasted_iota(jnp.int32, (sign_order, sign_order), 0)
    col_index = lax.broadcasted_iota(jnp.int32, (sign_order, sign_order), 1)
    common = jnp.bitwise_and(row_index, col_index)
    parity = jnp.zeros((sign_order, sign_order), jnp.int32)
    for bit_index in range(sign_order.bit_length() - 1):
        parity = parity + jnp.bitwise_and(jnp.right_shift(common, bit_index), 1)
    return 1.0 - 2.0 * jnp.bitwise_and(parity, 1).astype(jnp.float32)


def kurtosis_from(powers, row_count):
    average = powers[0] / row_count
    second = powers[1] / row_count - average * average
    fourth = (
        powers[3] / row_count
        - 4.0 * average * powers[2] / row_count
        + 6.0 * average * average * powers[1] / row_count
        - 3.0 * average * average * average * average
    )
    return fourth / (second * second + 1e-06)


def shards(
    tokens, x_weight, bc_weight, dt_weight, conv_x, conv_bc, dt_bias, a_log, d_skip, norm_gain
):
    tok_rows = tokens.shape[1]
    model_width = tokens.shape[2]
    signs = hadamard_signs(ROOT)
    blocks = tokens.reshape(tok_rows, ROOT, ROOT)
    first_pass = jnp.einsum(
        "tab,ac->tcb", blocks, signs.astype(jnp.bfloat16), preferred_element_type=jnp.float32
    )
    second = jnp.einsum("tcb,bd->tcd", first_pass, signs, precision=HIGH)
    rotated = (second.reshape(tok_rows, model_width) / ROOT).astype(jnp.bfloat16)
    channel_share = model_width // lax.axis_size("mp")
    own_cols = lax.dynamic_slice_in_dim(
        rotated, lax.axis_index("mp") * channel_share, channel_share, 1
    ).astype(jnp.float32)
    square = own_cols * own_cols
    powers = jnp.stack(
        [
            jnp.sum(own_cols, 0),
            jnp.sum(square, 0),
            jnp.sum(square * own_cols, 0),
            jnp.sum(square * square, 0),
        ]
    )
    row_count = float(tok_rows * lax.axis_size("dp") * lax.axis_size("ctx"))
    totals = lax.psum(lax.psum(powers, "ctx"), "dp")
    totals, rotated = lax.optimization_barrier((totals, rotated))
    kurtosis = kurtosis_from(totals, row_count)
    local_panel = jnp.concatenate([x_weight, bc_weight, dt_weight], 1)
    panel = lax.all_gather(local_panel, "ctx", axis=0, tiled=True)
    seqs = lax.axis_size("dp")
    share = model_width // seqs
    rim = 8
    earlier = passed_along(rotated[tok_rows - rim :], "ctx", 1)
    extended = jnp.concatenate([earlier, rotated], 0)
    outgoing = extended.reshape(tok_rows + rim, seqs, share).transpose(1, 0, 2)
    incoming = lax.all_to_all(outgoing, "dp", 0, 0)
    partials = jnp.einsum("kti,io->kto", incoming, panel, preferred_element_type=jnp.float32)
    both_ext = lax.psum_scatter(partials, "dp", scatter_dimension=0, tiled=False)
    both = both_ext[rim:]
    x_end = x_weight.shape[1]
    bc_end = x_end + bc_weight.shape[1]
    projected = (both[:, :x_end], both[:, x_end:bc_end], both[:, bc_end:])
    x_cols = x_weight.shape[1]
    joined_ext = both_ext[:, :bc_end].astype(jnp.bfloat16)
    dt_proj = lax.optimization_barrier(projected[2].astype(jnp.bfloat16))
    conv_taps = jnp.concatenate([conv_x, conv_bc], 1)
    kernel = conv_taps.shape[0] - 1
    padded = joined_ext[rim - (kernel - 1) :]
    conv_sum = conv_taps[kernel]
    for tap_index in range(kernel):
        conv_sum = conv_sum + conv_taps[tap_index] * padded[tap_index : tap_index + tok_rows]
    convolved = jax.nn.silu(conv_sum).astype(jnp.bfloat16)
    x_conv = convolved[:, :x_cols]
    heads_dev = dt_weight.shape[1]
    head_size = x_cols // heads_dev
    per_group = HEADS // G
    groups_here = max(1, heads_dev // per_group)
    heads_local = heads_dev // groups_here
    first_group = lax.axis_index("mp") * heads_dev // per_group
    bc_own = convolved[:, x_cols:]
    mp_count = lax.axis_size("mp")
    if bc_own.shape[1] == NS and mp_count == 2 * G and groups_here == 1:
        owner = [m * heads_dev // per_group for m in range(mp_count)]
        odd_first = [(owner[m] if m % 2 == 0 else G + owner[m], m) for m in range(mp_count)]
        even_first = [(G + owner[m] if m % 2 == 0 else owner[m], m) for m in range(mp_count)]
        got_a = lax.ppermute(bc_own, "mp", odd_first)
        got_b = lax.ppermute(bc_own, "mp", even_first)
        even = lax.axis_index("mp") % 2 == 0
        write_here = jnp.where(even, got_a, got_b).reshape(tok_rows, 1, NS)
        read_here = jnp.where(even, got_b, got_a).reshape(tok_rows, 1, NS)
    else:
        group_all = lax.all_gather(bc_own, "mp", axis=1, tiled=True)
        write_all = group_all[:, : G * NS].reshape(tok_rows, G, NS)
        read_all = group_all[:, G * NS :].reshape(tok_rows, G, NS)
        write_here = lax.dynamic_slice_in_dim(write_all, first_group, groups_here, 1)
        read_here = lax.dynamic_slice_in_dim(read_all, first_group, groups_here, 1)
    step_size = jax.nn.softplus(dt_proj.astype(jnp.float32) + dt_bias)
    decay_rate = step_size * jnp.exp(a_log)
    cumulative = jnp.cumsum(decay_rate, 0)
    block_end = cumulative[-1]
    causal = lax.broadcasted_iota(jnp.int32, (tok_rows, tok_rows), 0) >= lax.broadcasted_iota(
        jnp.int32, (tok_rows, tok_rows), 1
    )
    spread = cumulative.T[:, :, None] - cumulative.T[:, None, :]
    decay_mask = jnp.where(causal, jnp.exp(-jnp.where(causal, spread, 0.0)), 0.0)
    scores = jnp.einsum("tgn,sgn->gts", read_here, write_here, preferred_element_type=jnp.float32)
    weights = (
        scores[:, None]
        * decay_mask.reshape(groups_here, heads_local, tok_rows, tok_rows)
        * step_size.T.reshape(groups_here, heads_local, 1, tok_rows)
    ).astype(jnp.bfloat16)
    x_heads = x_conv.reshape(tok_rows, groups_here, heads_local, head_size)
    within_block = jnp.einsum(
        "ghts,sghp->tghp", weights, x_heads, preferred_element_type=jnp.float32
    )
    update = (
        (jnp.exp(-(block_end - cumulative)) * step_size).reshape(
            tok_rows, groups_here, heads_local
        )[..., None]
        * x_heads
    ).astype(jnp.bfloat16)
    contrib = jnp.einsum("sghp,sgn->ghpn", update, write_here, preferred_element_type=jnp.float32)
    carried = entering(jnp.exp(-block_end).reshape(groups_here, heads_local), contrib, "ctx")
    from_before = jnp.exp(-cumulative).reshape(tok_rows, groups_here, heads_local)[
        ..., None
    ] * jnp.einsum("tgn,ghpn->tghp", read_here.astype(jnp.float32), carried, precision=HIGH)
    output_raw = (
        within_block
        + from_before
        + d_skip.reshape(groups_here, heads_local)[None, :, :, None] * x_heads.astype(jnp.float32)
    )
    mean_square = jnp.mean(output_raw * output_raw, -1, keepdims=True)
    normed = (
        output_raw
        * lax.rsqrt(mean_square + 1e-05)
        * norm_gain.reshape(groups_here, heads_local, head_size)
    )
    return (normed.reshape(1, tok_rows, x_cols).astype(jnp.bfloat16), kurtosis)


def solution(mesh):
    return jax.shard_map(
        shards,
        mesh=mesh,
        in_specs=(
            P("dp", "ctx", None),
            P(("dp", "ctx"), "mp"),
            P(("dp", "ctx"), "mp"),
            P(("dp", "ctx"), "mp"),
            P(None, "mp"),
            P(None, "mp"),
            P("mp"),
            P("mp"),
            P("mp"),
            P("mp"),
        ),
        out_specs=(P("dp", "ctx", "mp"), P("mp")),
        check_vma=False,
    )
```

```python
import jax
import jax.numpy as jnp
from jax import lax
from jax.sharding import PartitionSpec as P

ROOT = 64
HEADS = 128
G = 4
NS = 128


HIGH = lax.Precision.HIGHEST


def passed_along(value, axis, steps):
    count = lax.axis_size(axis)
    first, last = (max(0, -steps), min(count, count - steps))
    return lax.ppermute(value, axis, [(source, source + steps) for source in range(first, last)])


def entering(decay, contrib, axis):
    count, place = (lax.axis_size(axis), lax.axis_index(axis))
    lanes = contrib.shape[-1]
    head_rows = contrib.shape[-2]
    heads = decay.size
    chunk = contrib.size // lanes // count
    pieces = contrib.reshape(count, chunk, lanes)
    tail = jnp.zeros((count, 8, lanes), jnp.float32)
    tail = tail.at[:, 0, :heads].set(jnp.broadcast_to(decay.reshape(1, heads), (count, heads)))
    outgoing = jnp.concatenate([pieces, tail], 1).astype(jnp.bfloat16)
    incoming = lax.all_to_all(outgoing, axis, 0, 0).astype(jnp.float32)
    states = incoming[:, :chunk]
    decays = incoming[:, chunk, :heads]
    row_head = (place * chunk + lax.broadcasted_iota(jnp.int32, (chunk, heads), 0)) // head_rows
    pick = row_head == lax.broadcasted_iota(jnp.int32, (chunk, heads), 1)
    row_decay = jnp.sum(jnp.where(pick[None], decays[:, None, :], 0.0), -1)
    target = lax.broadcasted_iota(jnp.int32, (count, count, count), 0)
    source = lax.broadcasted_iota(jnp.int32, (count, count, count), 1)
    between = lax.broadcasted_iota(jnp.int32, (count, count, count), 2)
    inside = jnp.logical_and(between > source, between < target)
    factors = jnp.where(inside[..., None], row_decay[None, None], 1.0)
    weights = jnp.prod(factors, 2)
    weights = jnp.where((source[:, :, 0] < target[:, :, 0])[..., None], weights, 0.0)
    carried = jnp.einsum("kjr,jrl->krl", weights, states, precision=HIGH)
    returned = lax.all_to_all(carried.astype(jnp.bfloat16), axis, 0, 0)
    return returned.astype(jnp.float32).reshape(contrib.shape)


def hadamard_signs(sign_order):
    row_index = lax.broadcasted_iota(jnp.int32, (sign_order, sign_order), 0)
    col_index = lax.broadcasted_iota(jnp.int32, (sign_order, sign_order), 1)
    common = jnp.bitwise_and(row_index, col_index)
    parity = jnp.zeros((sign_order, sign_order), jnp.int32)
    for bit_index in range(sign_order.bit_length() - 1):
        parity = parity + jnp.bitwise_and(jnp.right_shift(common, bit_index), 1)
    return 1.0 - 2.0 * jnp.bitwise_and(parity, 1).astype(jnp.float32)


def kurtosis_from(powers, row_count):
    average = powers[0] / row_count
    second = powers[1] / row_count - average * average
    fourth = (
        powers[3] / row_count
        - 4.0 * average * powers[2] / row_count
        + 6.0 * average * average * powers[1] / row_count
        - 3.0 * average * average * average * average
    )
    return fourth / (second * second + 1e-06)


def shards(
    tokens, x_weight, bc_weight, dt_weight, conv_x, conv_bc, dt_bias, a_log, d_skip, norm_gain
):
    tok_rows = tokens.shape[1]
    model_width = tokens.shape[2]
    signs = hadamard_signs(ROOT)
    blocks = tokens.reshape(tok_rows, ROOT, ROOT)
    first_pass = jnp.einsum(
        "tab,ac->tcb", blocks, signs.astype(jnp.bfloat16), preferred_element_type=jnp.float32
    )
    second = jnp.einsum("tcb,bd->tcd", first_pass, signs, precision=HIGH)
    rotated = (second.reshape(tok_rows, model_width) / ROOT).astype(jnp.bfloat16)
    channel_share = model_width // lax.axis_size("mp")
    own_cols = lax.dynamic_slice_in_dim(
        rotated, lax.axis_index("mp") * channel_share, channel_share, 1
    ).astype(jnp.float32)
    square = own_cols * own_cols
    powers = jnp.stack(
        [
            jnp.sum(own_cols, 0),
            jnp.sum(square, 0),
            jnp.sum(square * own_cols, 0),
            jnp.sum(square * square, 0),
        ]
    )
    row_count = float(tok_rows * lax.axis_size("dp") * lax.axis_size("ctx"))
    totals = lax.psum(lax.psum(powers, "ctx"), "dp")
    totals, rotated = lax.optimization_barrier((totals, rotated))
    kurtosis = kurtosis_from(totals, row_count)
    local_panel = jnp.concatenate([x_weight, bc_weight, dt_weight], 1)
    panel = lax.all_gather(local_panel, "ctx", axis=0, tiled=True)
    seqs = lax.axis_size("dp")
    share = model_width // seqs
    rim = 8
    earlier = passed_along(rotated[tok_rows - rim :], "ctx", 1)
    extended = jnp.concatenate([earlier, rotated], 0)
    outgoing = extended.reshape(tok_rows + rim, seqs, share).transpose(1, 0, 2)
    incoming = lax.all_to_all(outgoing, "dp", 0, 0)
    partials = jnp.einsum("kti,io->kto", incoming, panel, preferred_element_type=jnp.float32)
    returned = lax.all_to_all(partials.astype(jnp.bfloat16), "dp", 0, 0)
    both_ext = jnp.sum(returned.astype(jnp.float32), 0)
    both = both_ext[rim:]
    x_end = x_weight.shape[1]
    bc_end = x_end + bc_weight.shape[1]
    projected = (both[:, :x_end], both[:, x_end:bc_end], both[:, bc_end:])
    x_cols = x_weight.shape[1]
    joined_ext = both_ext[:, :bc_end].astype(jnp.bfloat16)
    dt_proj = lax.optimization_barrier(projected[2].astype(jnp.bfloat16))
    conv_taps = jnp.concatenate([conv_x, conv_bc], 1)
    kernel = conv_taps.shape[0] - 1
    padded = joined_ext[rim - (kernel - 1) :]
    conv_sum = conv_taps[kernel]
    for tap_index in range(kernel):
        conv_sum = conv_sum + conv_taps[tap_index] * padded[tap_index : tap_index + tok_rows]
    convolved = jax.nn.silu(conv_sum).astype(jnp.bfloat16)
    x_conv = convolved[:, :x_cols]
    heads_dev = dt_weight.shape[1]
    head_size = x_cols // heads_dev
    per_group = HEADS // G
    groups_here = max(1, heads_dev // per_group)
    heads_local = heads_dev // groups_here
    first_group = lax.axis_index("mp") * heads_dev // per_group
    bc_own = convolved[:, x_cols:]
    mp_count = lax.axis_size("mp")
    if bc_own.shape[1] == NS and mp_count == 2 * G and groups_here == 1:
        owner = [m * heads_dev // per_group for m in range(mp_count)]
        odd_first = [(owner[m] if m % 2 == 0 else G + owner[m], m) for m in range(mp_count)]
        even_first = [(G + owner[m] if m % 2 == 0 else owner[m], m) for m in range(mp_count)]
        got_a = lax.ppermute(bc_own, "mp", odd_first)
        got_b = lax.ppermute(bc_own, "mp", even_first)
        even = lax.axis_index("mp") % 2 == 0
        write_here = jnp.where(even, got_a, got_b).reshape(tok_rows, 1, NS)
        read_here = jnp.where(even, got_b, got_a).reshape(tok_rows, 1, NS)
    else:
        group_all = lax.all_gather(bc_own, "mp", axis=1, tiled=True)
        write_all = group_all[:, : G * NS].reshape(tok_rows, G, NS)
        read_all = group_all[:, G * NS :].reshape(tok_rows, G, NS)
        write_here = lax.dynamic_slice_in_dim(write_all, first_group, groups_here, 1)
        read_here = lax.dynamic_slice_in_dim(read_all, first_group, groups_here, 1)
    step_size = jax.nn.softplus(dt_proj.astype(jnp.float32) + dt_bias)
    decay_rate = step_size * jnp.exp(a_log)
    cumulative = jnp.cumsum(decay_rate, 0)
    block_end = cumulative[-1]
    causal = lax.broadcasted_iota(jnp.int32, (tok_rows, tok_rows), 0) >= lax.broadcasted_iota(
        jnp.int32, (tok_rows, tok_rows), 1
    )
    spread = cumulative.T[:, :, None] - cumulative.T[:, None, :]
    decay_mask = jnp.where(causal, jnp.exp(-jnp.where(causal, spread, 0.0)), 0.0)
    scores = jnp.einsum("tgn,sgn->gts", read_here, write_here, preferred_element_type=jnp.float32)
    weights = (
        scores[:, None]
        * decay_mask.reshape(groups_here, heads_local, tok_rows, tok_rows)
        * step_size.T.reshape(groups_here, heads_local, 1, tok_rows)
    ).astype(jnp.bfloat16)
    x_heads = x_conv.reshape(tok_rows, groups_here, heads_local, head_size)
    within_block = jnp.einsum(
        "ghts,sghp->tghp", weights, x_heads, preferred_element_type=jnp.float32
    )
    update = (
        (jnp.exp(-(block_end - cumulative)) * step_size).reshape(
            tok_rows, groups_here, heads_local
        )[..., None]
        * x_heads
    ).astype(jnp.bfloat16)
    contrib = jnp.einsum("sghp,sgn->ghpn", update, write_here, preferred_element_type=jnp.float32)
    carried = entering(jnp.exp(-block_end).reshape(groups_here, heads_local), contrib, "ctx")
    from_before = jnp.exp(-cumulative).reshape(tok_rows, groups_here, heads_local)[
        ..., None
    ] * jnp.einsum("tgn,ghpn->tghp", read_here.astype(jnp.float32), carried, precision=HIGH)
    output_raw = (
        within_block
        + from_before
        + d_skip.reshape(groups_here, heads_local)[None, :, :, None] * x_heads.astype(jnp.float32)
    )
    mean_square = jnp.mean(output_raw * output_raw, -1, keepdims=True)
    normed = (
        output_raw
        * lax.rsqrt(mean_square + 1e-05)
        * norm_gain.reshape(groups_here, heads_local, head_size)
    )
    return (normed.reshape(1, tok_rows, x_cols).astype(jnp.bfloat16), kurtosis)


def solution(mesh):
    return jax.shard_map(
        shards,
        mesh=mesh,
        in_specs=(
            P("dp", "ctx", None),
            P(("dp", "ctx"), "mp"),
            P(("dp", "ctx"), "mp"),
            P(("dp", "ctx"), "mp"),
            P(None, "mp"),
            P(None, "mp"),
            P("mp"),
            P("mp"),
            P("mp"),
            P("mp"),
        ),
        out_specs=(P("dp", "ctx", "mp"), P("mp")),
        check_vma=False,
    )
```

```python
import jax
import jax.numpy as jnp
from jax import lax
from jax.sharding import PartitionSpec as P

ROOT = 64
HEADS = 128
G = 4
NS = 128


HIGH = lax.Precision.HIGHEST


def passed_along(value, axis, steps):
    count = lax.axis_size(axis)
    first, last = (max(0, -steps), min(count, count - steps))
    return lax.ppermute(value, axis, [(source, source + steps) for source in range(first, last)])


def ring_gather(block, axis):
    count, place = (lax.axis_size(axis), lax.axis_index(axis))
    ahead = [(source, (source + 1) % count) for source in range(count)]
    behind = [(source, (source - 1) % count) for source in range(count)]
    back_steps = count // 2
    fore_steps = count - 1 - back_steps
    from_behind, from_ahead = ([], [])
    moving_back, moving_fore = (block, block)
    for step in range(back_steps):
        moving_back = lax.ppermute(moving_back, axis, ahead)
        from_behind.append(moving_back)
        if step < fore_steps:
            moving_fore = lax.ppermute(moving_fore, axis, behind)
            from_ahead.append(moving_fore)
    ordered = from_behind[::-1] + [block] + from_ahead
    stacked = jnp.concatenate(ordered, 0)
    rows = block.shape[0]
    return jnp.roll(stacked, (place - back_steps) * rows, 0)


def entering(decay, contrib, axis):
    count, place = (lax.axis_size(axis), lax.axis_index(axis))
    lanes = contrib.shape[-1]
    head_rows = contrib.shape[-2]
    heads = decay.size
    chunk = contrib.size // lanes // count
    pieces = contrib.reshape(count, chunk, lanes)
    tail = jnp.zeros((count, 8, lanes), jnp.float32)
    tail = tail.at[:, 0, :heads].set(jnp.broadcast_to(decay.reshape(1, heads), (count, heads)))
    outgoing = jnp.concatenate([pieces, tail], 1).astype(jnp.bfloat16)
    incoming = lax.all_to_all(outgoing, axis, 0, 0).astype(jnp.float32)
    states = incoming[:, :chunk]
    decays = incoming[:, chunk, :heads]
    row_head = (place * chunk + lax.broadcasted_iota(jnp.int32, (chunk, heads), 0)) // head_rows
    pick = row_head == lax.broadcasted_iota(jnp.int32, (chunk, heads), 1)
    row_decay = jnp.sum(jnp.where(pick[None], decays[:, None, :], 0.0), -1)
    target = lax.broadcasted_iota(jnp.int32, (count, count, count), 0)
    source = lax.broadcasted_iota(jnp.int32, (count, count, count), 1)
    between = lax.broadcasted_iota(jnp.int32, (count, count, count), 2)
    inside = jnp.logical_and(between > source, between < target)
    factors = jnp.where(inside[..., None], row_decay[None, None], 1.0)
    weights = jnp.prod(factors, 2)
    weights = jnp.where((source[:, :, 0] < target[:, :, 0])[..., None], weights, 0.0)
    carried = jnp.einsum("kjr,jrl->krl", weights, states, precision=HIGH)
    returned = lax.all_to_all(carried.astype(jnp.bfloat16), axis, 0, 0)
    return returned.astype(jnp.float32).reshape(contrib.shape)


def hadamard_signs(sign_order):
    row_index = lax.broadcasted_iota(jnp.int32, (sign_order, sign_order), 0)
    col_index = lax.broadcasted_iota(jnp.int32, (sign_order, sign_order), 1)
    common = jnp.bitwise_and(row_index, col_index)
    parity = jnp.zeros((sign_order, sign_order), jnp.int32)
    for bit_index in range(sign_order.bit_length() - 1):
        parity = parity + jnp.bitwise_and(jnp.right_shift(common, bit_index), 1)
    return 1.0 - 2.0 * jnp.bitwise_and(parity, 1).astype(jnp.float32)


def kurtosis_from(powers, row_count):
    average = powers[0] / row_count
    second = powers[1] / row_count - average * average
    fourth = (
        powers[3] / row_count
        - 4.0 * average * powers[2] / row_count
        + 6.0 * average * average * powers[1] / row_count
        - 3.0 * average * average * average * average
    )
    return fourth / (second * second + 1e-06)


def shards(
    tokens, x_weight, bc_weight, dt_weight, conv_x, conv_bc, dt_bias, a_log, d_skip, norm_gain
):
    tok_rows = tokens.shape[1]
    model_width = tokens.shape[2]
    signs = hadamard_signs(ROOT)
    blocks = tokens.reshape(tok_rows, ROOT, ROOT)
    first_pass = jnp.einsum(
        "tab,ac->tcb", blocks, signs.astype(jnp.bfloat16), preferred_element_type=jnp.float32
    )
    second = jnp.einsum("tcb,bd->tcd", first_pass, signs, precision=HIGH)
    rotated = (second.reshape(tok_rows, model_width) / ROOT).astype(jnp.bfloat16)
    channel_share = model_width // lax.axis_size("mp")
    own_cols = lax.dynamic_slice_in_dim(
        rotated, lax.axis_index("mp") * channel_share, channel_share, 1
    ).astype(jnp.float32)
    square = own_cols * own_cols
    powers = jnp.stack(
        [
            jnp.sum(own_cols, 0),
            jnp.sum(square, 0),
            jnp.sum(square * own_cols, 0),
            jnp.sum(square * square, 0),
        ]
    )
    row_count = float(tok_rows * lax.axis_size("dp") * lax.axis_size("ctx"))
    local_panel = jnp.concatenate([x_weight, bc_weight, dt_weight], 1)
    panel = ring_gather(local_panel, "ctx")
    seqs = lax.axis_size("dp")
    share = model_width // seqs
    rim = 8
    earlier = passed_along(rotated[tok_rows - rim :], "ctx", 1)
    extended = jnp.concatenate([earlier, rotated], 0)
    outgoing = extended.reshape(tok_rows + rim, seqs, share).transpose(1, 0, 2)
    incoming = lax.all_to_all(outgoing, "dp", 0, 0)
    partials = jnp.einsum("kti,io->kto", incoming, panel, preferred_element_type=jnp.float32)
    returned = lax.all_to_all(partials.astype(jnp.bfloat16), "dp", 0, 0)
    both_ext = jnp.sum(returned.astype(jnp.float32), 0)
    both = both_ext[rim:]
    x_end = x_weight.shape[1]
    bc_end = x_end + bc_weight.shape[1]
    projected = (both[:, :x_end], both[:, x_end:bc_end], both[:, bc_end:])
    x_cols = x_weight.shape[1]
    joined_ext = both_ext[:, :bc_end].astype(jnp.bfloat16)
    dt_proj = lax.optimization_barrier(projected[2].astype(jnp.bfloat16))
    conv_taps = jnp.concatenate([conv_x, conv_bc], 1)
    kernel = conv_taps.shape[0] - 1
    padded = joined_ext[rim - (kernel - 1) :]
    conv_sum = conv_taps[kernel]
    for tap_index in range(kernel):
        conv_sum = conv_sum + conv_taps[tap_index] * padded[tap_index : tap_index + tok_rows]
    convolved = jax.nn.silu(conv_sum).astype(jnp.bfloat16)
    x_conv = convolved[:, :x_cols]
    heads_dev = dt_weight.shape[1]
    head_size = x_cols // heads_dev
    per_group = HEADS // G
    groups_here = max(1, heads_dev // per_group)
    heads_local = heads_dev // groups_here
    first_group = lax.axis_index("mp") * heads_dev // per_group
    bc_own = convolved[:, x_cols:]
    mp_count = lax.axis_size("mp")
    if bc_own.shape[1] == NS and mp_count == 2 * G and groups_here == 1:
        owner = [m * heads_dev // per_group for m in range(mp_count)]
        odd_first = [(owner[m] if m % 2 == 0 else G + owner[m], m) for m in range(mp_count)]
        even_first = [(G + owner[m] if m % 2 == 0 else owner[m], m) for m in range(mp_count)]
        got_a = lax.ppermute(bc_own, "mp", odd_first)
        got_b = lax.ppermute(bc_own, "mp", even_first)
        even = lax.axis_index("mp") % 2 == 0
        write_here = jnp.where(even, got_a, got_b).reshape(tok_rows, 1, NS)
        read_here = jnp.where(even, got_b, got_a).reshape(tok_rows, 1, NS)
    else:
        group_all = lax.all_gather(bc_own, "mp", axis=1, tiled=True)
        write_all = group_all[:, : G * NS].reshape(tok_rows, G, NS)
        read_all = group_all[:, G * NS :].reshape(tok_rows, G, NS)
        write_here = lax.dynamic_slice_in_dim(write_all, first_group, groups_here, 1)
        read_here = lax.dynamic_slice_in_dim(read_all, first_group, groups_here, 1)
    step_size = jax.nn.softplus(dt_proj.astype(jnp.float32) + dt_bias)
    decay_rate = step_size * jnp.exp(a_log)
    cumulative = jnp.cumsum(decay_rate, 0)
    block_end = cumulative[-1]
    causal = lax.broadcasted_iota(jnp.int32, (tok_rows, tok_rows), 0) >= lax.broadcasted_iota(
        jnp.int32, (tok_rows, tok_rows), 1
    )
    spread = cumulative.T[:, :, None] - cumulative.T[:, None, :]
    decay_mask = jnp.where(causal, jnp.exp(-jnp.where(causal, spread, 0.0)), 0.0)
    scores = jnp.einsum("tgn,sgn->gts", read_here, write_here, preferred_element_type=jnp.float32)
    weights = (
        scores[:, None]
        * decay_mask.reshape(groups_here, heads_local, tok_rows, tok_rows)
        * step_size.T.reshape(groups_here, heads_local, 1, tok_rows)
    ).astype(jnp.bfloat16)
    x_heads = x_conv.reshape(tok_rows, groups_here, heads_local, head_size)
    within_block = jnp.einsum(
        "ghts,sghp->tghp", weights, x_heads, preferred_element_type=jnp.float32
    )
    update = (
        (jnp.exp(-(block_end - cumulative)) * step_size).reshape(
            tok_rows, groups_here, heads_local
        )[..., None]
        * x_heads
    ).astype(jnp.bfloat16)
    contrib = jnp.einsum("sghp,sgn->ghpn", update, write_here, preferred_element_type=jnp.float32)
    powers, contrib = lax.optimization_barrier((powers, contrib))
    totals = lax.psum(lax.psum(powers, "ctx"), "dp")
    kurtosis = kurtosis_from(totals, row_count)
    carried = entering(jnp.exp(-block_end).reshape(groups_here, heads_local), contrib, "ctx")
    from_before = jnp.exp(-cumulative).reshape(tok_rows, groups_here, heads_local)[
        ..., None
    ] * jnp.einsum("tgn,ghpn->tghp", read_here.astype(jnp.float32), carried, precision=HIGH)
    output_raw = (
        within_block
        + from_before
        + d_skip.reshape(groups_here, heads_local)[None, :, :, None] * x_heads.astype(jnp.float32)
    )
    mean_square = jnp.mean(output_raw * output_raw, -1, keepdims=True)
    normed = (
        output_raw
        * lax.rsqrt(mean_square + 1e-05)
        * norm_gain.reshape(groups_here, heads_local, head_size)
    )
    return (normed.reshape(1, tok_rows, x_cols).astype(jnp.bfloat16), kurtosis)


def solution(mesh):
    return jax.shard_map(
        shards,
        mesh=mesh,
        in_specs=(
            P("dp", "ctx", None),
            P(("dp", "ctx"), "mp"),
            P(("dp", "ctx"), "mp"),
            P(("dp", "ctx"), "mp"),
            P(None, "mp"),
            P(None, "mp"),
            P("mp"),
            P("mp"),
            P("mp"),
            P("mp"),
        ),
        out_specs=(P("dp", "ctx", "mp"), P("mp")),
        check_vma=False,
    )
```

```python
import jax
import jax.numpy as jnp
from jax import lax
from jax.sharding import PartitionSpec as P

ROOT = 64
HEADS = 128
G = 4
NS = 128


HIGH = lax.Precision.HIGHEST


def passed_along(value, axis, steps):
    count = lax.axis_size(axis)
    first, last = (max(0, -steps), min(count, count - steps))
    return lax.ppermute(value, axis, [(source, source + steps) for source in range(first, last)])


def entering(decay, contrib, axis):
    count, place = (lax.axis_size(axis), lax.axis_index(axis))
    lanes = contrib.shape[-1]
    head_rows = contrib.shape[-2]
    heads = decay.size
    chunk = contrib.size // lanes // count
    pieces = contrib.reshape(count, chunk, lanes)
    tail = jnp.zeros((count, 8, lanes), jnp.float32)
    tail = tail.at[:, 0, :heads].set(jnp.broadcast_to(decay.reshape(1, heads), (count, heads)))
    outgoing = jnp.concatenate([pieces, tail], 1).astype(jnp.bfloat16)
    incoming = lax.all_to_all(outgoing, axis, 0, 0).astype(jnp.float32)
    states = incoming[:, :chunk]
    decays = incoming[:, chunk, :heads]
    row_head = (place * chunk + lax.broadcasted_iota(jnp.int32, (chunk, heads), 0)) // head_rows
    pick = row_head == lax.broadcasted_iota(jnp.int32, (chunk, heads), 1)
    row_decay = jnp.sum(jnp.where(pick[None], decays[:, None, :], 0.0), -1)
    target = lax.broadcasted_iota(jnp.int32, (count, count, count), 0)
    source = lax.broadcasted_iota(jnp.int32, (count, count, count), 1)
    between = lax.broadcasted_iota(jnp.int32, (count, count, count), 2)
    inside = jnp.logical_and(between > source, between < target)
    factors = jnp.where(inside[..., None], row_decay[None, None], 1.0)
    weights = jnp.prod(factors, 2)
    weights = jnp.where((source[:, :, 0] < target[:, :, 0])[..., None], weights, 0.0)
    carried = jnp.einsum("kjr,jrl->krl", weights, states, precision=HIGH)
    returned = lax.all_to_all(carried.astype(jnp.bfloat16), axis, 0, 0)
    return returned.astype(jnp.float32).reshape(contrib.shape)


def hadamard_signs(sign_order):
    row_index = lax.broadcasted_iota(jnp.int32, (sign_order, sign_order), 0)
    col_index = lax.broadcasted_iota(jnp.int32, (sign_order, sign_order), 1)
    common = jnp.bitwise_and(row_index, col_index)
    parity = jnp.zeros((sign_order, sign_order), jnp.int32)
    for bit_index in range(sign_order.bit_length() - 1):
        parity = parity + jnp.bitwise_and(jnp.right_shift(common, bit_index), 1)
    return 1.0 - 2.0 * jnp.bitwise_and(parity, 1).astype(jnp.float32)


def kurtosis_from(powers, row_count):
    average = powers[0] / row_count
    second = powers[1] / row_count - average * average
    fourth = (
        powers[3] / row_count
        - 4.0 * average * powers[2] / row_count
        + 6.0 * average * average * powers[1] / row_count
        - 3.0 * average * average * average * average
    )
    return fourth / (second * second + 1e-06)


def shards(
    tokens, x_weight, bc_weight, dt_weight, conv_x, conv_bc, dt_bias, a_log, d_skip, norm_gain
):
    tok_rows = tokens.shape[1]
    model_width = tokens.shape[2]
    signs = hadamard_signs(ROOT)
    blocks = tokens.reshape(tok_rows, ROOT, ROOT)
    first_pass = jnp.einsum(
        "tab,ac->tcb", blocks, signs.astype(jnp.bfloat16), preferred_element_type=jnp.float32
    )
    second = jnp.einsum("tcb,bd->tcd", first_pass, signs, precision=HIGH)
    rotated = (second.reshape(tok_rows, model_width) / ROOT).astype(jnp.bfloat16)
    channel_share = model_width // lax.axis_size("mp")
    own_cols = lax.dynamic_slice_in_dim(
        rotated, lax.axis_index("mp") * channel_share, channel_share, 1
    ).astype(jnp.float32)
    square = own_cols * own_cols
    powers = jnp.stack(
        [
            jnp.sum(own_cols, 0),
            jnp.sum(square, 0),
            jnp.sum(square * own_cols, 0),
            jnp.sum(square * square, 0),
        ]
    )
    row_count = float(tok_rows * lax.axis_size("dp") * lax.axis_size("ctx"))
    totals = lax.psum(lax.psum(powers, "ctx"), "dp")
    totals, rotated = lax.optimization_barrier((totals, rotated))
    kurtosis = kurtosis_from(totals, row_count)
    local_panel = jnp.concatenate([x_weight, bc_weight, dt_weight], 1)
    panel = lax.all_gather(local_panel, "ctx", axis=0, tiled=True)
    seqs = lax.axis_size("dp")
    share = model_width // seqs
    rim = 8
    earlier = passed_along(rotated[tok_rows - rim :], "ctx", 1)
    extended = jnp.concatenate([earlier, rotated], 0)
    outgoing = extended.reshape(tok_rows + rim, seqs, share).transpose(1, 0, 2)
    incoming = lax.all_to_all(outgoing, "dp", 0, 0)
    x_end = x_weight.shape[1]
    bc_end = x_end + bc_weight.shape[1]
    side_partials = jnp.einsum(
        "kti,io->kto", incoming, panel[:, x_end:], preferred_element_type=jnp.float32
    )
    side_back = lax.all_to_all(side_partials.astype(jnp.bfloat16), "dp", 0, 0)
    x_partials = jnp.einsum(
        "kti,io->kto", incoming, panel[:, :x_end], preferred_element_type=jnp.float32
    )
    x_back = lax.all_to_all(x_partials.astype(jnp.bfloat16), "dp", 0, 0)
    side_ext = jnp.sum(side_back.astype(jnp.float32), 0)
    x_ext = jnp.sum(x_back.astype(jnp.float32), 0)
    x_cols = x_end
    bc_width = bc_end - x_end
    dt_proj = lax.optimization_barrier(side_ext[rim:, bc_width:].astype(jnp.bfloat16))
    kernel = conv_x.shape[0] - 1

    def causal_conv(rows, taps):
        padded = rows.astype(jnp.bfloat16)[rim - (kernel - 1) :]
        total = taps[kernel]
        for tap_index in range(kernel):
            total = total + taps[tap_index] * padded[tap_index : tap_index + tok_rows]
        return jax.nn.silu(total).astype(jnp.bfloat16)

    bc_own = causal_conv(side_ext[:, :bc_width], conv_bc)
    x_conv = causal_conv(x_ext, conv_x)
    heads_dev = dt_weight.shape[1]
    head_size = x_cols // heads_dev
    per_group = HEADS // G
    groups_here = max(1, heads_dev // per_group)
    heads_local = heads_dev // groups_here
    first_group = lax.axis_index("mp") * heads_dev // per_group
    mp_count = lax.axis_size("mp")
    if bc_own.shape[1] == NS and mp_count == 2 * G and groups_here == 1:
        owner = [m * heads_dev // per_group for m in range(mp_count)]
        odd_first = [(owner[m] if m % 2 == 0 else G + owner[m], m) for m in range(mp_count)]
        even_first = [(G + owner[m] if m % 2 == 0 else owner[m], m) for m in range(mp_count)]
        got_a = lax.ppermute(bc_own, "mp", odd_first)
        got_b = lax.ppermute(bc_own, "mp", even_first)
        even = lax.axis_index("mp") % 2 == 0
        write_here = jnp.where(even, got_a, got_b).reshape(tok_rows, 1, NS)
        read_here = jnp.where(even, got_b, got_a).reshape(tok_rows, 1, NS)
    else:
        group_all = lax.all_gather(bc_own, "mp", axis=1, tiled=True)
        write_all = group_all[:, : G * NS].reshape(tok_rows, G, NS)
        read_all = group_all[:, G * NS :].reshape(tok_rows, G, NS)
        write_here = lax.dynamic_slice_in_dim(write_all, first_group, groups_here, 1)
        read_here = lax.dynamic_slice_in_dim(read_all, first_group, groups_here, 1)
    step_size = jax.nn.softplus(dt_proj.astype(jnp.float32) + dt_bias)
    decay_rate = step_size * jnp.exp(a_log)
    cumulative = jnp.cumsum(decay_rate, 0)
    block_end = cumulative[-1]
    causal = lax.broadcasted_iota(jnp.int32, (tok_rows, tok_rows), 0) >= lax.broadcasted_iota(
        jnp.int32, (tok_rows, tok_rows), 1
    )
    spread = cumulative.T[:, :, None] - cumulative.T[:, None, :]
    decay_mask = jnp.where(causal, jnp.exp(-jnp.where(causal, spread, 0.0)), 0.0)
    scores = jnp.einsum("tgn,sgn->gts", read_here, write_here, preferred_element_type=jnp.float32)
    weights = (
        scores[:, None]
        * decay_mask.reshape(groups_here, heads_local, tok_rows, tok_rows)
        * step_size.T.reshape(groups_here, heads_local, 1, tok_rows)
    ).astype(jnp.bfloat16)
    x_heads = x_conv.reshape(tok_rows, groups_here, heads_local, head_size)
    within_block = jnp.einsum(
        "ghts,sghp->tghp", weights, x_heads, preferred_element_type=jnp.float32
    )
    update = (
        (jnp.exp(-(block_end - cumulative)) * step_size).reshape(
            tok_rows, groups_here, heads_local
        )[..., None]
        * x_heads
    ).astype(jnp.bfloat16)
    contrib = jnp.einsum("sghp,sgn->ghpn", update, write_here, preferred_element_type=jnp.float32)
    carried = entering(jnp.exp(-block_end).reshape(groups_here, heads_local), contrib, "ctx")
    from_before = jnp.exp(-cumulative).reshape(tok_rows, groups_here, heads_local)[
        ..., None
    ] * jnp.einsum("tgn,ghpn->tghp", read_here.astype(jnp.float32), carried, precision=HIGH)
    output_raw = (
        within_block
        + from_before
        + d_skip.reshape(groups_here, heads_local)[None, :, :, None] * x_heads.astype(jnp.float32)
    )
    mean_square = jnp.mean(output_raw * output_raw, -1, keepdims=True)
    normed = (
        output_raw
        * lax.rsqrt(mean_square + 1e-05)
        * norm_gain.reshape(groups_here, heads_local, head_size)
    )
    return (normed.reshape(1, tok_rows, x_cols).astype(jnp.bfloat16), kurtosis)


def solution(mesh):
    return jax.shard_map(
        shards,
        mesh=mesh,
        in_specs=(
            P("dp", "ctx", None),
            P(("dp", "ctx"), "mp"),
            P(("dp", "ctx"), "mp"),
            P(("dp", "ctx"), "mp"),
            P(None, "mp"),
            P(None, "mp"),
            P("mp"),
            P("mp"),
            P("mp"),
            P("mp"),
        ),
        out_specs=(P("dp", "ctx", "mp"), P("mp")),
        check_vma=False,
    )
```

```python
import jax
import jax.numpy as jnp
from jax import lax
from jax.sharding import PartitionSpec as P

ROOT = 64
HEADS = 128
G = 4
NS = 128


HIGH = lax.Precision.HIGHEST


def passed_along(value, axis, steps):
    count = lax.axis_size(axis)
    first, last = (max(0, -steps), min(count, count - steps))
    return lax.ppermute(value, axis, [(source, source + steps) for source in range(first, last)])


def entering(decay, contrib, axis):
    count, place = (lax.axis_size(axis), lax.axis_index(axis))
    lanes = contrib.shape[-1]
    head_rows = contrib.shape[-2]
    heads = decay.size
    chunk = contrib.size // lanes // count
    pieces = contrib.reshape(count, chunk, lanes)
    tail = jnp.zeros((count, 8, lanes), jnp.float32)
    tail = tail.at[:, 0, :heads].set(jnp.broadcast_to(decay.reshape(1, heads), (count, heads)))
    outgoing = jnp.concatenate([pieces, tail], 1).astype(jnp.bfloat16)
    incoming = lax.all_to_all(outgoing, axis, 0, 0).astype(jnp.float32)
    states = incoming[:, :chunk]
    decays = incoming[:, chunk, :heads]
    row_head = (place * chunk + lax.broadcasted_iota(jnp.int32, (chunk, heads), 0)) // head_rows
    pick = row_head == lax.broadcasted_iota(jnp.int32, (chunk, heads), 1)
    row_decay = jnp.sum(jnp.where(pick[None], decays[:, None, :], 0.0), -1)
    target = lax.broadcasted_iota(jnp.int32, (count, count, count), 0)
    source = lax.broadcasted_iota(jnp.int32, (count, count, count), 1)
    between = lax.broadcasted_iota(jnp.int32, (count, count, count), 2)
    inside = jnp.logical_and(between > source, between < target)
    factors = jnp.where(inside[..., None], row_decay[None, None], 1.0)
    weights = jnp.prod(factors, 2)
    weights = jnp.where((source[:, :, 0] < target[:, :, 0])[..., None], weights, 0.0)
    carried = jnp.einsum("kjr,jrl->krl", weights, states, precision=HIGH)
    returned = lax.all_to_all(carried.astype(jnp.bfloat16), axis, 0, 0)
    return returned.astype(jnp.float32).reshape(contrib.shape)


def hadamard_signs(sign_order):
    row_index = lax.broadcasted_iota(jnp.int32, (sign_order, sign_order), 0)
    col_index = lax.broadcasted_iota(jnp.int32, (sign_order, sign_order), 1)
    common = jnp.bitwise_and(row_index, col_index)
    parity = jnp.zeros((sign_order, sign_order), jnp.int32)
    for bit_index in range(sign_order.bit_length() - 1):
        parity = parity + jnp.bitwise_and(jnp.right_shift(common, bit_index), 1)
    return 1.0 - 2.0 * jnp.bitwise_and(parity, 1).astype(jnp.float32)


def kurtosis_from(powers, row_count):
    average = powers[0] / row_count
    second = powers[1] / row_count - average * average
    fourth = (
        powers[3] / row_count
        - 4.0 * average * powers[2] / row_count
        + 6.0 * average * average * powers[1] / row_count
        - 3.0 * average * average * average * average
    )
    return fourth / (second * second + 1e-06)


def shards(
    tokens, x_weight, bc_weight, dt_weight, conv_x, conv_bc, dt_bias, a_log, d_skip, norm_gain
):
    tok_rows = tokens.shape[1]
    model_width = tokens.shape[2]
    signs = hadamard_signs(ROOT)
    blocks = tokens.reshape(tok_rows, ROOT, ROOT)
    first_pass = jnp.einsum(
        "tab,ac->tcb", blocks, signs.astype(jnp.bfloat16), preferred_element_type=jnp.float32
    )
    second = jnp.einsum("tcb,bd->tcd", first_pass, signs, precision=HIGH)
    rotated = (second.reshape(tok_rows, model_width) / ROOT).astype(jnp.bfloat16)
    channel_share = model_width // lax.axis_size("mp")
    own_cols = lax.dynamic_slice_in_dim(
        rotated, lax.axis_index("mp") * channel_share, channel_share, 1
    ).astype(jnp.float32)
    square = own_cols * own_cols
    powers = jnp.stack(
        [
            jnp.sum(own_cols, 0),
            jnp.sum(square, 0),
            jnp.sum(square * own_cols, 0),
            jnp.sum(square * square, 0),
        ]
    )
    row_count = float(tok_rows * lax.axis_size("dp") * lax.axis_size("ctx"))
    totals = lax.psum(lax.psum(powers, "ctx"), "dp")
    totals, rotated = lax.optimization_barrier((totals, rotated))
    kurtosis = kurtosis_from(totals, row_count)
    x_end = x_weight.shape[1]
    half = x_end // 2
    first_panel = lax.all_gather(
        jnp.concatenate([x_weight[:, :half], bc_weight, dt_weight], 1), "ctx", axis=0, tiled=True
    )
    second_local, rotated = lax.optimization_barrier((x_weight[:, half:], rotated))
    second_panel = lax.all_gather(second_local, "ctx", axis=0, tiled=True)
    seqs = lax.axis_size("dp")
    share = model_width // seqs
    rim = 8
    earlier = passed_along(rotated[tok_rows - rim :], "ctx", 1)
    extended = jnp.concatenate([earlier, rotated], 0)
    outgoing = extended.reshape(tok_rows + rim, seqs, share).transpose(1, 0, 2)
    incoming = lax.all_to_all(outgoing, "dp", 0, 0)
    def projected_rows(panel):
        partials = jnp.einsum("kti,io->kto", incoming, panel, preferred_element_type=jnp.float32)
        back = lax.all_to_all(partials.astype(jnp.bfloat16), "dp", 0, 0)
        return jnp.sum(back.astype(jnp.float32), 0)

    first_ext = projected_rows(first_panel)
    side_ext = first_ext[:, half:]
    x_cols = x_end
    bc_width = bc_weight.shape[1]
    dt_proj = lax.optimization_barrier(side_ext[rim:, bc_width:].astype(jnp.bfloat16))
    kernel = conv_x.shape[0] - 1

    def causal_conv(rows, taps):
        padded = rows.astype(jnp.bfloat16)[rim - (kernel - 1) :]
        total = taps[kernel]
        for tap_index in range(kernel):
            total = total + taps[tap_index] * padded[tap_index : tap_index + tok_rows]
        return jax.nn.silu(total).astype(jnp.bfloat16)

    bc_own = causal_conv(side_ext[:, :bc_width], conv_bc)
    x_conv_parts = [causal_conv(first_ext[:, :half], conv_x[:, :half])]
    heads_dev = dt_weight.shape[1]
    head_size = x_cols // heads_dev
    per_group = HEADS // G
    groups_here = max(1, heads_dev // per_group)
    heads_local = heads_dev // groups_here
    first_group = lax.axis_index("mp") * heads_dev // per_group
    mp_count = lax.axis_size("mp")
    if bc_own.shape[1] == NS and mp_count == 2 * G and groups_here == 1:
        owner = [m * heads_dev // per_group for m in range(mp_count)]
        odd_first = [(owner[m] if m % 2 == 0 else G + owner[m], m) for m in range(mp_count)]
        even_first = [(G + owner[m] if m % 2 == 0 else owner[m], m) for m in range(mp_count)]
        got_a = lax.ppermute(bc_own, "mp", odd_first)
        got_b = lax.ppermute(bc_own, "mp", even_first)
        even = lax.axis_index("mp") % 2 == 0
        write_here = jnp.where(even, got_a, got_b).reshape(tok_rows, 1, NS)
        read_here = jnp.where(even, got_b, got_a).reshape(tok_rows, 1, NS)
    else:
        group_all = lax.all_gather(bc_own, "mp", axis=1, tiled=True)
        write_all = group_all[:, : G * NS].reshape(tok_rows, G, NS)
        read_all = group_all[:, G * NS :].reshape(tok_rows, G, NS)
        write_here = lax.dynamic_slice_in_dim(write_all, first_group, groups_here, 1)
        read_here = lax.dynamic_slice_in_dim(read_all, first_group, groups_here, 1)
    step_size = jax.nn.softplus(dt_proj.astype(jnp.float32) + dt_bias)
    decay_rate = step_size * jnp.exp(a_log)
    cumulative = jnp.cumsum(decay_rate, 0)
    block_end = cumulative[-1]
    causal = lax.broadcasted_iota(jnp.int32, (tok_rows, tok_rows), 0) >= lax.broadcasted_iota(
        jnp.int32, (tok_rows, tok_rows), 1
    )
    spread = cumulative.T[:, :, None] - cumulative.T[:, None, :]
    decay_mask = jnp.where(causal, jnp.exp(-jnp.where(causal, spread, 0.0)), 0.0)
    scores = jnp.einsum("tgn,sgn->gts", read_here, write_here, preferred_element_type=jnp.float32)
    weights = (
        scores[:, None]
        * decay_mask.reshape(groups_here, heads_local, tok_rows, tok_rows)
        * step_size.T.reshape(groups_here, heads_local, 1, tok_rows)
    ).astype(jnp.bfloat16)
    head_share = heads_local // 2
    factor = (jnp.exp(-(block_end - cumulative)) * step_size).reshape(
        tok_rows, groups_here, heads_local
    )
    block_decay = jnp.exp(-block_end).reshape(groups_here, heads_local)
    carried_parts = []
    for part_index in range(2):
        if part_index == 1:
            second_panel, carried_parts[0] = lax.optimization_barrier(
                (second_panel, carried_parts[0])
            )
            second_ext = projected_rows(second_panel)
            x_conv_parts.append(causal_conv(second_ext, conv_x[:, half:]))
        part = x_conv_parts[part_index]
        heads_part = slice(part_index * head_share, (part_index + 1) * head_share)
        update = (
            factor[:, :, heads_part, None]
            * part.reshape(tok_rows, groups_here, head_share, head_size)
        ).astype(jnp.bfloat16)
        contrib = jnp.einsum(
            "sghp,sgn->ghpn", update, write_here, preferred_element_type=jnp.float32
        )
        carried_parts.append(entering(block_decay[:, heads_part], contrib, "ctx"))
    carried = jnp.concatenate(carried_parts, 1)
    x_conv = jnp.concatenate(x_conv_parts, 1)
    x_heads = x_conv.reshape(tok_rows, groups_here, heads_local, head_size)
    within_block = jnp.einsum(
        "ghts,sghp->tghp", weights, x_heads, preferred_element_type=jnp.float32
    )
    from_before = jnp.exp(-cumulative).reshape(tok_rows, groups_here, heads_local)[
        ..., None
    ] * jnp.einsum("tgn,ghpn->tghp", read_here.astype(jnp.float32), carried, precision=HIGH)
    output_raw = (
        within_block
        + from_before
        + d_skip.reshape(groups_here, heads_local)[None, :, :, None] * x_heads.astype(jnp.float32)
    )
    mean_square = jnp.mean(output_raw * output_raw, -1, keepdims=True)
    normed = (
        output_raw
        * lax.rsqrt(mean_square + 1e-05)
        * norm_gain.reshape(groups_here, heads_local, head_size)
    )
    return (normed.reshape(1, tok_rows, x_cols).astype(jnp.bfloat16), kurtosis)


def solution(mesh):
    return jax.shard_map(
        shards,
        mesh=mesh,
        in_specs=(
            P("dp", "ctx", None),
            P(("dp", "ctx"), "mp"),
            P(("dp", "ctx"), "mp"),
            P(("dp", "ctx"), "mp"),
            P(None, "mp"),
            P(None, "mp"),
            P("mp"),
            P("mp"),
            P("mp"),
            P("mp"),
        ),
        out_specs=(P("dp", "ctx", "mp"), P("mp")),
        check_vma=False,
    )
```

```python
import jax
import jax.numpy as jnp
from jax import lax
from jax.sharding import PartitionSpec as P

ROOT = 64
HEADS = 128
G = 4
NS = 128


HIGH = lax.Precision.HIGHEST
CTX = ("ch", "cl")


def passed_along(value, axis, steps, count):
    first, last = (max(0, -steps), min(count, count - steps))
    return lax.ppermute(value, axis, [(source, source + steps) for source in range(first, last)])


def decay_products(row_decay, targets):
    count = row_decay.shape[0]
    target = lax.broadcasted_iota(jnp.int32, (targets, count, count), 0)
    source = lax.broadcasted_iota(jnp.int32, (targets, count, count), 1)
    between = lax.broadcasted_iota(jnp.int32, (targets, count, count), 2)
    inside = jnp.logical_and(between > source, between < target)
    factors = jnp.where(inside[..., None], row_decay[None, None], 1.0)
    products = jnp.prod(factors, 2)
    return jnp.where((source[:, :, 0] < target[:, :, 0])[..., None], products, 0.0)


def entering(decay, contrib):
    quads, quad = (lax.axis_index("ch"), lax.axis_size("cl"))
    place = lax.axis_index("cl")
    lanes = contrib.shape[-1]
    head_rows = contrib.shape[-2]
    heads = decay.size
    chunk = contrib.size // lanes // quad
    pieces = contrib.reshape(quad, chunk, lanes)
    tail = jnp.zeros((quad, 8, lanes), jnp.float32)
    tail = tail.at[:, 0, :heads].set(jnp.broadcast_to(decay.reshape(1, heads), (quad, heads)))
    outgoing = jnp.concatenate([pieces, tail], 1).astype(jnp.bfloat16)
    incoming = lax.all_to_all(outgoing, "cl", 0, 0).astype(jnp.float32)
    states = incoming[:, :chunk]
    decays = incoming[:, chunk, :heads]
    row_head = (place * chunk + lax.broadcasted_iota(jnp.int32, (chunk, heads), 0)) // head_rows
    pick = row_head == lax.broadcasted_iota(jnp.int32, (chunk, heads), 1)
    row_decay = jnp.sum(jnp.where(pick[None], decays[:, None, :], 0.0), -1)
    local = jnp.einsum(
        "kjr,jrl->krl", decay_products(row_decay, quad + 1), states, precision=HIGH
    )
    step = lax.broadcasted_iota(jnp.int32, (quad + 1, quad, chunk), 0)
    index = lax.broadcasted_iota(jnp.int32, (quad + 1, quad, chunk), 1)
    entry = jnp.prod(jnp.where(index < step, row_decay[None], 1.0), 1)
    pad_rows = 8 - (chunk // lanes) % 8
    summary = jnp.concatenate(
        [local[quad], entry[quad].reshape(chunk // lanes, lanes), jnp.zeros((pad_rows, lanes))]
    )
    count_hi = lax.axis_size("ch")
    shared = lax.all_to_all(jnp.broadcast_to(summary, (count_hi,) + summary.shape), "ch", 0, 0)
    totals = shared[:, :chunk]
    quad_decay = shared[:, chunk : chunk + chunk // lanes].reshape(count_hi, chunk)
    earlier = lax.broadcasted_iota(jnp.int32, (count_hi, count_hi, chunk), 0)
    middle = lax.broadcasted_iota(jnp.int32, (count_hi, count_hi, chunk), 1)
    spans = jnp.logical_and(middle > earlier, middle < quads)
    across = jnp.prod(jnp.where(spans, quad_decay[None], 1.0), 1)
    across = jnp.where(earlier[:, 0] < quads, across, 0.0)
    entering_state = jnp.einsum("qr,qrl->rl", across, totals, precision=HIGH)
    carried = local[:quad] + entry[:quad, :, None] * entering_state[None]
    returned = lax.all_to_all(carried.astype(jnp.bfloat16), "cl", 0, 0)
    return returned.astype(jnp.float32).reshape(contrib.shape)


def hadamard_signs(sign_order):
    row_index = lax.broadcasted_iota(jnp.int32, (sign_order, sign_order), 0)
    col_index = lax.broadcasted_iota(jnp.int32, (sign_order, sign_order), 1)
    common = jnp.bitwise_and(row_index, col_index)
    parity = jnp.zeros((sign_order, sign_order), jnp.int32)
    for bit_index in range(sign_order.bit_length() - 1):
        parity = parity + jnp.bitwise_and(jnp.right_shift(common, bit_index), 1)
    return 1.0 - 2.0 * jnp.bitwise_and(parity, 1).astype(jnp.float32)


def kurtosis_from(powers, row_count):
    average = powers[0] / row_count
    second = powers[1] / row_count - average * average
    fourth = (
        powers[3] / row_count
        - 4.0 * average * powers[2] / row_count
        + 6.0 * average * average * powers[1] / row_count
        - 3.0 * average * average * average * average
    )
    return fourth / (second * second + 1e-06)


def shards(
    tokens, x_weight, bc_weight, dt_weight, conv_x, conv_bc, dt_bias, a_log, d_skip, norm_gain
):
    tok_rows = tokens.shape[1]
    model_width = tokens.shape[2]
    signs = hadamard_signs(ROOT)
    blocks = tokens.reshape(tok_rows, ROOT, ROOT)
    first_pass = jnp.einsum(
        "tab,ac->tcb", blocks, signs.astype(jnp.bfloat16), preferred_element_type=jnp.float32
    )
    second = jnp.einsum("tcb,bd->tcd", first_pass, signs, precision=HIGH)
    rotated = (second.reshape(tok_rows, model_width) / ROOT).astype(jnp.bfloat16)
    channel_share = model_width // lax.axis_size("mp")
    own_cols = lax.dynamic_slice_in_dim(
        rotated, lax.axis_index("mp") * channel_share, channel_share, 1
    ).astype(jnp.float32)
    square = own_cols * own_cols
    powers = jnp.stack(
        [
            jnp.sum(own_cols, 0),
            jnp.sum(square, 0),
            jnp.sum(square * own_cols, 0),
            jnp.sum(square * square, 0),
        ]
    )
    ctx_count = lax.axis_size("ch") * lax.axis_size("cl")
    row_count = float(tok_rows * lax.axis_size("dp") * ctx_count)
    totals = lax.psum(lax.psum(powers, CTX), "dp")
    totals, rotated = lax.optimization_barrier((totals, rotated))
    kurtosis = kurtosis_from(totals, row_count)
    local_panel = jnp.concatenate([x_weight, bc_weight, dt_weight], 1)
    panel = lax.all_gather(local_panel, CTX, axis=0, tiled=True)
    seqs = lax.axis_size("dp")
    share = model_width // seqs
    rim = 8
    earlier = passed_along(rotated[tok_rows - rim :], CTX, 1, ctx_count)
    extended = jnp.concatenate([earlier, rotated], 0)
    outgoing = extended.reshape(tok_rows + rim, seqs, share).transpose(1, 0, 2)
    incoming = lax.all_to_all(outgoing, "dp", 0, 0)
    x_end = x_weight.shape[1]
    bc_end = x_end + bc_weight.shape[1]
    side_partials = jnp.einsum(
        "kti,io->kto", incoming, panel[:, x_end:], preferred_element_type=jnp.float32
    )
    side_back = lax.all_to_all(side_partials.astype(jnp.bfloat16), "dp", 0, 0)
    x_partials = jnp.einsum(
        "kti,io->kto", incoming, panel[:, :x_end], preferred_element_type=jnp.float32
    )
    x_back = lax.all_to_all(x_partials.astype(jnp.bfloat16), "dp", 0, 0)
    side_ext = jnp.sum(side_back.astype(jnp.float32), 0)
    x_ext = jnp.sum(x_back.astype(jnp.float32), 0)
    x_cols = x_end
    bc_width = bc_end - x_end
    dt_proj = lax.optimization_barrier(side_ext[rim:, bc_width:].astype(jnp.bfloat16))
    kernel = conv_x.shape[0] - 1

    def causal_conv(rows, taps):
        padded = rows.astype(jnp.bfloat16)[rim - (kernel - 1) :]
        total = taps[kernel]
        for tap_index in range(kernel):
            total = total + taps[tap_index] * padded[tap_index : tap_index + tok_rows]
        return jax.nn.silu(total).astype(jnp.bfloat16)

    bc_own = causal_conv(side_ext[:, :bc_width], conv_bc)
    x_conv = causal_conv(x_ext, conv_x)
    heads_dev = dt_weight.shape[1]
    head_size = x_cols // heads_dev
    per_group = HEADS // G
    groups_here = max(1, heads_dev // per_group)
    heads_local = heads_dev // groups_here
    first_group = lax.axis_index("mp") * heads_dev // per_group
    mp_count = lax.axis_size("mp")
    if bc_own.shape[1] == NS and mp_count == 2 * G and groups_here == 1:
        owner = [m * heads_dev // per_group for m in range(mp_count)]
        odd_first = [(owner[m] if m % 2 == 0 else G + owner[m], m) for m in range(mp_count)]
        even_first = [(G + owner[m] if m % 2 == 0 else owner[m], m) for m in range(mp_count)]
        got_a = lax.ppermute(bc_own, "mp", odd_first)
        got_b = lax.ppermute(bc_own, "mp", even_first)
        even = lax.axis_index("mp") % 2 == 0
        write_here = jnp.where(even, got_a, got_b).reshape(tok_rows, 1, NS)
        read_here = jnp.where(even, got_b, got_a).reshape(tok_rows, 1, NS)
    else:
        group_all = lax.all_gather(bc_own, "mp", axis=1, tiled=True)
        write_all = group_all[:, : G * NS].reshape(tok_rows, G, NS)
        read_all = group_all[:, G * NS :].reshape(tok_rows, G, NS)
        write_here = lax.dynamic_slice_in_dim(write_all, first_group, groups_here, 1)
        read_here = lax.dynamic_slice_in_dim(read_all, first_group, groups_here, 1)
    step_size = jax.nn.softplus(dt_proj.astype(jnp.float32) + dt_bias)
    decay_rate = step_size * jnp.exp(a_log)
    cumulative = jnp.cumsum(decay_rate, 0)
    block_end = cumulative[-1]
    causal = lax.broadcasted_iota(jnp.int32, (tok_rows, tok_rows), 0) >= lax.broadcasted_iota(
        jnp.int32, (tok_rows, tok_rows), 1
    )
    spread = cumulative.T[:, :, None] - cumulative.T[:, None, :]
    decay_mask = jnp.where(causal, jnp.exp(-jnp.where(causal, spread, 0.0)), 0.0)
    scores = jnp.einsum("tgn,sgn->gts", read_here, write_here, preferred_element_type=jnp.float32)
    weights = (
        scores[:, None]
        * decay_mask.reshape(groups_here, heads_local, tok_rows, tok_rows)
        * step_size.T.reshape(groups_here, heads_local, 1, tok_rows)
    ).astype(jnp.bfloat16)
    x_heads = x_conv.reshape(tok_rows, groups_here, heads_local, head_size)
    within_block = jnp.einsum(
        "ghts,sghp->tghp", weights, x_heads, preferred_element_type=jnp.float32
    )
    update = (
        (jnp.exp(-(block_end - cumulative)) * step_size).reshape(
            tok_rows, groups_here, heads_local
        )[..., None]
        * x_heads
    ).astype(jnp.bfloat16)
    contrib = jnp.einsum("sghp,sgn->ghpn", update, write_here, preferred_element_type=jnp.float32)
    carried = entering(jnp.exp(-block_end).reshape(groups_here, heads_local), contrib)
    from_before = jnp.exp(-cumulative).reshape(tok_rows, groups_here, heads_local)[
        ..., None
    ] * jnp.einsum("tgn,ghpn->tghp", read_here.astype(jnp.float32), carried, precision=HIGH)
    output_raw = (
        within_block
        + from_before
        + d_skip.reshape(groups_here, heads_local)[None, :, :, None] * x_heads.astype(jnp.float32)
    )
    mean_square = jnp.mean(output_raw * output_raw, -1, keepdims=True)
    normed = (
        output_raw
        * lax.rsqrt(mean_square + 1e-05)
        * norm_gain.reshape(groups_here, heads_local, head_size)
    )
    return (normed.reshape(1, tok_rows, x_cols).astype(jnp.bfloat16), kurtosis)


def solution(mesh):
    grid = mesh.devices
    quad = 4 if grid.shape[1] % 4 == 0 else 1
    split = jax.sharding.Mesh(
        grid.reshape(grid.shape[0], grid.shape[1] // quad, quad, grid.shape[2]),
        ("dp", "ch", "cl", "mp"),
    )
    return jax.shard_map(
        shards,
        mesh=split,
        in_specs=(
            P("dp", CTX, None),
            P(("dp",) + CTX, "mp"),
            P(("dp",) + CTX, "mp"),
            P(("dp",) + CTX, "mp"),
            P(None, "mp"),
            P(None, "mp"),
            P("mp"),
            P("mp"),
            P("mp"),
            P("mp"),
        ),
        out_specs=(P("dp", CTX, "mp"), P("mp")),
        check_vma=False,
    )
```

```python
import jax
import jax.numpy as jnp
from jax import lax
from jax.sharding import PartitionSpec as P

ROOT = 64
HEADS = 128
G = 4
NS = 128


HIGH = lax.Precision.HIGHEST
CTX = ("ch", "cl")


def passed_along(value, axis, steps, count):
    first, last = (max(0, -steps), min(count, count - steps))
    return lax.ppermute(value, axis, [(source, source + steps) for source in range(first, last)])


def decay_products(row_decay, targets):
    count = row_decay.shape[0]
    target = lax.broadcasted_iota(jnp.int32, (targets, count, count), 0)
    source = lax.broadcasted_iota(jnp.int32, (targets, count, count), 1)
    between = lax.broadcasted_iota(jnp.int32, (targets, count, count), 2)
    inside = jnp.logical_and(between > source, between < target)
    factors = jnp.where(inside[..., None], row_decay[None, None], 1.0)
    products = jnp.prod(factors, 2)
    return jnp.where((source[:, :, 0] < target[:, :, 0])[..., None], products, 0.0)


def entering(decay, contrib):
    quads, quad = (lax.axis_index("ch"), lax.axis_size("cl"))
    place = lax.axis_index("cl")
    lanes = contrib.shape[-1]
    head_rows = contrib.shape[-2]
    heads = decay.size
    chunk = contrib.size // lanes // quad
    pieces = contrib.reshape(quad, chunk, lanes)
    tail = jnp.zeros((quad, 8, lanes), jnp.float32)
    tail = tail.at[:, 0, :heads].set(jnp.broadcast_to(decay.reshape(1, heads), (quad, heads)))
    outgoing = jnp.concatenate([pieces, tail], 1).astype(jnp.bfloat16)
    incoming = lax.all_to_all(outgoing, "cl", 0, 0).astype(jnp.float32)
    states = incoming[:, :chunk]
    decays = incoming[:, chunk, :heads]
    row_head = (place * chunk + lax.broadcasted_iota(jnp.int32, (chunk, heads), 0)) // head_rows
    pick = row_head == lax.broadcasted_iota(jnp.int32, (chunk, heads), 1)
    row_decay = jnp.sum(jnp.where(pick[None], decays[:, None, :], 0.0), -1)
    local = jnp.einsum(
        "kjr,jrl->krl", decay_products(row_decay, quad + 1), states, precision=HIGH
    )
    step = lax.broadcasted_iota(jnp.int32, (quad + 1, quad, chunk), 0)
    index = lax.broadcasted_iota(jnp.int32, (quad + 1, quad, chunk), 1)
    entry = jnp.prod(jnp.where(index < step, row_decay[None], 1.0), 1)
    pad_rows = 8 - (chunk // lanes) % 8
    summary = jnp.concatenate(
        [local[quad], entry[quad].reshape(chunk // lanes, lanes), jnp.zeros((pad_rows, lanes))]
    )
    count_hi = lax.axis_size("ch")
    shared = lax.all_to_all(
        jnp.broadcast_to(summary.astype(jnp.bfloat16), (count_hi,) + summary.shape), "ch", 0, 0
    ).astype(jnp.float32)
    totals = shared[:, :chunk]
    quad_decay = shared[:, chunk : chunk + chunk // lanes].reshape(count_hi, chunk)
    earlier = lax.broadcasted_iota(jnp.int32, (count_hi, count_hi, chunk), 0)
    middle = lax.broadcasted_iota(jnp.int32, (count_hi, count_hi, chunk), 1)
    spans = jnp.logical_and(middle > earlier, middle < quads)
    across = jnp.prod(jnp.where(spans, quad_decay[None], 1.0), 1)
    across = jnp.where(earlier[:, 0] < quads, across, 0.0)
    entering_state = jnp.einsum("qr,qrl->rl", across, totals, precision=HIGH)
    carried = local[:quad] + entry[:quad, :, None] * entering_state[None]
    returned = lax.all_to_all(carried.astype(jnp.bfloat16), "cl", 0, 0)
    return returned.astype(jnp.float32).reshape(contrib.shape)


def hadamard_signs(sign_order):
    row_index = lax.broadcasted_iota(jnp.int32, (sign_order, sign_order), 0)
    col_index = lax.broadcasted_iota(jnp.int32, (sign_order, sign_order), 1)
    common = jnp.bitwise_and(row_index, col_index)
    parity = jnp.zeros((sign_order, sign_order), jnp.int32)
    for bit_index in range(sign_order.bit_length() - 1):
        parity = parity + jnp.bitwise_and(jnp.right_shift(common, bit_index), 1)
    return 1.0 - 2.0 * jnp.bitwise_and(parity, 1).astype(jnp.float32)


def kurtosis_from(powers, row_count):
    average = powers[0] / row_count
    second = powers[1] / row_count - average * average
    fourth = (
        powers[3] / row_count
        - 4.0 * average * powers[2] / row_count
        + 6.0 * average * average * powers[1] / row_count
        - 3.0 * average * average * average * average
    )
    return fourth / (second * second + 1e-06)


def shards(
    tokens, x_weight, bc_weight, dt_weight, conv_x, conv_bc, dt_bias, a_log, d_skip, norm_gain
):
    tok_rows = tokens.shape[1]
    model_width = tokens.shape[2]
    signs = hadamard_signs(ROOT)
    blocks = tokens.reshape(tok_rows, ROOT, ROOT)
    first_pass = jnp.einsum(
        "tab,ac->tcb", blocks, signs.astype(jnp.bfloat16), preferred_element_type=jnp.float32
    )
    second = jnp.einsum("tcb,bd->tcd", first_pass, signs, precision=HIGH)
    rotated = (second.reshape(tok_rows, model_width) / ROOT).astype(jnp.bfloat16)
    channel_share = model_width // lax.axis_size("mp")
    own_cols = lax.dynamic_slice_in_dim(
        rotated, lax.axis_index("mp") * channel_share, channel_share, 1
    ).astype(jnp.float32)
    square = own_cols * own_cols
    powers = jnp.stack(
        [
            jnp.sum(own_cols, 0),
            jnp.sum(square, 0),
            jnp.sum(square * own_cols, 0),
            jnp.sum(square * square, 0),
        ]
    )
    ctx_count = lax.axis_size("ch") * lax.axis_size("cl")
    row_count = float(tok_rows * lax.axis_size("dp") * ctx_count)
    totals = lax.psum(lax.psum(powers, CTX), "dp")
    totals, rotated = lax.optimization_barrier((totals, rotated))
    kurtosis = kurtosis_from(totals, row_count)
    local_panel = jnp.concatenate([x_weight, bc_weight, dt_weight], 1)
    panel = lax.all_gather(local_panel, CTX, axis=0, tiled=True)
    seqs = lax.axis_size("dp")
    share = model_width // seqs
    rim = 8
    earlier = passed_along(rotated[tok_rows - rim :], CTX, 1, ctx_count)
    extended = jnp.concatenate([earlier, rotated], 0)
    outgoing = extended.reshape(tok_rows + rim, seqs, share).transpose(1, 0, 2)
    incoming = lax.all_to_all(outgoing, "dp", 0, 0)
    x_end = x_weight.shape[1]
    bc_end = x_end + bc_weight.shape[1]
    side_partials = jnp.einsum(
        "kti,io->kto", incoming, panel[:, x_end:], preferred_element_type=jnp.float32
    )
    side_back = lax.all_to_all(side_partials.astype(jnp.bfloat16), "dp", 0, 0)
    x_partials = jnp.einsum(
        "kti,io->kto", incoming, panel[:, :x_end], preferred_element_type=jnp.float32
    )
    x_back = lax.all_to_all(x_partials.astype(jnp.bfloat16), "dp", 0, 0)
    side_ext = jnp.sum(side_back.astype(jnp.float32), 0)
    x_ext = jnp.sum(x_back.astype(jnp.float32), 0)
    x_cols = x_end
    bc_width = bc_end - x_end
    dt_proj = lax.optimization_barrier(side_ext[rim:, bc_width:].astype(jnp.bfloat16))
    kernel = conv_x.shape[0] - 1

    def causal_conv(rows, taps):
        padded = rows.astype(jnp.bfloat16)[rim - (kernel - 1) :]
        total = taps[kernel]
        for tap_index in range(kernel):
            total = total + taps[tap_index] * padded[tap_index : tap_index + tok_rows]
        return jax.nn.silu(total).astype(jnp.bfloat16)

    bc_own = causal_conv(side_ext[:, :bc_width], conv_bc)
    x_conv = causal_conv(x_ext, conv_x)
    heads_dev = dt_weight.shape[1]
    head_size = x_cols // heads_dev
    per_group = HEADS // G
    groups_here = max(1, heads_dev // per_group)
    heads_local = heads_dev // groups_here
    first_group = lax.axis_index("mp") * heads_dev // per_group
    mp_count = lax.axis_size("mp")
    if bc_own.shape[1] == NS and mp_count == 2 * G and groups_here == 1:
        owner = [m * heads_dev // per_group for m in range(mp_count)]
        odd_first = [(owner[m] if m % 2 == 0 else G + owner[m], m) for m in range(mp_count)]
        even_first = [(G + owner[m] if m % 2 == 0 else owner[m], m) for m in range(mp_count)]
        got_a = lax.ppermute(bc_own, "mp", odd_first)
        got_b = lax.ppermute(bc_own, "mp", even_first)
        even = lax.axis_index("mp") % 2 == 0
        write_here = jnp.where(even, got_a, got_b).reshape(tok_rows, 1, NS)
        read_here = jnp.where(even, got_b, got_a).reshape(tok_rows, 1, NS)
    else:
        group_all = lax.all_gather(bc_own, "mp", axis=1, tiled=True)
        write_all = group_all[:, : G * NS].reshape(tok_rows, G, NS)
        read_all = group_all[:, G * NS :].reshape(tok_rows, G, NS)
        write_here = lax.dynamic_slice_in_dim(write_all, first_group, groups_here, 1)
        read_here = lax.dynamic_slice_in_dim(read_all, first_group, groups_here, 1)
    step_size = jax.nn.softplus(dt_proj.astype(jnp.float32) + dt_bias)
    decay_rate = step_size * jnp.exp(a_log)
    cumulative = jnp.cumsum(decay_rate, 0)
    block_end = cumulative[-1]
    causal = lax.broadcasted_iota(jnp.int32, (tok_rows, tok_rows), 0) >= lax.broadcasted_iota(
        jnp.int32, (tok_rows, tok_rows), 1
    )
    spread = cumulative.T[:, :, None] - cumulative.T[:, None, :]
    decay_mask = jnp.where(causal, jnp.exp(-jnp.where(causal, spread, 0.0)), 0.0)
    scores = jnp.einsum("tgn,sgn->gts", read_here, write_here, preferred_element_type=jnp.float32)
    weights = (
        scores[:, None]
        * decay_mask.reshape(groups_here, heads_local, tok_rows, tok_rows)
        * step_size.T.reshape(groups_here, heads_local, 1, tok_rows)
    ).astype(jnp.bfloat16)
    x_heads = x_conv.reshape(tok_rows, groups_here, heads_local, head_size)
    within_block = jnp.einsum(
        "ghts,sghp->tghp", weights, x_heads, preferred_element_type=jnp.float32
    )
    update = (
        (jnp.exp(-(block_end - cumulative)) * step_size).reshape(
            tok_rows, groups_here, heads_local
        )[..., None]
        * x_heads
    ).astype(jnp.bfloat16)
    contrib = jnp.einsum("sghp,sgn->ghpn", update, write_here, preferred_element_type=jnp.float32)
    carried = entering(jnp.exp(-block_end).reshape(groups_here, heads_local), contrib)
    from_before = jnp.exp(-cumulative).reshape(tok_rows, groups_here, heads_local)[
        ..., None
    ] * jnp.einsum("tgn,ghpn->tghp", read_here.astype(jnp.float32), carried, precision=HIGH)
    output_raw = (
        within_block
        + from_before
        + d_skip.reshape(groups_here, heads_local)[None, :, :, None] * x_heads.astype(jnp.float32)
    )
    mean_square = jnp.mean(output_raw * output_raw, -1, keepdims=True)
    normed = (
        output_raw
        * lax.rsqrt(mean_square + 1e-05)
        * norm_gain.reshape(groups_here, heads_local, head_size)
    )
    return (normed.reshape(1, tok_rows, x_cols).astype(jnp.bfloat16), kurtosis)


def solution(mesh):
    grid = mesh.devices
    quad = 4 if grid.shape[1] % 4 == 0 else 1
    split = jax.sharding.Mesh(
        grid.reshape(grid.shape[0], grid.shape[1] // quad, quad, grid.shape[2]),
        ("dp", "ch", "cl", "mp"),
    )
    return jax.shard_map(
        shards,
        mesh=split,
        in_specs=(
            P("dp", CTX, None),
            P(("dp",) + CTX, "mp"),
            P(("dp",) + CTX, "mp"),
            P(("dp",) + CTX, "mp"),
            P(None, "mp"),
            P(None, "mp"),
            P("mp"),
            P("mp"),
            P("mp"),
            P("mp"),
        ),
        out_specs=(P("dp", CTX, "mp"), P("mp")),
        check_vma=False,
    )
```

```python
import jax
import jax.numpy as jnp
from jax import lax
from jax.sharding import PartitionSpec as P

ROOT = 64
HEADS = 128
G = 4
NS = 128


HIGH = lax.Precision.HIGHEST
CTX = ("ch", "cl")


def passed_along(value, axis, steps, count):
    first, last = (max(0, -steps), min(count, count - steps))
    return lax.ppermute(value, axis, [(source, source + steps) for source in range(first, last)])


def decay_products(row_decay, targets):
    count = row_decay.shape[0]
    target = lax.broadcasted_iota(jnp.int32, (targets, count, count), 0)
    source = lax.broadcasted_iota(jnp.int32, (targets, count, count), 1)
    between = lax.broadcasted_iota(jnp.int32, (targets, count, count), 2)
    inside = jnp.logical_and(between > source, between < target)
    factors = jnp.where(inside[..., None], row_decay[None, None], 1.0)
    products = jnp.prod(factors, 2)
    return jnp.where((source[:, :, 0] < target[:, :, 0])[..., None], products, 0.0)


def entering(decay, contrib):
    quads, quad = (lax.axis_index("ch"), lax.axis_size("cl"))
    place = lax.axis_index("cl")
    lanes = contrib.shape[-1]
    head_rows = contrib.shape[-2]
    heads = decay.size
    chunk = contrib.size // lanes // quad
    pieces = contrib.reshape(quad, chunk, lanes)
    tail = jnp.zeros((quad, 8, lanes), jnp.float32)
    tail = tail.at[:, 0, :heads].set(jnp.broadcast_to(decay.reshape(1, heads), (quad, heads)))
    outgoing = jnp.concatenate([pieces, tail], 1).astype(jnp.bfloat16)
    incoming = lax.all_to_all(outgoing, "cl", 0, 0).astype(jnp.float32)
    states = incoming[:, :chunk]
    decays = incoming[:, chunk, :heads]
    row_head = (place * chunk + lax.broadcasted_iota(jnp.int32, (chunk, heads), 0)) // head_rows
    pick = row_head == lax.broadcasted_iota(jnp.int32, (chunk, heads), 1)
    row_decay = jnp.sum(jnp.where(pick[None], decays[:, None, :], 0.0), -1)
    local = jnp.einsum(
        "kjr,jrl->krl", decay_products(row_decay, quad + 1), states, precision=HIGH
    )
    step = lax.broadcasted_iota(jnp.int32, (quad + 1, quad, chunk), 0)
    index = lax.broadcasted_iota(jnp.int32, (quad + 1, quad, chunk), 1)
    entry = jnp.prod(jnp.where(index < step, row_decay[None], 1.0), 1)
    pad_rows = 8 - (chunk // lanes) % 8
    summary = jnp.concatenate(
        [local[quad], entry[quad].reshape(chunk // lanes, lanes), jnp.zeros((pad_rows, lanes))]
    )
    count_hi = lax.axis_size("ch")
    shared = lax.all_gather(summary.astype(jnp.bfloat16), "ch").astype(jnp.float32)
    totals = shared[:, :chunk]
    quad_decay = shared[:, chunk : chunk + chunk // lanes].reshape(count_hi, chunk)
    earlier = lax.broadcasted_iota(jnp.int32, (count_hi, count_hi, chunk), 0)
    middle = lax.broadcasted_iota(jnp.int32, (count_hi, count_hi, chunk), 1)
    spans = jnp.logical_and(middle > earlier, middle < quads)
    across = jnp.prod(jnp.where(spans, quad_decay[None], 1.0), 1)
    across = jnp.where(earlier[:, 0] < quads, across, 0.0)
    entering_state = jnp.einsum("qr,qrl->rl", across, totals, precision=HIGH)
    carried = local[:quad] + entry[:quad, :, None] * entering_state[None]
    returned = lax.all_to_all(carried.astype(jnp.bfloat16), "cl", 0, 0)
    return returned.astype(jnp.float32).reshape(contrib.shape)


def hadamard_signs(sign_order):
    row_index = lax.broadcasted_iota(jnp.int32, (sign_order, sign_order), 0)
    col_index = lax.broadcasted_iota(jnp.int32, (sign_order, sign_order), 1)
    common = jnp.bitwise_and(row_index, col_index)
    parity = jnp.zeros((sign_order, sign_order), jnp.int32)
    for bit_index in range(sign_order.bit_length() - 1):
        parity = parity + jnp.bitwise_and(jnp.right_shift(common, bit_index), 1)
    return 1.0 - 2.0 * jnp.bitwise_and(parity, 1).astype(jnp.float32)


def kurtosis_from(powers, row_count):
    average = powers[0] / row_count
    second = powers[1] / row_count - average * average
    fourth = (
        powers[3] / row_count
        - 4.0 * average * powers[2] / row_count
        + 6.0 * average * average * powers[1] / row_count
        - 3.0 * average * average * average * average
    )
    return fourth / (second * second + 1e-06)


def shards(
    tokens, x_weight, bc_weight, dt_weight, conv_x, conv_bc, dt_bias, a_log, d_skip, norm_gain
):
    tok_rows = tokens.shape[1]
    model_width = tokens.shape[2]
    signs = hadamard_signs(ROOT)
    blocks = tokens.reshape(tok_rows, ROOT, ROOT)
    first_pass = jnp.einsum(
        "tab,ac->tcb", blocks, signs.astype(jnp.bfloat16), preferred_element_type=jnp.float32
    )
    second = jnp.einsum("tcb,bd->tcd", first_pass, signs, precision=HIGH)
    rotated = (second.reshape(tok_rows, model_width) / ROOT).astype(jnp.bfloat16)
    channel_share = model_width // lax.axis_size("mp")
    own_cols = lax.dynamic_slice_in_dim(
        rotated, lax.axis_index("mp") * channel_share, channel_share, 1
    ).astype(jnp.float32)
    square = own_cols * own_cols
    powers = jnp.stack(
        [
            jnp.sum(own_cols, 0),
            jnp.sum(square, 0),
            jnp.sum(square * own_cols, 0),
            jnp.sum(square * square, 0),
        ]
    )
    ctx_count = lax.axis_size("ch") * lax.axis_size("cl")
    row_count = float(tok_rows * lax.axis_size("dp") * ctx_count)
    totals = lax.psum(lax.psum(powers, CTX), "dp")
    totals, rotated = lax.optimization_barrier((totals, rotated))
    kurtosis = kurtosis_from(totals, row_count)
    local_panel = jnp.concatenate([x_weight, bc_weight, dt_weight], 1)
    panel = lax.all_gather(local_panel, CTX, axis=0, tiled=True)
    seqs = lax.axis_size("dp")
    share = model_width // seqs
    rim = 8
    earlier = passed_along(rotated[tok_rows - rim :], CTX, 1, ctx_count)
    extended = jnp.concatenate([earlier, rotated], 0)
    outgoing = extended.reshape(tok_rows + rim, seqs, share).transpose(1, 0, 2)
    incoming = lax.all_to_all(outgoing, "dp", 0, 0)
    x_end = x_weight.shape[1]
    bc_end = x_end + bc_weight.shape[1]
    side_partials = jnp.einsum(
        "kti,io->kto", incoming, panel[:, x_end:], preferred_element_type=jnp.float32
    )
    side_back = lax.all_to_all(side_partials.astype(jnp.bfloat16), "dp", 0, 0)
    x_partials = jnp.einsum(
        "kti,io->kto", incoming, panel[:, :x_end], preferred_element_type=jnp.float32
    )
    x_back = lax.all_to_all(x_partials.astype(jnp.bfloat16), "dp", 0, 0)
    side_ext = jnp.sum(side_back.astype(jnp.float32), 0)
    x_ext = jnp.sum(x_back.astype(jnp.float32), 0)
    x_cols = x_end
    bc_width = bc_end - x_end
    dt_proj = lax.optimization_barrier(side_ext[rim:, bc_width:].astype(jnp.bfloat16))
    kernel = conv_x.shape[0] - 1

    def causal_conv(rows, taps):
        padded = rows.astype(jnp.bfloat16)[rim - (kernel - 1) :]
        total = taps[kernel]
        for tap_index in range(kernel):
            total = total + taps[tap_index] * padded[tap_index : tap_index + tok_rows]
        return jax.nn.silu(total).astype(jnp.bfloat16)

    bc_own = causal_conv(side_ext[:, :bc_width], conv_bc)
    x_conv = causal_conv(x_ext, conv_x)
    heads_dev = dt_weight.shape[1]
    head_size = x_cols // heads_dev
    per_group = HEADS // G
    groups_here = max(1, heads_dev // per_group)
    heads_local = heads_dev // groups_here
    first_group = lax.axis_index("mp") * heads_dev // per_group
    mp_count = lax.axis_size("mp")
    if bc_own.shape[1] == NS and mp_count == 2 * G and groups_here == 1:
        owner = [m * heads_dev // per_group for m in range(mp_count)]
        odd_first = [(owner[m] if m % 2 == 0 else G + owner[m], m) for m in range(mp_count)]
        even_first = [(G + owner[m] if m % 2 == 0 else owner[m], m) for m in range(mp_count)]
        got_a = lax.ppermute(bc_own, "mp", odd_first)
        got_b = lax.ppermute(bc_own, "mp", even_first)
        even = lax.axis_index("mp") % 2 == 0
        write_here = jnp.where(even, got_a, got_b).reshape(tok_rows, 1, NS)
        read_here = jnp.where(even, got_b, got_a).reshape(tok_rows, 1, NS)
    else:
        group_all = lax.all_gather(bc_own, "mp", axis=1, tiled=True)
        write_all = group_all[:, : G * NS].reshape(tok_rows, G, NS)
        read_all = group_all[:, G * NS :].reshape(tok_rows, G, NS)
        write_here = lax.dynamic_slice_in_dim(write_all, first_group, groups_here, 1)
        read_here = lax.dynamic_slice_in_dim(read_all, first_group, groups_here, 1)
    step_size = jax.nn.softplus(dt_proj.astype(jnp.float32) + dt_bias)
    decay_rate = step_size * jnp.exp(a_log)
    cumulative = jnp.cumsum(decay_rate, 0)
    block_end = cumulative[-1]
    causal = lax.broadcasted_iota(jnp.int32, (tok_rows, tok_rows), 0) >= lax.broadcasted_iota(
        jnp.int32, (tok_rows, tok_rows), 1
    )
    spread = cumulative.T[:, :, None] - cumulative.T[:, None, :]
    decay_mask = jnp.where(causal, jnp.exp(-jnp.where(causal, spread, 0.0)), 0.0)
    scores = jnp.einsum("tgn,sgn->gts", read_here, write_here, preferred_element_type=jnp.float32)
    weights = (
        scores[:, None]
        * decay_mask.reshape(groups_here, heads_local, tok_rows, tok_rows)
        * step_size.T.reshape(groups_here, heads_local, 1, tok_rows)
    ).astype(jnp.bfloat16)
    x_heads = x_conv.reshape(tok_rows, groups_here, heads_local, head_size)
    within_block = jnp.einsum(
        "ghts,sghp->tghp", weights, x_heads, preferred_element_type=jnp.float32
    )
    update = (
        (jnp.exp(-(block_end - cumulative)) * step_size).reshape(
            tok_rows, groups_here, heads_local
        )[..., None]
        * x_heads
    ).astype(jnp.bfloat16)
    contrib = jnp.einsum("sghp,sgn->ghpn", update, write_here, preferred_element_type=jnp.float32)
    carried = entering(jnp.exp(-block_end).reshape(groups_here, heads_local), contrib)
    from_before = jnp.exp(-cumulative).reshape(tok_rows, groups_here, heads_local)[
        ..., None
    ] * jnp.einsum("tgn,ghpn->tghp", read_here.astype(jnp.float32), carried, precision=HIGH)
    output_raw = (
        within_block
        + from_before
        + d_skip.reshape(groups_here, heads_local)[None, :, :, None] * x_heads.astype(jnp.float32)
    )
    mean_square = jnp.mean(output_raw * output_raw, -1, keepdims=True)
    normed = (
        output_raw
        * lax.rsqrt(mean_square + 1e-05)
        * norm_gain.reshape(groups_here, heads_local, head_size)
    )
    return (normed.reshape(1, tok_rows, x_cols).astype(jnp.bfloat16), kurtosis)


def solution(mesh):
    grid = mesh.devices
    quad = 4 if grid.shape[1] % 4 == 0 else 1
    split = jax.sharding.Mesh(
        grid.reshape(grid.shape[0], grid.shape[1] // quad, quad, grid.shape[2]),
        ("dp", "ch", "cl", "mp"),
    )
    return jax.shard_map(
        shards,
        mesh=split,
        in_specs=(
            P("dp", CTX, None),
            P(("dp",) + CTX, "mp"),
            P(("dp",) + CTX, "mp"),
            P(("dp",) + CTX, "mp"),
            P(None, "mp"),
            P(None, "mp"),
            P("mp"),
            P("mp"),
            P("mp"),
            P("mp"),
        ),
        out_specs=(P("dp", CTX, "mp"), P("mp")),
        check_vma=False,
    )
```

```python
import jax
import jax.numpy as jnp
from jax import lax
from jax.sharding import PartitionSpec as P

ROOT = 64
HEADS = 128
G = 4
NS = 128


HIGH = lax.Precision.HIGHEST
CTX = ("ch", "cl")


def passed_along(value, axis, steps, count):
    first, last = (max(0, -steps), min(count, count - steps))
    return lax.ppermute(value, axis, [(source, source + steps) for source in range(first, last)])


def decay_products(row_decay, targets):
    count = row_decay.shape[0]
    target = lax.broadcasted_iota(jnp.int32, (targets, count, count), 0)
    source = lax.broadcasted_iota(jnp.int32, (targets, count, count), 1)
    between = lax.broadcasted_iota(jnp.int32, (targets, count, count), 2)
    inside = jnp.logical_and(between > source, between < target)
    factors = jnp.where(inside[..., None], row_decay[None, None], 1.0)
    products = jnp.prod(factors, 2)
    return jnp.where((source[:, :, 0] < target[:, :, 0])[..., None], products, 0.0)


def entering(decay, contrib):
    quads, quad = (lax.axis_index("ch"), lax.axis_size("cl"))
    place = lax.axis_index("cl")
    lanes = contrib.shape[-1]
    head_rows = contrib.shape[-2]
    heads = decay.size
    chunk = contrib.size // lanes // quad
    pieces = contrib.reshape(quad, chunk, lanes)
    tail = jnp.zeros((quad, 8, lanes), jnp.float32)
    tail = tail.at[:, 0, :heads].set(jnp.broadcast_to(decay.reshape(1, heads), (quad, heads)))
    outgoing = jnp.concatenate([pieces, tail], 1).astype(jnp.bfloat16)
    incoming = lax.all_to_all(outgoing, "cl", 0, 0).astype(jnp.float32)
    states = incoming[:, :chunk]
    decays = incoming[:, chunk, :heads]
    row_head = (place * chunk + lax.broadcasted_iota(jnp.int32, (chunk, heads), 0)) // head_rows
    pick = row_head == lax.broadcasted_iota(jnp.int32, (chunk, heads), 1)
    row_decay = jnp.sum(jnp.where(pick[None], decays[:, None, :], 0.0), -1)
    local = jnp.einsum(
        "kjr,jrl->krl", decay_products(row_decay, quad + 1), states, precision=HIGH
    )
    step = lax.broadcasted_iota(jnp.int32, (quad + 1, quad, chunk), 0)
    index = lax.broadcasted_iota(jnp.int32, (quad + 1, quad, chunk), 1)
    entry = jnp.prod(jnp.where(index < step, row_decay[None], 1.0), 1)
    pad_rows = 8 - (chunk // lanes) % 8
    summary = jnp.concatenate(
        [local[quad], entry[quad].reshape(chunk // lanes, lanes), jnp.zeros((pad_rows, lanes))]
    )
    count_hi = lax.axis_size("ch")
    summary = summary.astype(jnp.bfloat16)
    entering_state = jnp.zeros((chunk, lanes), jnp.float32)
    scale = jnp.ones((chunk,), jnp.float32)
    for shift in range(1, count_hi):
        pairs = [(source, source + shift) for source in range(count_hi - shift)]
        arrived = lax.ppermute(summary, "ch", pairs).astype(jnp.float32)
        entering_state = entering_state + scale[:, None] * arrived[:chunk]
        scale = scale * arrived[chunk : chunk + chunk // lanes].reshape(chunk)
    carried = local[:quad] + entry[:quad, :, None] * entering_state[None]
    returned = lax.all_to_all(carried.astype(jnp.bfloat16), "cl", 0, 0)
    return returned.astype(jnp.float32).reshape(contrib.shape)


def hadamard_signs(sign_order):
    row_index = lax.broadcasted_iota(jnp.int32, (sign_order, sign_order), 0)
    col_index = lax.broadcasted_iota(jnp.int32, (sign_order, sign_order), 1)
    common = jnp.bitwise_and(row_index, col_index)
    parity = jnp.zeros((sign_order, sign_order), jnp.int32)
    for bit_index in range(sign_order.bit_length() - 1):
        parity = parity + jnp.bitwise_and(jnp.right_shift(common, bit_index), 1)
    return 1.0 - 2.0 * jnp.bitwise_and(parity, 1).astype(jnp.float32)


def kurtosis_from(powers, row_count):
    average = powers[0] / row_count
    second = powers[1] / row_count - average * average
    fourth = (
        powers[3] / row_count
        - 4.0 * average * powers[2] / row_count
        + 6.0 * average * average * powers[1] / row_count
        - 3.0 * average * average * average * average
    )
    return fourth / (second * second + 1e-06)


def shards(
    tokens, x_weight, bc_weight, dt_weight, conv_x, conv_bc, dt_bias, a_log, d_skip, norm_gain
):
    tok_rows = tokens.shape[1]
    model_width = tokens.shape[2]
    signs = hadamard_signs(ROOT)
    blocks = tokens.reshape(tok_rows, ROOT, ROOT)
    first_pass = jnp.einsum(
        "tab,ac->tcb", blocks, signs.astype(jnp.bfloat16), preferred_element_type=jnp.float32
    )
    second = jnp.einsum("tcb,bd->tcd", first_pass, signs, precision=HIGH)
    rotated = (second.reshape(tok_rows, model_width) / ROOT).astype(jnp.bfloat16)
    channel_share = model_width // lax.axis_size("mp")
    own_cols = lax.dynamic_slice_in_dim(
        rotated, lax.axis_index("mp") * channel_share, channel_share, 1
    ).astype(jnp.float32)
    square = own_cols * own_cols
    powers = jnp.stack(
        [
            jnp.sum(own_cols, 0),
            jnp.sum(square, 0),
            jnp.sum(square * own_cols, 0),
            jnp.sum(square * square, 0),
        ]
    )
    ctx_count = lax.axis_size("ch") * lax.axis_size("cl")
    row_count = float(tok_rows * lax.axis_size("dp") * ctx_count)
    totals = lax.psum(lax.psum(powers, CTX), "dp")
    totals, rotated = lax.optimization_barrier((totals, rotated))
    kurtosis = kurtosis_from(totals, row_count)
    local_panel = jnp.concatenate([x_weight, bc_weight, dt_weight], 1)
    panel = lax.all_gather(local_panel, CTX, axis=0, tiled=True)
    seqs = lax.axis_size("dp")
    share = model_width // seqs
    rim = 8
    earlier = passed_along(rotated[tok_rows - rim :], CTX, 1, ctx_count)
    extended = jnp.concatenate([earlier, rotated], 0)
    outgoing = extended.reshape(tok_rows + rim, seqs, share).transpose(1, 0, 2)
    incoming = lax.all_to_all(outgoing, "dp", 0, 0)
    x_end = x_weight.shape[1]
    bc_end = x_end + bc_weight.shape[1]
    side_partials = jnp.einsum(
        "kti,io->kto", incoming, panel[:, x_end:], preferred_element_type=jnp.float32
    )
    side_back = lax.all_to_all(side_partials.astype(jnp.bfloat16), "dp", 0, 0)
    x_partials = jnp.einsum(
        "kti,io->kto", incoming, panel[:, :x_end], preferred_element_type=jnp.float32
    )
    x_back = lax.all_to_all(x_partials.astype(jnp.bfloat16), "dp", 0, 0)
    side_ext = jnp.sum(side_back.astype(jnp.float32), 0)
    x_ext = jnp.sum(x_back.astype(jnp.float32), 0)
    x_cols = x_end
    bc_width = bc_end - x_end
    dt_proj = lax.optimization_barrier(side_ext[rim:, bc_width:].astype(jnp.bfloat16))
    kernel = conv_x.shape[0] - 1

    def causal_conv(rows, taps):
        padded = rows.astype(jnp.bfloat16)[rim - (kernel - 1) :]
        total = taps[kernel]
        for tap_index in range(kernel):
            total = total + taps[tap_index] * padded[tap_index : tap_index + tok_rows]
        return jax.nn.silu(total).astype(jnp.bfloat16)

    bc_own = causal_conv(side_ext[:, :bc_width], conv_bc)
    x_conv = causal_conv(x_ext, conv_x)
    heads_dev = dt_weight.shape[1]
    head_size = x_cols // heads_dev
    per_group = HEADS // G
    groups_here = max(1, heads_dev // per_group)
    heads_local = heads_dev // groups_here
    first_group = lax.axis_index("mp") * heads_dev // per_group
    mp_count = lax.axis_size("mp")
    if bc_own.shape[1] == NS and mp_count == 2 * G and groups_here == 1:
        owner = [m * heads_dev // per_group for m in range(mp_count)]
        odd_first = [(owner[m] if m % 2 == 0 else G + owner[m], m) for m in range(mp_count)]
        even_first = [(G + owner[m] if m % 2 == 0 else owner[m], m) for m in range(mp_count)]
        got_a = lax.ppermute(bc_own, "mp", odd_first)
        got_b = lax.ppermute(bc_own, "mp", even_first)
        even = lax.axis_index("mp") % 2 == 0
        write_here = jnp.where(even, got_a, got_b).reshape(tok_rows, 1, NS)
        read_here = jnp.where(even, got_b, got_a).reshape(tok_rows, 1, NS)
    else:
        group_all = lax.all_gather(bc_own, "mp", axis=1, tiled=True)
        write_all = group_all[:, : G * NS].reshape(tok_rows, G, NS)
        read_all = group_all[:, G * NS :].reshape(tok_rows, G, NS)
        write_here = lax.dynamic_slice_in_dim(write_all, first_group, groups_here, 1)
        read_here = lax.dynamic_slice_in_dim(read_all, first_group, groups_here, 1)
    step_size = jax.nn.softplus(dt_proj.astype(jnp.float32) + dt_bias)
    decay_rate = step_size * jnp.exp(a_log)
    cumulative = jnp.cumsum(decay_rate, 0)
    block_end = cumulative[-1]
    causal = lax.broadcasted_iota(jnp.int32, (tok_rows, tok_rows), 0) >= lax.broadcasted_iota(
        jnp.int32, (tok_rows, tok_rows), 1
    )
    spread = cumulative.T[:, :, None] - cumulative.T[:, None, :]
    decay_mask = jnp.where(causal, jnp.exp(-jnp.where(causal, spread, 0.0)), 0.0)
    scores = jnp.einsum("tgn,sgn->gts", read_here, write_here, preferred_element_type=jnp.float32)
    weights = (
        scores[:, None]
        * decay_mask.reshape(groups_here, heads_local, tok_rows, tok_rows)
        * step_size.T.reshape(groups_here, heads_local, 1, tok_rows)
    ).astype(jnp.bfloat16)
    x_heads = x_conv.reshape(tok_rows, groups_here, heads_local, head_size)
    within_block = jnp.einsum(
        "ghts,sghp->tghp", weights, x_heads, preferred_element_type=jnp.float32
    )
    update = (
        (jnp.exp(-(block_end - cumulative)) * step_size).reshape(
            tok_rows, groups_here, heads_local
        )[..., None]
        * x_heads
    ).astype(jnp.bfloat16)
    contrib = jnp.einsum("sghp,sgn->ghpn", update, write_here, preferred_element_type=jnp.float32)
    carried = entering(jnp.exp(-block_end).reshape(groups_here, heads_local), contrib)
    from_before = jnp.exp(-cumulative).reshape(tok_rows, groups_here, heads_local)[
        ..., None
    ] * jnp.einsum("tgn,ghpn->tghp", read_here.astype(jnp.float32), carried, precision=HIGH)
    output_raw = (
        within_block
        + from_before
        + d_skip.reshape(groups_here, heads_local)[None, :, :, None] * x_heads.astype(jnp.float32)
    )
    mean_square = jnp.mean(output_raw * output_raw, -1, keepdims=True)
    normed = (
        output_raw
        * lax.rsqrt(mean_square + 1e-05)
        * norm_gain.reshape(groups_here, heads_local, head_size)
    )
    return (normed.reshape(1, tok_rows, x_cols).astype(jnp.bfloat16), kurtosis)


def solution(mesh):
    grid = mesh.devices
    quad = 4 if grid.shape[1] % 4 == 0 else 1
    split = jax.sharding.Mesh(
        grid.reshape(grid.shape[0], grid.shape[1] // quad, quad, grid.shape[2]),
        ("dp", "ch", "cl", "mp"),
    )
    return jax.shard_map(
        shards,
        mesh=split,
        in_specs=(
            P("dp", CTX, None),
            P(("dp",) + CTX, "mp"),
            P(("dp",) + CTX, "mp"),
            P(("dp",) + CTX, "mp"),
            P(None, "mp"),
            P(None, "mp"),
            P("mp"),
            P("mp"),
            P("mp"),
            P("mp"),
        ),
        out_specs=(P("dp", CTX, "mp"), P("mp")),
        check_vma=False,
    )
```

```python
import jax
import jax.numpy as jnp
from jax import lax
from jax.sharding import PartitionSpec as P

ROOT = 64
HEADS = 128
G = 4
NS = 128


HIGH = lax.Precision.HIGHEST
CTX = ("ch", "cl")


def passed_along(value, axis, steps, count):
    first, last = (max(0, -steps), min(count, count - steps))
    return lax.ppermute(value, axis, [(source, source + steps) for source in range(first, last)])


def decay_products(row_decay, targets):
    count = row_decay.shape[0]
    target = lax.broadcasted_iota(jnp.int32, (targets, count, count), 0)
    source = lax.broadcasted_iota(jnp.int32, (targets, count, count), 1)
    between = lax.broadcasted_iota(jnp.int32, (targets, count, count), 2)
    inside = jnp.logical_and(between > source, between < target)
    factors = jnp.where(inside[..., None], row_decay[None, None], 1.0)
    products = jnp.prod(factors, 2)
    return jnp.where((source[:, :, 0] < target[:, :, 0])[..., None], products, 0.0)


def entering(decay, contrib):
    quads, quad = (lax.axis_index("ch"), lax.axis_size("cl"))
    place = lax.axis_index("cl")
    lanes = contrib.shape[-1]
    head_rows = contrib.shape[-2]
    heads = decay.size
    chunk = contrib.size // lanes // quad
    pieces = contrib.reshape(quad, chunk, lanes)
    tail = jnp.zeros((quad, 8, lanes), jnp.float32)
    tail = tail.at[:, 0, :heads].set(jnp.broadcast_to(decay.reshape(1, heads), (quad, heads)))
    outgoing = jnp.concatenate([pieces, tail], 1).astype(jnp.bfloat16)
    incoming = lax.all_to_all(outgoing, "cl", 0, 0).astype(jnp.float32)
    states = incoming[:, :chunk]
    decays = incoming[:, chunk, :heads]
    row_head = (place * chunk + lax.broadcasted_iota(jnp.int32, (chunk, heads), 0)) // head_rows
    pick = row_head == lax.broadcasted_iota(jnp.int32, (chunk, heads), 1)
    row_decay = jnp.sum(jnp.where(pick[None], decays[:, None, :], 0.0), -1)
    local = jnp.einsum(
        "kjr,jrl->krl", decay_products(row_decay, quad + 1), states, precision=HIGH
    )
    step = lax.broadcasted_iota(jnp.int32, (quad + 1, quad, chunk), 0)
    index = lax.broadcasted_iota(jnp.int32, (quad + 1, quad, chunk), 1)
    entry = jnp.prod(jnp.where(index < step, row_decay[None], 1.0), 1)
    pad_rows = 8 - (chunk // lanes) % 8
    summary = jnp.concatenate(
        [local[quad], entry[quad].reshape(chunk // lanes, lanes), jnp.zeros((pad_rows, lanes))]
    )
    count_hi = lax.axis_size("ch")
    shared = lax.all_gather(summary.astype(jnp.bfloat16), "ch").astype(jnp.float32)
    totals = shared[:, :chunk]
    quad_decay = shared[:, chunk : chunk + chunk // lanes].reshape(count_hi, chunk)
    earlier = lax.broadcasted_iota(jnp.int32, (count_hi, count_hi, chunk), 0)
    middle = lax.broadcasted_iota(jnp.int32, (count_hi, count_hi, chunk), 1)
    spans = jnp.logical_and(middle > earlier, middle < quads)
    across = jnp.prod(jnp.where(spans, quad_decay[None], 1.0), 1)
    across = jnp.where(earlier[:, 0] < quads, across, 0.0)
    entering_state = jnp.einsum("qr,qrl->rl", across, totals, precision=HIGH)
    carried = local[:quad] + entry[:quad, :, None] * entering_state[None]
    returned = lax.all_to_all(carried.astype(jnp.bfloat16), "cl", 0, 0)
    return returned.astype(jnp.float32).reshape(contrib.shape)


def hadamard_signs(sign_order):
    row_index = lax.broadcasted_iota(jnp.int32, (sign_order, sign_order), 0)
    col_index = lax.broadcasted_iota(jnp.int32, (sign_order, sign_order), 1)
    common = jnp.bitwise_and(row_index, col_index)
    parity = jnp.zeros((sign_order, sign_order), jnp.int32)
    for bit_index in range(sign_order.bit_length() - 1):
        parity = parity + jnp.bitwise_and(jnp.right_shift(common, bit_index), 1)
    return 1.0 - 2.0 * jnp.bitwise_and(parity, 1).astype(jnp.float32)


def kurtosis_from(powers, row_count):
    average = powers[0] / row_count
    second = powers[1] / row_count - average * average
    fourth = (
        powers[3] / row_count
        - 4.0 * average * powers[2] / row_count
        + 6.0 * average * average * powers[1] / row_count
        - 3.0 * average * average * average * average
    )
    return fourth / (second * second + 1e-06)


def shards(
    tokens, x_weight, bc_weight, dt_weight, conv_x, conv_bc, dt_bias, a_log, d_skip, norm_gain
):
    tok_rows = tokens.shape[1]
    model_width = tokens.shape[2]
    signs = hadamard_signs(ROOT)
    blocks = tokens.reshape(tok_rows, ROOT, ROOT)
    first_pass = jnp.einsum(
        "tab,ac->tcb", blocks, signs.astype(jnp.bfloat16), preferred_element_type=jnp.float32
    )
    second = jnp.einsum("tcb,bd->tcd", first_pass, signs, precision=HIGH)
    rotated = (second.reshape(tok_rows, model_width) / ROOT).astype(jnp.bfloat16)
    channel_share = model_width // lax.axis_size("mp")
    own_cols = lax.dynamic_slice_in_dim(
        rotated, lax.axis_index("mp") * channel_share, channel_share, 1
    ).astype(jnp.float32)
    square = own_cols * own_cols
    powers = jnp.stack(
        [
            jnp.sum(own_cols, 0),
            jnp.sum(square, 0),
            jnp.sum(square * own_cols, 0),
            jnp.sum(square * square, 0),
        ]
    )
    ctx_count = lax.axis_size("ch") * lax.axis_size("cl")
    row_count = float(tok_rows * lax.axis_size("dp") * ctx_count)
    totals = lax.psum(lax.psum(powers, CTX), "dp")
    totals, rotated = lax.optimization_barrier((totals, rotated))
    kurtosis = kurtosis_from(totals, row_count)
    local_panel = jnp.concatenate([x_weight, bc_weight, dt_weight], 1)
    panel = lax.all_gather(local_panel, CTX, axis=0, tiled=True)
    seqs = lax.axis_size("dp")
    share = model_width // seqs
    rim = 8
    earlier = passed_along(rotated[tok_rows - rim :], CTX, 1, ctx_count)
    extended = jnp.concatenate([earlier, rotated], 0)
    outgoing = extended.reshape(tok_rows + rim, seqs, share).transpose(1, 0, 2)
    incoming = lax.all_to_all(outgoing, "dp", 0, 0)
    x_end = x_weight.shape[1]
    bc_end = x_end + bc_weight.shape[1]
    side_partials = jnp.einsum(
        "kti,io->kto", incoming, panel[:, x_end:], preferred_element_type=jnp.float32
    )
    side_back = lax.all_to_all(side_partials, "dp", 0, 0)
    x_partials = jnp.einsum(
        "kti,io->kto", incoming, panel[:, :x_end], preferred_element_type=jnp.float32
    )
    x_back = lax.all_to_all(x_partials, "dp", 0, 0)
    side_ext = jnp.sum(side_back, 0)
    x_ext = jnp.sum(x_back, 0)
    x_cols = x_end
    bc_width = bc_end - x_end
    dt_proj = lax.optimization_barrier(side_ext[rim:, bc_width:].astype(jnp.bfloat16))
    kernel = conv_x.shape[0] - 1

    def causal_conv(rows, taps):
        padded = rows.astype(jnp.bfloat16)[rim - (kernel - 1) :]
        total = taps[kernel]
        for tap_index in range(kernel):
            total = total + taps[tap_index] * padded[tap_index : tap_index + tok_rows]
        return jax.nn.silu(total).astype(jnp.bfloat16)

    bc_own = causal_conv(side_ext[:, :bc_width], conv_bc)
    x_conv = causal_conv(x_ext, conv_x)
    heads_dev = dt_weight.shape[1]
    head_size = x_cols // heads_dev
    per_group = HEADS // G
    groups_here = max(1, heads_dev // per_group)
    heads_local = heads_dev // groups_here
    first_group = lax.axis_index("mp") * heads_dev // per_group
    mp_count = lax.axis_size("mp")
    if bc_own.shape[1] == NS and mp_count == 2 * G and groups_here == 1:
        owner = [m * heads_dev // per_group for m in range(mp_count)]
        odd_first = [(owner[m] if m % 2 == 0 else G + owner[m], m) for m in range(mp_count)]
        even_first = [(G + owner[m] if m % 2 == 0 else owner[m], m) for m in range(mp_count)]
        got_a = lax.ppermute(bc_own, "mp", odd_first)
        got_b = lax.ppermute(bc_own, "mp", even_first)
        even = lax.axis_index("mp") % 2 == 0
        write_here = jnp.where(even, got_a, got_b).reshape(tok_rows, 1, NS)
        read_here = jnp.where(even, got_b, got_a).reshape(tok_rows, 1, NS)
    else:
        group_all = lax.all_gather(bc_own, "mp", axis=1, tiled=True)
        write_all = group_all[:, : G * NS].reshape(tok_rows, G, NS)
        read_all = group_all[:, G * NS :].reshape(tok_rows, G, NS)
        write_here = lax.dynamic_slice_in_dim(write_all, first_group, groups_here, 1)
        read_here = lax.dynamic_slice_in_dim(read_all, first_group, groups_here, 1)
    step_size = jax.nn.softplus(dt_proj.astype(jnp.float32) + dt_bias)
    decay_rate = step_size * jnp.exp(a_log)
    cumulative = jnp.cumsum(decay_rate, 0)
    block_end = cumulative[-1]
    causal = lax.broadcasted_iota(jnp.int32, (tok_rows, tok_rows), 0) >= lax.broadcasted_iota(
        jnp.int32, (tok_rows, tok_rows), 1
    )
    spread = cumulative.T[:, :, None] - cumulative.T[:, None, :]
    decay_mask = jnp.where(causal, jnp.exp(-jnp.where(causal, spread, 0.0)), 0.0)
    scores = jnp.einsum("tgn,sgn->gts", read_here, write_here, preferred_element_type=jnp.float32)
    weights = (
        scores[:, None]
        * decay_mask.reshape(groups_here, heads_local, tok_rows, tok_rows)
        * step_size.T.reshape(groups_here, heads_local, 1, tok_rows)
    ).astype(jnp.bfloat16)
    x_heads = x_conv.reshape(tok_rows, groups_here, heads_local, head_size)
    within_block = jnp.einsum(
        "ghts,sghp->tghp", weights, x_heads, preferred_element_type=jnp.float32
    )
    update = (
        (jnp.exp(-(block_end - cumulative)) * step_size).reshape(
            tok_rows, groups_here, heads_local
        )[..., None]
        * x_heads
    ).astype(jnp.bfloat16)
    contrib = jnp.einsum("sghp,sgn->ghpn", update, write_here, preferred_element_type=jnp.float32)
    carried = entering(jnp.exp(-block_end).reshape(groups_here, heads_local), contrib)
    from_before = jnp.exp(-cumulative).reshape(tok_rows, groups_here, heads_local)[
        ..., None
    ] * jnp.einsum("tgn,ghpn->tghp", read_here.astype(jnp.float32), carried, precision=HIGH)
    output_raw = (
        within_block
        + from_before
        + d_skip.reshape(groups_here, heads_local)[None, :, :, None] * x_heads.astype(jnp.float32)
    )
    mean_square = jnp.mean(output_raw * output_raw, -1, keepdims=True)
    normed = (
        output_raw
        * lax.rsqrt(mean_square + 1e-05)
        * norm_gain.reshape(groups_here, heads_local, head_size)
    )
    return (normed.reshape(1, tok_rows, x_cols).astype(jnp.bfloat16), kurtosis)


def solution(mesh):
    grid = mesh.devices
    quad = 4 if grid.shape[1] % 4 == 0 else 1
    split = jax.sharding.Mesh(
        grid.reshape(grid.shape[0], grid.shape[1] // quad, quad, grid.shape[2]),
        ("dp", "ch", "cl", "mp"),
    )
    return jax.shard_map(
        shards,
        mesh=split,
        in_specs=(
            P("dp", CTX, None),
            P(("dp",) + CTX, "mp"),
            P(("dp",) + CTX, "mp"),
            P(("dp",) + CTX, "mp"),
            P(None, "mp"),
            P(None, "mp"),
            P("mp"),
            P("mp"),
            P("mp"),
            P("mp"),
        ),
        out_specs=(P("dp", CTX, "mp"), P("mp")),
        check_vma=False,
    )
```

```python
import jax
import jax.numpy as jnp
from jax import lax
from jax.sharding import PartitionSpec as P

ROOT = 64
HEADS = 128
G = 4
NS = 128


HIGH = lax.Precision.HIGHEST
CTX = ("ch", "cl")


def passed_along(value, axis, steps, count):
    first, last = (max(0, -steps), min(count, count - steps))
    return lax.ppermute(value, axis, [(source, source + steps) for source in range(first, last)])


def decay_products(row_decay, targets):
    count = row_decay.shape[0]
    target = lax.broadcasted_iota(jnp.int32, (targets, count, count), 0)
    source = lax.broadcasted_iota(jnp.int32, (targets, count, count), 1)
    between = lax.broadcasted_iota(jnp.int32, (targets, count, count), 2)
    inside = jnp.logical_and(between > source, between < target)
    factors = jnp.where(inside[..., None], row_decay[None, None], 1.0)
    products = jnp.prod(factors, 2)
    return jnp.where((source[:, :, 0] < target[:, :, 0])[..., None], products, 0.0)


def entering(decay, contrib):
    quads, quad = (lax.axis_index("ch"), lax.axis_size("cl"))
    place = lax.axis_index("cl")
    lanes = contrib.shape[-1]
    head_rows = contrib.shape[-2]
    heads = decay.size
    chunk = contrib.size // lanes // quad
    pieces = contrib.reshape(quad, chunk, lanes)
    tail = jnp.zeros((quad, 8, lanes), jnp.float32)
    tail = tail.at[:, 0, :heads].set(jnp.broadcast_to(decay.reshape(1, heads), (quad, heads)))
    outgoing = jnp.concatenate([pieces, tail], 1).astype(jnp.bfloat16)
    incoming = lax.all_to_all(outgoing, "cl", 0, 0).astype(jnp.float32)
    states = incoming[:, :chunk]
    decays = incoming[:, chunk, :heads]
    row_head = (place * chunk + lax.broadcasted_iota(jnp.int32, (chunk, heads), 0)) // head_rows
    pick = row_head == lax.broadcasted_iota(jnp.int32, (chunk, heads), 1)
    row_decay = jnp.sum(jnp.where(pick[None], decays[:, None, :], 0.0), -1)
    local = jnp.einsum(
        "kjr,jrl->krl", decay_products(row_decay, quad + 1), states, precision=HIGH
    )
    step = lax.broadcasted_iota(jnp.int32, (quad + 1, quad, chunk), 0)
    index = lax.broadcasted_iota(jnp.int32, (quad + 1, quad, chunk), 1)
    entry = jnp.prod(jnp.where(index < step, row_decay[None], 1.0), 1)
    pad_rows = 8 - (chunk // lanes) % 8
    summary = jnp.concatenate(
        [local[quad], entry[quad].reshape(chunk // lanes, lanes), jnp.zeros((pad_rows, lanes))]
    )
    count_hi = lax.axis_size("ch")
    shared = lax.all_gather(summary.astype(jnp.bfloat16), "ch").astype(jnp.float32)
    totals = shared[:, :chunk]
    quad_decay = shared[:, chunk : chunk + chunk // lanes].reshape(count_hi, chunk)
    earlier = lax.broadcasted_iota(jnp.int32, (count_hi, count_hi, chunk), 0)
    middle = lax.broadcasted_iota(jnp.int32, (count_hi, count_hi, chunk), 1)
    spans = jnp.logical_and(middle > earlier, middle < quads)
    across = jnp.prod(jnp.where(spans, quad_decay[None], 1.0), 1)
    across = jnp.where(earlier[:, 0] < quads, across, 0.0)
    entering_state = jnp.einsum("qr,qrl->rl", across, totals, precision=HIGH)
    carried = local[:quad] + entry[:quad, :, None] * entering_state[None]
    returned = lax.all_to_all(carried.astype(jnp.bfloat16), "cl", 0, 0)
    return returned.astype(jnp.float32).reshape(contrib.shape)


def hadamard_signs(sign_order):
    row_index = lax.broadcasted_iota(jnp.int32, (sign_order, sign_order), 0)
    col_index = lax.broadcasted_iota(jnp.int32, (sign_order, sign_order), 1)
    common = jnp.bitwise_and(row_index, col_index)
    parity = jnp.zeros((sign_order, sign_order), jnp.int32)
    for bit_index in range(sign_order.bit_length() - 1):
        parity = parity + jnp.bitwise_and(jnp.right_shift(common, bit_index), 1)
    return 1.0 - 2.0 * jnp.bitwise_and(parity, 1).astype(jnp.float32)


def kurtosis_from(powers, row_count):
    average = powers[0] / row_count
    second = powers[1] / row_count - average * average
    fourth = (
        powers[3] / row_count
        - 4.0 * average * powers[2] / row_count
        + 6.0 * average * average * powers[1] / row_count
        - 3.0 * average * average * average * average
    )
    return fourth / (second * second + 1e-06)


def shards(
    tokens, x_weight, bc_weight, dt_weight, conv_x, conv_bc, dt_bias, a_log, d_skip, norm_gain
):
    tok_rows = tokens.shape[1]
    model_width = tokens.shape[2]
    signs = hadamard_signs(ROOT)
    blocks = tokens.reshape(tok_rows, ROOT, ROOT)
    first_pass = jnp.einsum(
        "tab,ac->tcb", blocks, signs.astype(jnp.bfloat16), preferred_element_type=jnp.float32
    )
    second = jnp.einsum("tcb,bd->tcd", first_pass, signs, precision=HIGH)
    rotated = (second.reshape(tok_rows, model_width) / ROOT).astype(jnp.bfloat16)
    channel_share = model_width // lax.axis_size("mp")
    own_cols = lax.dynamic_slice_in_dim(
        rotated, lax.axis_index("mp") * channel_share, channel_share, 1
    ).astype(jnp.float32)
    square = own_cols * own_cols
    powers = jnp.stack(
        [
            jnp.sum(own_cols, 0),
            jnp.sum(square, 0),
            jnp.sum(square * own_cols, 0),
            jnp.sum(square * square, 0),
        ]
    )
    ctx_count = lax.axis_size("ch") * lax.axis_size("cl")
    row_count = float(tok_rows * lax.axis_size("dp") * ctx_count)
    totals = lax.psum(lax.psum(powers, CTX), "dp")
    totals, rotated = lax.optimization_barrier((totals, rotated))
    kurtosis = kurtosis_from(totals, row_count)
    local_panel = jnp.concatenate([x_weight, bc_weight, dt_weight], 1)
    panel = lax.all_gather(local_panel, CTX, axis=0, tiled=True)
    seqs = lax.axis_size("dp")
    share = model_width // seqs
    rim = 8
    earlier = passed_along(rotated[tok_rows - rim :], CTX, 1, ctx_count)
    extended = jnp.concatenate([earlier, rotated], 0)
    outgoing = extended.reshape(tok_rows + rim, seqs, share).transpose(1, 0, 2)
    incoming = lax.all_to_all(outgoing, "dp", 0, 0)
    x_end = x_weight.shape[1]
    bc_end = x_end + bc_weight.shape[1]
    side_partials = jnp.einsum(
        "kti,io->kto", incoming, panel[:, x_end:], preferred_element_type=jnp.float32
    )
    place_dp = lax.axis_index("dp")
    side_ext = lax.dynamic_index_in_dim(side_partials, place_dp, 0, keepdims=False)
    for shift in range(1, seqs):
        outgoing_side = lax.dynamic_index_in_dim(
            side_partials, (place_dp + shift) % seqs, 0, keepdims=False
        )
        side_ext = side_ext + lax.ppermute(
            outgoing_side, "dp", [(k, (k + shift) % seqs) for k in range(seqs)]
        )
    x_partials = jnp.einsum(
        "kti,io->kto", incoming, panel[:, :x_end], preferred_element_type=jnp.float32
    )
    x_back = lax.all_to_all(x_partials, "dp", 0, 0)
    x_ext = jnp.sum(x_back, 0)
    x_cols = x_end
    bc_width = bc_end - x_end
    dt_proj = lax.optimization_barrier(side_ext[rim:, bc_width:].astype(jnp.bfloat16))
    kernel = conv_x.shape[0] - 1

    def causal_conv(rows, taps):
        padded = rows.astype(jnp.bfloat16)[rim - (kernel - 1) :]
        total = taps[kernel]
        for tap_index in range(kernel):
            total = total + taps[tap_index] * padded[tap_index : tap_index + tok_rows]
        return jax.nn.silu(total).astype(jnp.bfloat16)

    bc_own = causal_conv(side_ext[:, :bc_width], conv_bc)
    x_conv = causal_conv(x_ext, conv_x)
    heads_dev = dt_weight.shape[1]
    head_size = x_cols // heads_dev
    per_group = HEADS // G
    groups_here = max(1, heads_dev // per_group)
    heads_local = heads_dev // groups_here
    first_group = lax.axis_index("mp") * heads_dev // per_group
    mp_count = lax.axis_size("mp")
    if bc_own.shape[1] == NS and mp_count == 2 * G and groups_here == 1:
        owner = [m * heads_dev // per_group for m in range(mp_count)]
        odd_first = [(owner[m] if m % 2 == 0 else G + owner[m], m) for m in range(mp_count)]
        even_first = [(G + owner[m] if m % 2 == 0 else owner[m], m) for m in range(mp_count)]
        got_a = lax.ppermute(bc_own, "mp", odd_first)
        got_b = lax.ppermute(bc_own, "mp", even_first)
        even = lax.axis_index("mp") % 2 == 0
        write_here = jnp.where(even, got_a, got_b).reshape(tok_rows, 1, NS)
        read_here = jnp.where(even, got_b, got_a).reshape(tok_rows, 1, NS)
    else:
        group_all = lax.all_gather(bc_own, "mp", axis=1, tiled=True)
        write_all = group_all[:, : G * NS].reshape(tok_rows, G, NS)
        read_all = group_all[:, G * NS :].reshape(tok_rows, G, NS)
        write_here = lax.dynamic_slice_in_dim(write_all, first_group, groups_here, 1)
        read_here = lax.dynamic_slice_in_dim(read_all, first_group, groups_here, 1)
    step_size = jax.nn.softplus(dt_proj.astype(jnp.float32) + dt_bias)
    decay_rate = step_size * jnp.exp(a_log)
    cumulative = jnp.cumsum(decay_rate, 0)
    block_end = cumulative[-1]
    causal = lax.broadcasted_iota(jnp.int32, (tok_rows, tok_rows), 0) >= lax.broadcasted_iota(
        jnp.int32, (tok_rows, tok_rows), 1
    )
    spread = cumulative.T[:, :, None] - cumulative.T[:, None, :]
    decay_mask = jnp.where(causal, jnp.exp(-jnp.where(causal, spread, 0.0)), 0.0)
    scores = jnp.einsum("tgn,sgn->gts", read_here, write_here, preferred_element_type=jnp.float32)
    weights = (
        scores[:, None]
        * decay_mask.reshape(groups_here, heads_local, tok_rows, tok_rows)
        * step_size.T.reshape(groups_here, heads_local, 1, tok_rows)
    ).astype(jnp.bfloat16)
    x_heads = x_conv.reshape(tok_rows, groups_here, heads_local, head_size)
    within_block = jnp.einsum(
        "ghts,sghp->tghp", weights, x_heads, preferred_element_type=jnp.float32
    )
    update = (
        (jnp.exp(-(block_end - cumulative)) * step_size).reshape(
            tok_rows, groups_here, heads_local
        )[..., None]
        * x_heads
    ).astype(jnp.bfloat16)
    contrib = jnp.einsum("sghp,sgn->ghpn", update, write_here, preferred_element_type=jnp.float32)
    carried = entering(jnp.exp(-block_end).reshape(groups_here, heads_local), contrib)
    from_before = jnp.exp(-cumulative).reshape(tok_rows, groups_here, heads_local)[
        ..., None
    ] * jnp.einsum("tgn,ghpn->tghp", read_here.astype(jnp.float32), carried, precision=HIGH)
    output_raw = (
        within_block
        + from_before
        + d_skip.reshape(groups_here, heads_local)[None, :, :, None] * x_heads.astype(jnp.float32)
    )
    mean_square = jnp.mean(output_raw * output_raw, -1, keepdims=True)
    normed = (
        output_raw
        * lax.rsqrt(mean_square + 1e-05)
        * norm_gain.reshape(groups_here, heads_local, head_size)
    )
    return (normed.reshape(1, tok_rows, x_cols).astype(jnp.bfloat16), kurtosis)


def solution(mesh):
    grid = mesh.devices
    quad = 4 if grid.shape[1] % 4 == 0 else 1
    split = jax.sharding.Mesh(
        grid.reshape(grid.shape[0], grid.shape[1] // quad, quad, grid.shape[2]),
        ("dp", "ch", "cl", "mp"),
    )
    return jax.shard_map(
        shards,
        mesh=split,
        in_specs=(
            P("dp", CTX, None),
            P(("dp",) + CTX, "mp"),
            P(("dp",) + CTX, "mp"),
            P(("dp",) + CTX, "mp"),
            P(None, "mp"),
            P(None, "mp"),
            P("mp"),
            P("mp"),
            P("mp"),
            P("mp"),
        ),
        out_specs=(P("dp", CTX, "mp"), P("mp")),
        check_vma=False,
    )
```

```python
import jax
import jax.numpy as jnp
from jax import lax
from jax.sharding import PartitionSpec as P

ROOT = 64
HEADS = 128
G = 4
NS = 128


HIGH = lax.Precision.HIGHEST
CTX = ("ch", "cl")


def passed_along(value, axis, steps, count):
    first, last = (max(0, -steps), min(count, count - steps))
    return lax.ppermute(value, axis, [(source, source + steps) for source in range(first, last)])


def decay_products(row_decay, targets):
    count = row_decay.shape[0]
    target = lax.broadcasted_iota(jnp.int32, (targets, count, count), 0)
    source = lax.broadcasted_iota(jnp.int32, (targets, count, count), 1)
    between = lax.broadcasted_iota(jnp.int32, (targets, count, count), 2)
    inside = jnp.logical_and(between > source, between < target)
    factors = jnp.where(inside[..., None], row_decay[None, None], 1.0)
    products = jnp.prod(factors, 2)
    return jnp.where((source[:, :, 0] < target[:, :, 0])[..., None], products, 0.0)


def entering(decay, contrib):
    quads, quad = (lax.axis_index("ch"), lax.axis_size("cl"))
    place = lax.axis_index("cl")
    lanes = contrib.shape[-1]
    head_rows = contrib.shape[-2]
    heads = decay.size
    chunk = contrib.size // lanes // quad
    pieces = contrib.reshape(quad, chunk, lanes)
    tail = jnp.zeros((quad, 8, lanes), jnp.float32)
    tail = tail.at[:, 0, :heads].set(jnp.broadcast_to(decay.reshape(1, heads), (quad, heads)))
    outgoing = jnp.concatenate([pieces, tail], 1).astype(jnp.bfloat16)
    incoming = lax.all_to_all(outgoing, "cl", 0, 0).astype(jnp.float32)
    states = incoming[:, :chunk]
    decays = incoming[:, chunk, :heads]
    row_head = (place * chunk + lax.broadcasted_iota(jnp.int32, (chunk, heads), 0)) // head_rows
    pick = row_head == lax.broadcasted_iota(jnp.int32, (chunk, heads), 1)
    row_decay = jnp.sum(jnp.where(pick[None], decays[:, None, :], 0.0), -1)
    local = jnp.einsum(
        "kjr,jrl->krl", decay_products(row_decay, quad + 1), states, precision=HIGH
    )
    step = lax.broadcasted_iota(jnp.int32, (quad + 1, quad, chunk), 0)
    index = lax.broadcasted_iota(jnp.int32, (quad + 1, quad, chunk), 1)
    entry = jnp.prod(jnp.where(index < step, row_decay[None], 1.0), 1)
    pad_rows = 8 - (chunk // lanes) % 8
    summary = jnp.concatenate(
        [local[quad], entry[quad].reshape(chunk // lanes, lanes), jnp.zeros((pad_rows, lanes))]
    )
    count_hi = lax.axis_size("ch")
    shared = lax.all_gather(summary.astype(jnp.bfloat16), "ch").astype(jnp.float32)
    totals = shared[:, :chunk]
    quad_decay = shared[:, chunk : chunk + chunk // lanes].reshape(count_hi, chunk)
    earlier = lax.broadcasted_iota(jnp.int32, (count_hi, count_hi, chunk), 0)
    middle = lax.broadcasted_iota(jnp.int32, (count_hi, count_hi, chunk), 1)
    spans = jnp.logical_and(middle > earlier, middle < quads)
    across = jnp.prod(jnp.where(spans, quad_decay[None], 1.0), 1)
    across = jnp.where(earlier[:, 0] < quads, across, 0.0)
    entering_state = jnp.einsum("qr,qrl->rl", across, totals, precision=HIGH)
    carried = local[:quad] + entry[:quad, :, None] * entering_state[None]
    returned = lax.all_to_all(carried.astype(jnp.bfloat16), "cl", 0, 0)
    return returned.astype(jnp.float32).reshape(contrib.shape)


def hadamard_signs(sign_order):
    row_index = lax.broadcasted_iota(jnp.int32, (sign_order, sign_order), 0)
    col_index = lax.broadcasted_iota(jnp.int32, (sign_order, sign_order), 1)
    common = jnp.bitwise_and(row_index, col_index)
    parity = jnp.zeros((sign_order, sign_order), jnp.int32)
    for bit_index in range(sign_order.bit_length() - 1):
        parity = parity + jnp.bitwise_and(jnp.right_shift(common, bit_index), 1)
    return 1.0 - 2.0 * jnp.bitwise_and(parity, 1).astype(jnp.float32)


def kurtosis_from(powers, row_count):
    average = powers[0] / row_count
    second = powers[1] / row_count - average * average
    fourth = (
        powers[3] / row_count
        - 4.0 * average * powers[2] / row_count
        + 6.0 * average * average * powers[1] / row_count
        - 3.0 * average * average * average * average
    )
    return fourth / (second * second + 1e-06)


def shards(
    tokens, x_weight, bc_weight, dt_weight, conv_x, conv_bc, dt_bias, a_log, d_skip, norm_gain
):
    tok_rows = tokens.shape[1]
    model_width = tokens.shape[2]
    signs = hadamard_signs(ROOT)
    blocks = tokens.reshape(tok_rows, ROOT, ROOT)
    first_pass = jnp.einsum(
        "tab,ac->tcb", blocks, signs.astype(jnp.bfloat16), preferred_element_type=jnp.float32
    )
    second = jnp.einsum("tcb,bd->tcd", first_pass, signs, precision=HIGH)
    rotated = (second.reshape(tok_rows, model_width) / ROOT).astype(jnp.bfloat16)
    channel_share = model_width // lax.axis_size("mp")
    own_cols = lax.dynamic_slice_in_dim(
        rotated, lax.axis_index("mp") * channel_share, channel_share, 1
    ).astype(jnp.float32)
    square = own_cols * own_cols
    powers = jnp.stack(
        [
            jnp.sum(own_cols, 0),
            jnp.sum(square, 0),
            jnp.sum(square * own_cols, 0),
            jnp.sum(square * square, 0),
        ]
    )
    ctx_count = lax.axis_size("ch") * lax.axis_size("cl")
    row_count = float(tok_rows * lax.axis_size("dp") * ctx_count)
    totals = lax.psum(lax.psum(powers, CTX), "dp")
    totals, rotated = lax.optimization_barrier((totals, rotated))
    kurtosis = kurtosis_from(totals, row_count)
    heads_dev = dt_weight.shape[1]
    per_group = HEADS // G
    mp_count = lax.axis_size("mp")
    owner = [m * heads_dev // per_group for m in range(mp_count)]
    write_first = [(owner[m] if m % 2 == 0 else G + owner[m], m) for m in range(mp_count)]
    read_first = [(G + owner[m] if m % 2 == 0 else owner[m], m) for m in range(mp_count)]
    even = lax.axis_index("mp") % 2 == 0

    def group_pair(value):
        got_a = lax.ppermute(value, "mp", write_first)
        got_b = lax.ppermute(value, "mp", read_first)
        return jnp.where(even, got_a, got_b), jnp.where(even, got_b, got_a)

    write_weight, read_weight = group_pair(bc_weight)
    write_taps, read_taps = group_pair(conv_bc)
    local_panel = jnp.concatenate([x_weight, write_weight, read_weight, dt_weight], 1)
    panel = lax.all_gather(local_panel, CTX, axis=0, tiled=True)
    seqs = lax.axis_size("dp")
    share = model_width // seqs
    rim = 8
    earlier = passed_along(rotated[tok_rows - rim :], CTX, 1, ctx_count)
    extended = jnp.concatenate([earlier, rotated], 0)
    outgoing = extended.reshape(tok_rows + rim, seqs, share).transpose(1, 0, 2)
    incoming = lax.all_to_all(outgoing, "dp", 0, 0)
    x_end = x_weight.shape[1]
    bc_end = x_end + bc_weight.shape[1]
    partials = jnp.einsum("kti,io->kto", incoming, panel, preferred_element_type=jnp.float32)
    both_ext = jnp.sum(lax.all_to_all(partials, "dp", 0, 0), 0)
    x_end = x_weight.shape[1]
    x_cols = x_end
    group_end = x_end + 2 * NS
    dt_proj = lax.optimization_barrier(both_ext[rim:, group_end:].astype(jnp.bfloat16))
    kernel = conv_x.shape[0] - 1

    def causal_conv(rows, taps):
        padded = rows.astype(jnp.bfloat16)[rim - (kernel - 1) :]
        total = taps[kernel]
        for tap_index in range(kernel):
            total = total + taps[tap_index] * padded[tap_index : tap_index + tok_rows]
        return jax.nn.silu(total).astype(jnp.bfloat16)

    x_conv = causal_conv(both_ext[:, :x_end], conv_x)
    write_here = causal_conv(both_ext[:, x_end : x_end + NS], write_taps).reshape(tok_rows, 1, NS)
    read_here = causal_conv(both_ext[:, x_end + NS : group_end], read_taps).reshape(tok_rows, 1, NS)
    head_size = x_cols // heads_dev
    groups_here = max(1, heads_dev // per_group)
    heads_local = heads_dev // groups_here
    step_size = jax.nn.softplus(dt_proj.astype(jnp.float32) + dt_bias)
    decay_rate = step_size * jnp.exp(a_log)
    cumulative = jnp.cumsum(decay_rate, 0)
    block_end = cumulative[-1]
    causal = lax.broadcasted_iota(jnp.int32, (tok_rows, tok_rows), 0) >= lax.broadcasted_iota(
        jnp.int32, (tok_rows, tok_rows), 1
    )
    spread = cumulative.T[:, :, None] - cumulative.T[:, None, :]
    decay_mask = jnp.where(causal, jnp.exp(-jnp.where(causal, spread, 0.0)), 0.0)
    scores = jnp.einsum("tgn,sgn->gts", read_here, write_here, preferred_element_type=jnp.float32)
    weights = (
        scores[:, None]
        * decay_mask.reshape(groups_here, heads_local, tok_rows, tok_rows)
        * step_size.T.reshape(groups_here, heads_local, 1, tok_rows)
    ).astype(jnp.bfloat16)
    x_heads = x_conv.reshape(tok_rows, groups_here, heads_local, head_size)
    within_block = jnp.einsum(
        "ghts,sghp->tghp", weights, x_heads, preferred_element_type=jnp.float32
    )
    update = (
        (jnp.exp(-(block_end - cumulative)) * step_size).reshape(
            tok_rows, groups_here, heads_local
        )[..., None]
        * x_heads
    ).astype(jnp.bfloat16)
    contrib = jnp.einsum("sghp,sgn->ghpn", update, write_here, preferred_element_type=jnp.float32)
    carried = entering(jnp.exp(-block_end).reshape(groups_here, heads_local), contrib)
    from_before = jnp.exp(-cumulative).reshape(tok_rows, groups_here, heads_local)[
        ..., None
    ] * jnp.einsum("tgn,ghpn->tghp", read_here.astype(jnp.float32), carried, precision=HIGH)
    output_raw = (
        within_block
        + from_before
        + d_skip.reshape(groups_here, heads_local)[None, :, :, None] * x_heads.astype(jnp.float32)
    )
    mean_square = jnp.mean(output_raw * output_raw, -1, keepdims=True)
    normed = (
        output_raw
        * lax.rsqrt(mean_square + 1e-05)
        * norm_gain.reshape(groups_here, heads_local, head_size)
    )
    return (normed.reshape(1, tok_rows, x_cols).astype(jnp.bfloat16), kurtosis)


def solution(mesh):
    grid = mesh.devices
    quad = 4 if grid.shape[1] % 4 == 0 else 1
    split = jax.sharding.Mesh(
        grid.reshape(grid.shape[0], grid.shape[1] // quad, quad, grid.shape[2]),
        ("dp", "ch", "cl", "mp"),
    )
    return jax.shard_map(
        shards,
        mesh=split,
        in_specs=(
            P("dp", CTX, None),
            P(("dp",) + CTX, "mp"),
            P(("dp",) + CTX, "mp"),
            P(("dp",) + CTX, "mp"),
            P(None, "mp"),
            P(None, "mp"),
            P("mp"),
            P("mp"),
            P("mp"),
            P("mp"),
        ),
        out_specs=(P("dp", CTX, "mp"), P("mp")),
        check_vma=False,
    )
```

```python
import jax
import jax.numpy as jnp
from jax import lax
from jax.sharding import PartitionSpec as P

ROOT = 64
HEADS = 128
G = 4
NS = 128


HIGH = lax.Precision.HIGHEST
CTX = ("ch", "cl")


def passed_along(value, axis, steps, count):
    first, last = (max(0, -steps), min(count, count - steps))
    return lax.ppermute(value, axis, [(source, source + steps) for source in range(first, last)])


def decay_products(row_decay, targets):
    count = row_decay.shape[0]
    target = lax.broadcasted_iota(jnp.int32, (targets, count, count), 0)
    source = lax.broadcasted_iota(jnp.int32, (targets, count, count), 1)
    between = lax.broadcasted_iota(jnp.int32, (targets, count, count), 2)
    inside = jnp.logical_and(between > source, between < target)
    factors = jnp.where(inside[..., None], row_decay[None, None], 1.0)
    products = jnp.prod(factors, 2)
    return jnp.where((source[:, :, 0] < target[:, :, 0])[..., None], products, 0.0)


def entering(decay, contrib):
    quads, quad = (lax.axis_index("ch"), lax.axis_size("cl"))
    place = lax.axis_index("cl")
    lanes = contrib.shape[-1]
    head_rows = contrib.shape[-2]
    heads = decay.size
    chunk = contrib.size // lanes // quad
    pieces = contrib.reshape(quad, chunk, lanes)
    tail = jnp.zeros((quad, 8, lanes), jnp.float32)
    tail = tail.at[:, 0, :heads].set(jnp.broadcast_to(decay.reshape(1, heads), (quad, heads)))
    outgoing = jnp.concatenate([pieces, tail], 1).astype(jnp.bfloat16)
    incoming = lax.all_to_all(outgoing, "cl", 0, 0).astype(jnp.float32)
    states = incoming[:, :chunk]
    decays = incoming[:, chunk, :heads]
    row_head = (place * chunk + lax.broadcasted_iota(jnp.int32, (chunk, heads), 0)) // head_rows
    pick = row_head == lax.broadcasted_iota(jnp.int32, (chunk, heads), 1)
    row_decay = jnp.sum(jnp.where(pick[None], decays[:, None, :], 0.0), -1)
    local = jnp.einsum(
        "kjr,jrl->krl", decay_products(row_decay, quad + 1), states, precision=HIGH
    )
    step = lax.broadcasted_iota(jnp.int32, (quad + 1, quad, chunk), 0)
    index = lax.broadcasted_iota(jnp.int32, (quad + 1, quad, chunk), 1)
    entry = jnp.prod(jnp.where(index < step, row_decay[None], 1.0), 1)
    pad_rows = 8 - (chunk // lanes) % 8
    summary = jnp.concatenate(
        [local[quad], entry[quad].reshape(chunk // lanes, lanes), jnp.zeros((pad_rows, lanes))]
    )
    count_hi = lax.axis_size("ch")
    shared = lax.all_gather(summary.astype(jnp.bfloat16), "ch").astype(jnp.float32)
    totals = shared[:, :chunk]
    quad_decay = shared[:, chunk : chunk + chunk // lanes].reshape(count_hi, chunk)
    earlier = lax.broadcasted_iota(jnp.int32, (count_hi, count_hi, chunk), 0)
    middle = lax.broadcasted_iota(jnp.int32, (count_hi, count_hi, chunk), 1)
    spans = jnp.logical_and(middle > earlier, middle < quads)
    across = jnp.prod(jnp.where(spans, quad_decay[None], 1.0), 1)
    across = jnp.where(earlier[:, 0] < quads, across, 0.0)
    entering_state = jnp.einsum("qr,qrl->rl", across, totals, precision=HIGH)
    carried = local[:quad] + entry[:quad, :, None] * entering_state[None]
    returned = lax.all_to_all(carried.astype(jnp.bfloat16), "cl", 0, 0)
    return returned.astype(jnp.float32).reshape(contrib.shape)


def hadamard_signs(sign_order):
    row_index = lax.broadcasted_iota(jnp.int32, (sign_order, sign_order), 0)
    col_index = lax.broadcasted_iota(jnp.int32, (sign_order, sign_order), 1)
    common = jnp.bitwise_and(row_index, col_index)
    parity = jnp.zeros((sign_order, sign_order), jnp.int32)
    for bit_index in range(sign_order.bit_length() - 1):
        parity = parity + jnp.bitwise_and(jnp.right_shift(common, bit_index), 1)
    return 1.0 - 2.0 * jnp.bitwise_and(parity, 1).astype(jnp.float32)


def kurtosis_from(powers, row_count):
    average = powers[0] / row_count
    second = powers[1] / row_count - average * average
    fourth = (
        powers[3] / row_count
        - 4.0 * average * powers[2] / row_count
        + 6.0 * average * average * powers[1] / row_count
        - 3.0 * average * average * average * average
    )
    return fourth / (second * second + 1e-06)


def shards(
    tokens, x_weight, bc_weight, dt_weight, conv_x, conv_bc, dt_bias, a_log, d_skip, norm_gain
):
    tok_rows = tokens.shape[1]
    model_width = tokens.shape[2]
    signs = hadamard_signs(ROOT)
    blocks = tokens.reshape(tok_rows, ROOT, ROOT)
    first_pass = jnp.einsum(
        "tab,ac->tcb", blocks, signs.astype(jnp.bfloat16), preferred_element_type=jnp.float32
    )
    second = jnp.einsum("tcb,bd->tcd", first_pass, signs, precision=HIGH)
    rotated = (second.reshape(tok_rows, model_width) / ROOT).astype(jnp.bfloat16)
    channel_share = model_width // lax.axis_size("mp")
    own_cols = lax.dynamic_slice_in_dim(
        rotated, lax.axis_index("mp") * channel_share, channel_share, 1
    ).astype(jnp.float32)
    square = own_cols * own_cols
    powers = jnp.stack(
        [
            jnp.sum(own_cols, 0),
            jnp.sum(square, 0),
            jnp.sum(square * own_cols, 0),
            jnp.sum(square * square, 0),
        ]
    )
    ctx_count = lax.axis_size("ch") * lax.axis_size("cl")
    row_count = float(tok_rows * lax.axis_size("dp") * ctx_count)
    totals = lax.psum(lax.psum(powers, CTX), "dp")
    totals, rotated = lax.optimization_barrier((totals, rotated))
    kurtosis = kurtosis_from(totals, row_count)
    local_panel = jnp.concatenate([x_weight, bc_weight, dt_weight], 1)
    panel = lax.all_gather(local_panel, CTX, axis=0, tiled=True)
    seqs = lax.axis_size("dp")
    share = model_width // seqs
    rim = 8
    earlier = passed_along(rotated[tok_rows - rim :], CTX, 1, ctx_count)
    extended = jnp.concatenate([earlier, rotated], 0)
    outgoing = extended.reshape(tok_rows + rim, seqs, share).transpose(1, 0, 2)
    incoming = lax.all_to_all(outgoing, "dp", 0, 0)
    x_end = x_weight.shape[1]
    bc_end = x_end + bc_weight.shape[1]
    side_partials = jnp.einsum(
        "kti,io->kto", incoming, panel[:, x_end:], preferred_element_type=jnp.float32
    )
    side_back = lax.all_to_all(side_partials, "dp", 0, 0)
    x_partials = jnp.einsum(
        "kti,io->kto", incoming, panel[:, :x_end], preferred_element_type=jnp.float32
    )
    x_back = lax.all_to_all(x_partials, "dp", 0, 0)
    side_ext = jnp.sum(side_back, 0)
    x_ext = jnp.sum(x_back, 0)
    x_cols = x_end
    bc_width = bc_end - x_end
    dt_proj = lax.optimization_barrier(side_ext[rim:, bc_width:].astype(jnp.bfloat16))
    kernel = conv_x.shape[0] - 1

    def causal_conv(rows, taps):
        padded = rows.astype(jnp.bfloat16)[rim - (kernel - 1) :]
        total = taps[kernel]
        for tap_index in range(kernel):
            total = total + taps[tap_index] * padded[tap_index : tap_index + tok_rows]
        return jax.nn.silu(total).astype(jnp.bfloat16)

    bc_own = causal_conv(side_ext[:, :bc_width], conv_bc)
    x_conv = causal_conv(x_ext, conv_x)
    heads_dev = dt_weight.shape[1]
    head_size = x_cols // heads_dev
    per_group = HEADS // G
    groups_here = max(1, heads_dev // per_group)
    heads_local = heads_dev // groups_here
    first_group = lax.axis_index("mp") * heads_dev // per_group
    mp_count = lax.axis_size("mp")
    if bc_own.shape[1] == NS and mp_count == 2 * G and groups_here == 1:
        owner = [m * heads_dev // per_group for m in range(mp_count)]
        odd_first = [(owner[m] if m % 2 == 0 else G + owner[m], m) for m in range(mp_count)]
        even_first = [(G + owner[m] if m % 2 == 0 else owner[m], m) for m in range(mp_count)]
        got_a = lax.ppermute(bc_own, "mp", odd_first)
        got_b = lax.ppermute(bc_own, "mp", even_first)
        even = lax.axis_index("mp") % 2 == 0
        write_here = jnp.where(even, got_a, got_b).reshape(tok_rows, 1, NS)
        read_here = jnp.where(even, got_b, got_a).reshape(tok_rows, 1, NS)
    else:
        group_all = lax.all_gather(bc_own, "mp", axis=1, tiled=True)
        write_all = group_all[:, : G * NS].reshape(tok_rows, G, NS)
        read_all = group_all[:, G * NS :].reshape(tok_rows, G, NS)
        write_here = lax.dynamic_slice_in_dim(write_all, first_group, groups_here, 1)
        read_here = lax.dynamic_slice_in_dim(read_all, first_group, groups_here, 1)
    step_size = jax.nn.softplus(dt_proj.astype(jnp.float32) + dt_bias)
    decay_rate = step_size * jnp.exp(a_log)
    cumulative = jnp.cumsum(decay_rate, 0)
    block_end = cumulative[-1]
    causal = lax.broadcasted_iota(jnp.int32, (tok_rows, tok_rows), 0) >= lax.broadcasted_iota(
        jnp.int32, (tok_rows, tok_rows), 1
    )
    spread = cumulative.T[:, :, None] - cumulative.T[:, None, :]
    decay_mask = jnp.where(causal, jnp.exp(-jnp.where(causal, spread, 0.0)), 0.0)
    scores = jnp.einsum("tgn,sgn->gts", read_here, write_here, preferred_element_type=jnp.float32)
    weights = (
        scores[:, None]
        * decay_mask.reshape(groups_here, heads_local, tok_rows, tok_rows)
        * step_size.T.reshape(groups_here, heads_local, 1, tok_rows)
    ).astype(jnp.bfloat16)
    x_heads = x_conv.reshape(tok_rows, groups_here, heads_local, head_size)
    within_block = jnp.einsum(
        "ghts,sghp->tghp", weights, x_heads, preferred_element_type=jnp.float32
    )
    update = (
        (jnp.exp(-(block_end - cumulative)) * step_size).reshape(
            tok_rows, groups_here, heads_local
        )[..., None]
        * x_heads
    ).astype(jnp.bfloat16)
    contrib = jnp.einsum("sghp,sgn->ghpn", update, write_here, preferred_element_type=jnp.float32)
    carried = entering(jnp.exp(-block_end).reshape(groups_here, heads_local), contrib)
    from_before = jnp.exp(-cumulative).reshape(tok_rows, groups_here, heads_local)[
        ..., None
    ] * jnp.einsum("tgn,ghpn->tghp", read_here.astype(jnp.float32), carried, precision=HIGH)
    output_raw = (
        within_block
        + from_before
        + d_skip.reshape(groups_here, heads_local)[None, :, :, None] * x_heads.astype(jnp.float32)
    )
    mean_square = jnp.mean(output_raw * output_raw, -1, keepdims=True)
    normed = (
        output_raw
        * lax.rsqrt(mean_square + 1e-05)
        * norm_gain.reshape(groups_here, heads_local, head_size)
    )
    return (normed.reshape(1, tok_rows, x_cols).astype(jnp.bfloat16), kurtosis)


def solution(mesh):
    grid = mesh.devices
    quad = 8 if grid.shape[1] % 8 == 0 else 1
    split = jax.sharding.Mesh(
        grid.reshape(grid.shape[0], grid.shape[1] // quad, quad, grid.shape[2]),
        ("dp", "ch", "cl", "mp"),
    )
    return jax.shard_map(
        shards,
        mesh=split,
        in_specs=(
            P("dp", CTX, None),
            P(("dp",) + CTX, "mp"),
            P(("dp",) + CTX, "mp"),
            P(("dp",) + CTX, "mp"),
            P(None, "mp"),
            P(None, "mp"),
            P("mp"),
            P("mp"),
            P("mp"),
            P("mp"),
        ),
        out_specs=(P("dp", CTX, "mp"), P("mp")),
        check_vma=False,
    )
```

```python
import jax
import jax.numpy as jnp
from jax import lax
from jax.sharding import PartitionSpec as P

ROOT = 64
HEADS = 128
G = 4
NS = 128


HIGH = lax.Precision.HIGHEST
CTX = ("ch", "cl")


def passed_along(value, axis, steps, count):
    first, last = (max(0, -steps), min(count, count - steps))
    return lax.ppermute(value, axis, [(source, source + steps) for source in range(first, last)])


def decay_products(row_decay, targets):
    count = row_decay.shape[0]
    target = lax.broadcasted_iota(jnp.int32, (targets, count, count), 0)
    source = lax.broadcasted_iota(jnp.int32, (targets, count, count), 1)
    between = lax.broadcasted_iota(jnp.int32, (targets, count, count), 2)
    inside = jnp.logical_and(between > source, between < target)
    factors = jnp.where(inside[..., None], row_decay[None, None], 1.0)
    products = jnp.prod(factors, 2)
    return jnp.where((source[:, :, 0] < target[:, :, 0])[..., None], products, 0.0)


def entering(decay, contrib):
    quads, quad = (lax.axis_index("ch"), lax.axis_size("cl"))
    place = lax.axis_index("cl")
    lanes = contrib.shape[-1]
    head_rows = contrib.shape[-2]
    heads = decay.size
    chunk = contrib.size // lanes // quad
    pieces = contrib.reshape(quad, chunk, lanes)
    tail = jnp.zeros((quad, 8, lanes), jnp.float32)
    tail = tail.at[:, 0, :heads].set(jnp.broadcast_to(decay.reshape(1, heads), (quad, heads)))
    outgoing = jnp.concatenate([pieces, tail], 1).astype(jnp.bfloat16)
    incoming = lax.all_to_all(outgoing, "cl", 0, 0).astype(jnp.float32)
    states = incoming[:, :chunk]
    decays = incoming[:, chunk, :heads]
    row_head = (place * chunk + lax.broadcasted_iota(jnp.int32, (chunk, heads), 0)) // head_rows
    pick = row_head == lax.broadcasted_iota(jnp.int32, (chunk, heads), 1)
    row_decay = jnp.sum(jnp.where(pick[None], decays[:, None, :], 0.0), -1)
    local = jnp.einsum(
        "kjr,jrl->krl", decay_products(row_decay, quad + 1), states, precision=HIGH
    )
    step = lax.broadcasted_iota(jnp.int32, (quad + 1, quad, chunk), 0)
    index = lax.broadcasted_iota(jnp.int32, (quad + 1, quad, chunk), 1)
    entry = jnp.prod(jnp.where(index < step, row_decay[None], 1.0), 1)
    pad_rows = 8 - (chunk // lanes) % 8
    summary = jnp.concatenate(
        [local[quad], entry[quad].reshape(chunk // lanes, lanes), jnp.zeros((pad_rows, lanes))]
    )
    count_hi = lax.axis_size("ch")
    shared = lax.all_gather(summary.astype(jnp.bfloat16), "ch").astype(jnp.float32)
    totals = shared[:, :chunk]
    quad_decay = shared[:, chunk : chunk + chunk // lanes].reshape(count_hi, chunk)
    earlier = lax.broadcasted_iota(jnp.int32, (count_hi, count_hi, chunk), 0)
    middle = lax.broadcasted_iota(jnp.int32, (count_hi, count_hi, chunk), 1)
    spans = jnp.logical_and(middle > earlier, middle < quads)
    across = jnp.prod(jnp.where(spans, quad_decay[None], 1.0), 1)
    across = jnp.where(earlier[:, 0] < quads, across, 0.0)
    entering_state = jnp.einsum("qr,qrl->rl", across, totals, precision=HIGH)
    carried = local[:quad] + entry[:quad, :, None] * entering_state[None]
    returned = lax.all_to_all(carried.astype(jnp.bfloat16), "cl", 0, 0)
    return returned.astype(jnp.float32).reshape(contrib.shape)


def hadamard_signs(sign_order):
    row_index = lax.broadcasted_iota(jnp.int32, (sign_order, sign_order), 0)
    col_index = lax.broadcasted_iota(jnp.int32, (sign_order, sign_order), 1)
    common = jnp.bitwise_and(row_index, col_index)
    parity = jnp.zeros((sign_order, sign_order), jnp.int32)
    for bit_index in range(sign_order.bit_length() - 1):
        parity = parity + jnp.bitwise_and(jnp.right_shift(common, bit_index), 1)
    return 1.0 - 2.0 * jnp.bitwise_and(parity, 1).astype(jnp.float32)


def kurtosis_from(powers, row_count):
    average = powers[0] / row_count
    second = powers[1] / row_count - average * average
    fourth = (
        powers[3] / row_count
        - 4.0 * average * powers[2] / row_count
        + 6.0 * average * average * powers[1] / row_count
        - 3.0 * average * average * average * average
    )
    return fourth / (second * second + 1e-06)


def shards(
    tokens, x_weight, bc_weight, dt_weight, conv_x, conv_bc, dt_bias, a_log, d_skip, norm_gain
):
    tok_rows = tokens.shape[1]
    model_width = tokens.shape[2]
    signs = hadamard_signs(ROOT)
    blocks = tokens.reshape(tok_rows, ROOT, ROOT)
    first_pass = jnp.einsum(
        "tab,ac->tcb", blocks, signs.astype(jnp.bfloat16), preferred_element_type=jnp.float32
    )
    second = jnp.einsum("tcb,bd->tcd", first_pass, signs, precision=HIGH)
    rotated = (second.reshape(tok_rows, model_width) / ROOT).astype(jnp.bfloat16)
    channel_share = model_width // lax.axis_size("mp")
    own_cols = lax.dynamic_slice_in_dim(
        rotated, lax.axis_index("mp") * channel_share, channel_share, 1
    ).astype(jnp.float32)
    square = own_cols * own_cols
    powers = jnp.stack(
        [
            jnp.sum(own_cols, 0),
            jnp.sum(square, 0),
            jnp.sum(square * own_cols, 0),
            jnp.sum(square * square, 0),
        ]
    )
    ctx_count = lax.axis_size("ch") * lax.axis_size("cl")
    row_count = float(tok_rows * lax.axis_size("dp") * ctx_count)
    totals = lax.psum(lax.psum(powers, CTX), "dp")
    totals, rotated = lax.optimization_barrier((totals, rotated))
    kurtosis = kurtosis_from(totals, row_count)
    local_panel = jnp.concatenate([x_weight, bc_weight, dt_weight], 1)
    panel = lax.all_gather(local_panel, CTX, axis=0, tiled=True)
    seqs = lax.axis_size("dp")
    share = model_width // seqs
    rim = 8
    earlier = passed_along(rotated[tok_rows - rim :], CTX, 1, ctx_count)
    extended = jnp.concatenate([earlier, rotated], 0)
    outgoing = extended.reshape(tok_rows + rim, seqs, share).transpose(1, 0, 2)
    incoming = lax.all_to_all(outgoing, "dp", 0, 0)
    x_end = x_weight.shape[1]
    bc_end = x_end + bc_weight.shape[1]
    side_partials = jnp.einsum(
        "kti,io->kto", incoming, panel[:, x_end:], preferred_element_type=jnp.float32
    )
    side_shape = side_partials.shape
    dense = side_partials.reshape(side_shape[0], -1, 128)
    side_back = lax.all_to_all(dense, "dp", 0, 0).reshape(side_shape)
    x_partials = jnp.einsum(
        "kti,io->kto", incoming, panel[:, :x_end], preferred_element_type=jnp.float32
    )
    x_back = lax.all_to_all(x_partials, "dp", 0, 0)
    side_ext = jnp.sum(side_back, 0)
    x_ext = jnp.sum(x_back, 0)
    x_cols = x_end
    bc_width = bc_end - x_end
    dt_proj = lax.optimization_barrier(side_ext[rim:, bc_width:].astype(jnp.bfloat16))
    kernel = conv_x.shape[0] - 1

    def causal_conv(rows, taps):
        padded = rows.astype(jnp.bfloat16)[rim - (kernel - 1) :]
        total = taps[kernel]
        for tap_index in range(kernel):
            total = total + taps[tap_index] * padded[tap_index : tap_index + tok_rows]
        return jax.nn.silu(total).astype(jnp.bfloat16)

    bc_own = causal_conv(side_ext[:, :bc_width], conv_bc)
    x_conv = causal_conv(x_ext, conv_x)
    heads_dev = dt_weight.shape[1]
    head_size = x_cols // heads_dev
    per_group = HEADS // G
    groups_here = max(1, heads_dev // per_group)
    heads_local = heads_dev // groups_here
    first_group = lax.axis_index("mp") * heads_dev // per_group
    mp_count = lax.axis_size("mp")
    if bc_own.shape[1] == NS and mp_count == 2 * G and groups_here == 1:
        owner = [m * heads_dev // per_group for m in range(mp_count)]
        odd_first = [(owner[m] if m % 2 == 0 else G + owner[m], m) for m in range(mp_count)]
        even_first = [(G + owner[m] if m % 2 == 0 else owner[m], m) for m in range(mp_count)]
        got_a = lax.ppermute(bc_own, "mp", odd_first)
        got_b = lax.ppermute(bc_own, "mp", even_first)
        even = lax.axis_index("mp") % 2 == 0
        write_here = jnp.where(even, got_a, got_b).reshape(tok_rows, 1, NS)
        read_here = jnp.where(even, got_b, got_a).reshape(tok_rows, 1, NS)
    else:
        group_all = lax.all_gather(bc_own, "mp", axis=1, tiled=True)
        write_all = group_all[:, : G * NS].reshape(tok_rows, G, NS)
        read_all = group_all[:, G * NS :].reshape(tok_rows, G, NS)
        write_here = lax.dynamic_slice_in_dim(write_all, first_group, groups_here, 1)
        read_here = lax.dynamic_slice_in_dim(read_all, first_group, groups_here, 1)
    step_size = jax.nn.softplus(dt_proj.astype(jnp.float32) + dt_bias)
    decay_rate = step_size * jnp.exp(a_log)
    cumulative = jnp.cumsum(decay_rate, 0)
    block_end = cumulative[-1]
    causal = lax.broadcasted_iota(jnp.int32, (tok_rows, tok_rows), 0) >= lax.broadcasted_iota(
        jnp.int32, (tok_rows, tok_rows), 1
    )
    spread = cumulative.T[:, :, None] - cumulative.T[:, None, :]
    decay_mask = jnp.where(causal, jnp.exp(-jnp.where(causal, spread, 0.0)), 0.0)
    scores = jnp.einsum("tgn,sgn->gts", read_here, write_here, preferred_element_type=jnp.float32)
    weights = (
        scores[:, None]
        * decay_mask.reshape(groups_here, heads_local, tok_rows, tok_rows)
        * step_size.T.reshape(groups_here, heads_local, 1, tok_rows)
    ).astype(jnp.bfloat16)
    x_heads = x_conv.reshape(tok_rows, groups_here, heads_local, head_size)
    within_block = jnp.einsum(
        "ghts,sghp->tghp", weights, x_heads, preferred_element_type=jnp.float32
    )
    update = (
        (jnp.exp(-(block_end - cumulative)) * step_size).reshape(
            tok_rows, groups_here, heads_local
        )[..., None]
        * x_heads
    ).astype(jnp.bfloat16)
    contrib = jnp.einsum("sghp,sgn->ghpn", update, write_here, preferred_element_type=jnp.float32)
    carried = entering(jnp.exp(-block_end).reshape(groups_here, heads_local), contrib)
    from_before = jnp.exp(-cumulative).reshape(tok_rows, groups_here, heads_local)[
        ..., None
    ] * jnp.einsum("tgn,ghpn->tghp", read_here.astype(jnp.float32), carried, precision=HIGH)
    output_raw = (
        within_block
        + from_before
        + d_skip.reshape(groups_here, heads_local)[None, :, :, None] * x_heads.astype(jnp.float32)
    )
    mean_square = jnp.mean(output_raw * output_raw, -1, keepdims=True)
    normed = (
        output_raw
        * lax.rsqrt(mean_square + 1e-05)
        * norm_gain.reshape(groups_here, heads_local, head_size)
    )
    return (normed.reshape(1, tok_rows, x_cols).astype(jnp.bfloat16), kurtosis)


def solution(mesh):
    grid = mesh.devices
    quad = 4 if grid.shape[1] % 4 == 0 else 1
    split = jax.sharding.Mesh(
        grid.reshape(grid.shape[0], grid.shape[1] // quad, quad, grid.shape[2]),
        ("dp", "ch", "cl", "mp"),
    )
    return jax.shard_map(
        shards,
        mesh=split,
        in_specs=(
            P("dp", CTX, None),
            P(("dp",) + CTX, "mp"),
            P(("dp",) + CTX, "mp"),
            P(("dp",) + CTX, "mp"),
            P(None, "mp"),
            P(None, "mp"),
            P("mp"),
            P("mp"),
            P("mp"),
            P("mp"),
        ),
        out_specs=(P("dp", CTX, "mp"), P("mp")),
        check_vma=False,
    )
```

```python
import jax
import jax.numpy as jnp
from jax import lax
from jax.sharding import PartitionSpec as P

ROOT = 64
HEADS = 128
G = 4
NS = 128


HIGH = lax.Precision.HIGHEST
CTX = ("ch", "cl")


def passed_along(value, axis, steps, count):
    first, last = (max(0, -steps), min(count, count - steps))
    return lax.ppermute(value, axis, [(source, source + steps) for source in range(first, last)])


def decay_products(row_decay, targets):
    count = row_decay.shape[0]
    target = lax.broadcasted_iota(jnp.int32, (targets, count, count), 0)
    source = lax.broadcasted_iota(jnp.int32, (targets, count, count), 1)
    between = lax.broadcasted_iota(jnp.int32, (targets, count, count), 2)
    inside = jnp.logical_and(between > source, between < target)
    factors = jnp.where(inside[..., None], row_decay[None, None], 1.0)
    products = jnp.prod(factors, 2)
    return jnp.where((source[:, :, 0] < target[:, :, 0])[..., None], products, 0.0)


def entering(decay, contrib):
    quads, quad = (lax.axis_index("ch"), lax.axis_size("cl"))
    place = lax.axis_index("cl")
    lanes = contrib.shape[-1]
    head_rows = contrib.shape[-2]
    heads = decay.size
    chunk = contrib.size // lanes // quad
    pieces = contrib.reshape(quad, chunk, lanes)
    tail = jnp.zeros((quad, 8, lanes), jnp.float32)
    tail = tail.at[:, 0, :heads].set(jnp.broadcast_to(decay.reshape(1, heads), (quad, heads)))
    outgoing = jnp.concatenate([pieces, tail], 1).astype(jnp.bfloat16)
    incoming = lax.all_to_all(outgoing, "cl", 0, 0).astype(jnp.float32)
    states = incoming[:, :chunk]
    decays = incoming[:, chunk, :heads]
    row_head = (place * chunk + lax.broadcasted_iota(jnp.int32, (chunk, heads), 0)) // head_rows
    pick = row_head == lax.broadcasted_iota(jnp.int32, (chunk, heads), 1)
    row_decay = jnp.sum(jnp.where(pick[None], decays[:, None, :], 0.0), -1)
    local = jnp.einsum(
        "kjr,jrl->krl", decay_products(row_decay, quad + 1), states, precision=HIGH
    )
    step = lax.broadcasted_iota(jnp.int32, (quad + 1, quad, chunk), 0)
    index = lax.broadcasted_iota(jnp.int32, (quad + 1, quad, chunk), 1)
    entry = jnp.prod(jnp.where(index < step, row_decay[None], 1.0), 1)
    pad_rows = 8 - (chunk // lanes) % 8
    summary = jnp.concatenate(
        [local[quad], entry[quad].reshape(chunk // lanes, lanes), jnp.zeros((pad_rows, lanes))]
    )
    count_hi = lax.axis_size("ch")
    shared = lax.all_gather(summary.astype(jnp.bfloat16), "ch").astype(jnp.float32)
    totals = shared[:, :chunk]
    quad_decay = shared[:, chunk : chunk + chunk // lanes].reshape(count_hi, chunk)
    earlier = lax.broadcasted_iota(jnp.int32, (count_hi, count_hi, chunk), 0)
    middle = lax.broadcasted_iota(jnp.int32, (count_hi, count_hi, chunk), 1)
    spans = jnp.logical_and(middle > earlier, middle < quads)
    across = jnp.prod(jnp.where(spans, quad_decay[None], 1.0), 1)
    across = jnp.where(earlier[:, 0] < quads, across, 0.0)
    entering_state = jnp.einsum("qr,qrl->rl", across, totals, precision=HIGH)
    carried = local[:quad] + entry[:quad, :, None] * entering_state[None]
    returned = lax.all_to_all(carried.astype(jnp.bfloat16), "cl", 0, 0)
    return returned.astype(jnp.float32).reshape(contrib.shape)


def hadamard_signs(sign_order):
    row_index = lax.broadcasted_iota(jnp.int32, (sign_order, sign_order), 0)
    col_index = lax.broadcasted_iota(jnp.int32, (sign_order, sign_order), 1)
    common = jnp.bitwise_and(row_index, col_index)
    parity = jnp.zeros((sign_order, sign_order), jnp.int32)
    for bit_index in range(sign_order.bit_length() - 1):
        parity = parity + jnp.bitwise_and(jnp.right_shift(common, bit_index), 1)
    return 1.0 - 2.0 * jnp.bitwise_and(parity, 1).astype(jnp.float32)


def kurtosis_from(powers, row_count):
    average = powers[0] / row_count
    second = powers[1] / row_count - average * average
    fourth = (
        powers[3] / row_count
        - 4.0 * average * powers[2] / row_count
        + 6.0 * average * average * powers[1] / row_count
        - 3.0 * average * average * average * average
    )
    return fourth / (second * second + 1e-06)


def shards(
    tokens, x_weight, bc_weight, dt_weight, conv_x, conv_bc, dt_bias, a_log, d_skip, norm_gain
):
    tok_rows = tokens.shape[1]
    model_width = tokens.shape[2]
    signs = hadamard_signs(ROOT)
    blocks = tokens.reshape(tok_rows, ROOT, ROOT)
    first_pass = jnp.einsum(
        "tab,ac->tcb", blocks, signs.astype(jnp.bfloat16), preferred_element_type=jnp.float32
    )
    second = jnp.einsum("tcb,bd->tcd", first_pass, signs, precision=HIGH)
    rotated = (second.reshape(tok_rows, model_width) / ROOT).astype(jnp.bfloat16)
    channel_share = model_width // lax.axis_size("mp")
    own_cols = lax.dynamic_slice_in_dim(
        rotated, lax.axis_index("mp") * channel_share, channel_share, 1
    ).astype(jnp.float32)
    square = own_cols * own_cols
    powers = jnp.stack(
        [
            jnp.sum(own_cols, 0),
            jnp.sum(square, 0),
            jnp.sum(square * own_cols, 0),
            jnp.sum(square * square, 0),
        ]
    )
    ctx_count = lax.axis_size("ch") * lax.axis_size("cl")
    row_count = float(tok_rows * lax.axis_size("dp") * ctx_count)
    totals = lax.psum(lax.psum(powers, CTX), "dp")
    totals, rotated = lax.optimization_barrier((totals, rotated))
    kurtosis = kurtosis_from(totals, row_count)
    local_panel = jnp.concatenate([x_weight, bc_weight, dt_weight], 1)
    panel = lax.all_gather(local_panel, CTX, axis=0, tiled=True)
    seqs = lax.axis_size("dp")
    share = model_width // seqs
    rim = 8
    earlier = passed_along(rotated[tok_rows - rim :], CTX, 1, ctx_count)
    extended = jnp.concatenate([earlier, rotated], 0)
    outgoing = extended.reshape(tok_rows + rim, seqs, share).transpose(1, 0, 2)
    incoming = lax.all_to_all(outgoing, "dp", 0, 0)
    x_end = x_weight.shape[1]
    bc_end = x_end + bc_weight.shape[1]
    side_partials = jnp.einsum(
        "kti,io->kto", incoming, panel[:, x_end:], preferred_element_type=jnp.float32
    )
    side_shape = side_partials.shape
    lead_cols = side_shape[2] - side_shape[2] % 128
    tail_rows = side_partials[:, :, lead_cols:].reshape(side_shape[0], -1, 128)
    dense = jnp.concatenate([side_partials[:, :, :lead_cols], tail_rows], 1)
    arrived = lax.all_to_all(dense, "dp", 0, 0)
    side_back = jnp.concatenate(
        [
            arrived[:, : side_shape[1]],
            arrived[:, side_shape[1] :].reshape(side_shape[0], side_shape[1], -1),
        ],
        2,
    )
    x_partials = jnp.einsum(
        "kti,io->kto", incoming, panel[:, :x_end], preferred_element_type=jnp.float32
    )
    x_back = lax.all_to_all(x_partials, "dp", 0, 0)
    side_ext = jnp.sum(side_back, 0)
    x_ext = jnp.sum(x_back, 0)
    x_cols = x_end
    bc_width = bc_end - x_end
    dt_proj = lax.optimization_barrier(side_ext[rim:, bc_width:].astype(jnp.bfloat16))
    kernel = conv_x.shape[0] - 1

    def causal_conv(rows, taps):
        padded = rows.astype(jnp.bfloat16)[rim - (kernel - 1) :]
        total = taps[kernel]
        for tap_index in range(kernel):
            total = total + taps[tap_index] * padded[tap_index : tap_index + tok_rows]
        return jax.nn.silu(total).astype(jnp.bfloat16)

    bc_own = causal_conv(side_ext[:, :bc_width], conv_bc)
    x_conv = causal_conv(x_ext, conv_x)
    heads_dev = dt_weight.shape[1]
    head_size = x_cols // heads_dev
    per_group = HEADS // G
    groups_here = max(1, heads_dev // per_group)
    heads_local = heads_dev // groups_here
    first_group = lax.axis_index("mp") * heads_dev // per_group
    mp_count = lax.axis_size("mp")
    if bc_own.shape[1] == NS and mp_count == 2 * G and groups_here == 1:
        owner = [m * heads_dev // per_group for m in range(mp_count)]
        odd_first = [(owner[m] if m % 2 == 0 else G + owner[m], m) for m in range(mp_count)]
        even_first = [(G + owner[m] if m % 2 == 0 else owner[m], m) for m in range(mp_count)]
        got_a = lax.ppermute(bc_own, "mp", odd_first)
        got_b = lax.ppermute(bc_own, "mp", even_first)
        even = lax.axis_index("mp") % 2 == 0
        write_here = jnp.where(even, got_a, got_b).reshape(tok_rows, 1, NS)
        read_here = jnp.where(even, got_b, got_a).reshape(tok_rows, 1, NS)
    else:
        group_all = lax.all_gather(bc_own, "mp", axis=1, tiled=True)
        write_all = group_all[:, : G * NS].reshape(tok_rows, G, NS)
        read_all = group_all[:, G * NS :].reshape(tok_rows, G, NS)
        write_here = lax.dynamic_slice_in_dim(write_all, first_group, groups_here, 1)
        read_here = lax.dynamic_slice_in_dim(read_all, first_group, groups_here, 1)
    step_size = jax.nn.softplus(dt_proj.astype(jnp.float32) + dt_bias)
    decay_rate = step_size * jnp.exp(a_log)
    cumulative = jnp.cumsum(decay_rate, 0)
    block_end = cumulative[-1]
    causal = lax.broadcasted_iota(jnp.int32, (tok_rows, tok_rows), 0) >= lax.broadcasted_iota(
        jnp.int32, (tok_rows, tok_rows), 1
    )
    spread = cumulative.T[:, :, None] - cumulative.T[:, None, :]
    decay_mask = jnp.where(causal, jnp.exp(-jnp.where(causal, spread, 0.0)), 0.0)
    scores = jnp.einsum("tgn,sgn->gts", read_here, write_here, preferred_element_type=jnp.float32)
    weights = (
        scores[:, None]
        * decay_mask.reshape(groups_here, heads_local, tok_rows, tok_rows)
        * step_size.T.reshape(groups_here, heads_local, 1, tok_rows)
    ).astype(jnp.bfloat16)
    x_heads = x_conv.reshape(tok_rows, groups_here, heads_local, head_size)
    within_block = jnp.einsum(
        "ghts,sghp->tghp", weights, x_heads, preferred_element_type=jnp.float32
    )
    update = (
        (jnp.exp(-(block_end - cumulative)) * step_size).reshape(
            tok_rows, groups_here, heads_local
        )[..., None]
        * x_heads
    ).astype(jnp.bfloat16)
    contrib = jnp.einsum("sghp,sgn->ghpn", update, write_here, preferred_element_type=jnp.float32)
    carried = entering(jnp.exp(-block_end).reshape(groups_here, heads_local), contrib)
    from_before = jnp.exp(-cumulative).reshape(tok_rows, groups_here, heads_local)[
        ..., None
    ] * jnp.einsum("tgn,ghpn->tghp", read_here.astype(jnp.float32), carried, precision=HIGH)
    output_raw = (
        within_block
        + from_before
        + d_skip.reshape(groups_here, heads_local)[None, :, :, None] * x_heads.astype(jnp.float32)
    )
    mean_square = jnp.mean(output_raw * output_raw, -1, keepdims=True)
    normed = (
        output_raw
        * lax.rsqrt(mean_square + 1e-05)
        * norm_gain.reshape(groups_here, heads_local, head_size)
    )
    return (normed.reshape(1, tok_rows, x_cols).astype(jnp.bfloat16), kurtosis)


def solution(mesh):
    grid = mesh.devices
    quad = 4 if grid.shape[1] % 4 == 0 else 1
    split = jax.sharding.Mesh(
        grid.reshape(grid.shape[0], grid.shape[1] // quad, quad, grid.shape[2]),
        ("dp", "ch", "cl", "mp"),
    )
    return jax.shard_map(
        shards,
        mesh=split,
        in_specs=(
            P("dp", CTX, None),
            P(("dp",) + CTX, "mp"),
            P(("dp",) + CTX, "mp"),
            P(("dp",) + CTX, "mp"),
            P(None, "mp"),
            P(None, "mp"),
            P("mp"),
            P("mp"),
            P("mp"),
            P("mp"),
        ),
        out_specs=(P("dp", CTX, "mp"), P("mp")),
        check_vma=False,
    )
```
